32 devices in a mesh: tm: 4 (over x, core), space: 8 (over z, y).
Axes of the slice: x: 2, y: 2, z: 4, core: 2. Of those that a mesh axis runs over, the one named last changes fastest.
Arguments:
- initial: float32 [4, 2, 64, 32, 128], P('tm', None, 'space'), may hold values from 0 to 1.5
- decay_rate: float32 [2, 64, 32, 128], P(None, 'space'), may hold values from 0.2 to 2
- source: float32 [2, 64, 32, 128], P(None, 'space'), may hold values from -2.5 to 2.5
- diffusivity: float32 [2], replicated, may hold values from 0.4 to 0.9
Outputs:
- end_state: float32 [4, 2, 64, 32, 128], P('tm', None, 'space')
The draws below stay inside these ranges and needn't reach their ends.
All inputs are finite; a program needn't handle non-finite values.
Results may differ from the reference program's by a relative error of at most 0.00002.
Values sent between devices are 32-bit elements; how exact they have to be, the bound alone decides.
No kernel may reach another device: no remote copies, remote signals or barrier semaphores. Data moves between devices by JAX's collectives and lax.ppermute only.
A program may use at most 64 MiB of HBM per device.

```python
import math
import jax
import jax.numpy as jnp
from jax import lax

NY = 32
NZ = 128
ROUNDS = 3
SLICES = 4
NX = 64


def block_levels(stream_key, extent, pieces, least, largest):
    gain = 1.0
    for position, blocks in pieces:
        heights = jax.random.uniform(jax.random.fold_in(jax.random.fold_in(stream_key, 6), position), (blocks,), jnp.float32, least / len(pieces), largest / len(pieces))
        gain = gain * jnp.repeat(jnp.exp(heights), extent[position] // blocks).reshape((-1,) + (1,) * (len(extent) - 1 - position))
    return gain


def centred(stream_key, extent, spread, bound, shards=(), held_as=jnp.bfloat16):
    entries = spread * jax.random.normal(stream_key, extent, jnp.float32)
    if shards:
        entries = entries * block_levels(stream_key, extent, shards, -0.22, 0.18)
    return jnp.clip(entries, -bound, bound).astype(held_as)


def setup_inputs(seed: int = 0) -> dict:
    key_list = jax.random.split(jax.random.key(seed), 5)
    initial = jnp.clip(1.5 * jax.random.uniform(key_list[0], (SLICES, 2, NX, NY, NZ), jnp.float32) ** block_levels(key_list[0], (SLICES, 2, NX, NY, NZ), ((0, 4), (2, 8)), -0.2, 0.2), 0.0, 1.5)
    decay_rate = jnp.clip(jnp.exp(math.log(2.0) - 2.3025851 * jax.random.uniform(key_list[1], (2, NX, NY, NZ), jnp.float32) ** block_levels(key_list[1], (2, NX, NY, NZ), ((1, 8),), -0.2, 0.2)), 0.2, 2.0)
    source = centred(key_list[2], (2, NX, NY, NZ), 0.5, 2.5, ((1, 8),), jnp.float32)
    diffusivity = jnp.clip(jnp.exp(jax.random.uniform(key_list[3], (2,), jnp.float32, math.log(0.4), math.log(0.9))), 0.4, 0.9)
    return dict(initial=initial, decay_rate=decay_rate, source=source, diffusivity=diffusivity)


step_length = 0.5

def lagrange_integral(nodes, j, upper_end):
    coeffs = [1.0]
    scale_down = 1.0
    for i in range(len(nodes)):
        if i != j:
            grown = [0.0] * (len(coeffs) + 1)
            for p in range(len(coeffs)):
                grown[p + 1] = grown[p + 1] + coeffs[p]
                grown[p] = grown[p] - nodes[i] * coeffs[p]
            coeffs = grown
            scale_down = scale_down * (nodes[j] - nodes[i])
    summed_up = 0.0
    for p in range(len(coeffs)):
        summed_up = summed_up + coeffs[p] * upper_end ** (p + 1) / (p + 1)
    return summed_up / scale_down

def node_tables():
    radical = math.sqrt(3.0 / 7.0)
    fine_nodes = [0.0, 0.5 * (1.0 - radical), 0.5, 0.5 * (1.0 + radical), 1.0]
    coarse_nodes = [0.0, 0.5, 1.0]
    integrals = [[lagrange_integral(fine_nodes, j, fine_nodes[m]) for j in range(5)] for m in range(5)]
    spread_table = [[float(step_length * (integrals[m + 1][j] - integrals[m][j])) for j in range(5)] for m in range(4)]
    grouped_table = [[spread_table[2 * c][j] + spread_table[2 * c + 1][j] for j in range(5)] for c in range(2)]
    interp_table = []
    for m in range(5):
        weights_row = []
        for k in range(3):
            factor = 1.0
            for i in range(3):
                if i != k:
                    factor = factor * (fine_nodes[m] - coarse_nodes[i]) / (coarse_nodes[k] - coarse_nodes[i])
            weights_row.append(factor)
        interp_table.append(weights_row)
    widths = [step_length * (fine_nodes[m + 1] - fine_nodes[m]) for m in range(4)]
    return (spread_table, grouped_table, interp_table, widths)

def restrict(field):
    upper = field[..., 0::2, 0::2, :] + field[..., 1::2, 0::2, :]
    lower = field[..., 0::2, 1::2, :] + field[..., 1::2, 1::2, :]
    return (upper + lower) * 0.25

def prolong(field):
    return jnp.repeat(jnp.repeat(field, 2, axis=-3), 2, axis=-2)

def react_terms(field, laplace, diffusivity, source):
    first_part = field[:, 0]
    second_part = field[:, 1]
    product = first_part * second_part * second_part
    return jnp.stack([diffusivity[0] * laplace[:, 0] - product + source[0], diffusivity[1] * laplace[:, 1] + product + source[1]], axis=1)

def fine_terms(field, diffusivity, source):
    pair_x = jnp.roll(field, -1, 2) + jnp.roll(field, 1, 2)
    pair_y = jnp.roll(field, -1, 3) + jnp.roll(field, 1, 3)
    pair_z = jnp.roll(field, -1, 4) + jnp.roll(field, 1, 4)
    laplace = pair_x + pair_y + pair_z - 6.0 * field
    return react_terms(field, laplace, diffusivity, source)

def coarse_terms(field, diffusivity, source_coarse):
    pair_x = jnp.roll(field, -1, 2) + jnp.roll(field, 1, 2)
    pair_y = jnp.roll(field, -1, 3) + jnp.roll(field, 1, 3)
    pair_z = jnp.roll(field, -1, 4) + jnp.roll(field, 1, 4)
    laplace = (pair_x - 2.0 * field) * 0.25 + (pair_y - 2.0 * field) * 0.25 + (pair_z - 2.0 * field)
    return react_terms(field, laplace, diffusivity, source_coarse)

def advance(states, begin_state, decay_rate, source, diffusivity, rate_coarse, source_coarse):
    spread_table, grouped_table, interp_table, widths = node_tables()
    old_terms = fine_terms(states, diffusivity, source)
    old_full = [old_terms[j] - decay_rate * states[j] for j in range(5)]
    swept = [begin_state]
    new_terms = [fine_terms(begin_state[None], diffusivity, source)[0]]
    for m in range(4):
        summed = spread_table[m][0] * old_full[0]
        for j in range(1, 5):
            summed = summed + spread_table[m][j] * old_full[j]
        numerator = swept[m] + widths[m] * (new_terms[m] - old_terms[m]) + widths[m] * decay_rate * states[m + 1] + summed
        swept.append(numerator / (1.0 + widths[m] * decay_rate))
        new_terms.append(fine_terms(swept[m + 1][None], diffusivity, source)[0])
    new_full = [new_terms[j] - decay_rate * swept[j] for j in range(5)]
    coarse_vals = [restrict(swept[0]), restrict(swept[2]), restrict(swept[4])]
    integrated = []
    for c in range(2):
        summed = grouped_table[c][0] * new_full[0]
        for j in range(1, 5):
            summed = summed + grouped_table[c][j] * new_full[j]
        integrated.append(restrict(summed))
    half_step = 0.5 * step_length
    divisor = 1.0 + half_step * rate_coarse
    coarse_one = (coarse_vals[0] + half_step * rate_coarse * coarse_vals[1] + integrated[0]) / divisor
    pair_terms = coarse_terms(jnp.stack([coarse_vals[1], coarse_one]), diffusivity, source_coarse)
    coarse_two = (coarse_one + half_step * (pair_terms[1] - pair_terms[0]) + half_step * rate_coarse * coarse_vals[2] + integrated[1]) / divisor
    delta_one = coarse_one - coarse_vals[1]
    delta_two = coarse_two - coarse_vals[2]
    result = [swept[0]]
    for m in range(1, 5):
        result.append(swept[m] + prolong(interp_table[m][1] * delta_one + interp_table[m][2] * delta_two))
    return jnp.stack(result)

def reference(initial, decay_rate, source, diffusivity):
    rate_coarse = restrict(decay_rate)
    source_coarse = restrict(source)
    states = jnp.broadcast_to(initial[:, None], (initial.shape[0], 5) + initial.shape[1:])
    for k in range(ROUNDS):
        begins = jnp.concatenate([initial[:1], states[:-1, 4]], axis=0)
        states = lax.map(lambda operands: advance(operands[0], operands[1], decay_rate, source, diffusivity, rate_coarse, source_coarse), (states, begins))
    return states[:, 4]
```

```python
import math

import jax
import jax.numpy as jnp
from jax import lax
from jax.sharding import PartitionSpec as P

ROUNDS = 3

START_HALO = 5

step_length = 0.5


def lagrange_integral(nodes, j, upper_end):
    coeffs = [1.0]
    scale_down = 1.0
    for i in range(len(nodes)):
        if i != j:
            grown = [0.0] * (len(coeffs) + 1)
            for p in range(len(coeffs)):
                grown[p + 1] = grown[p + 1] + coeffs[p]
                grown[p] = grown[p] - nodes[i] * coeffs[p]
            coeffs = grown
            scale_down = scale_down * (nodes[j] - nodes[i])
    summed_up = 0.0
    for p in range(len(coeffs)):
        summed_up = summed_up + coeffs[p] * upper_end ** (p + 1) / (p + 1)
    return summed_up / scale_down


def node_tables():
    radical = math.sqrt(3.0 / 7.0)
    fine_nodes = [0.0, 0.5 * (1.0 - radical), 0.5, 0.5 * (1.0 + radical), 1.0]
    coarse_nodes = [0.0, 0.5, 1.0]
    integrals = [
        [lagrange_integral(fine_nodes, j, fine_nodes[m]) for j in range(5)] for m in range(5)
    ]
    spread_table = [
        [float(step_length * (integrals[m + 1][j] - integrals[m][j])) for j in range(5)]
        for m in range(4)
    ]
    grouped_table = [
        [spread_table[2 * c][j] + spread_table[2 * c + 1][j] for j in range(5)] for c in range(2)
    ]
    interp_table = []
    for m in range(5):
        weights_row = []
        for k in range(3):
            factor = 1.0
            for i in range(3):
                if i != k:
                    factor = (
                        factor
                        * (fine_nodes[m] - coarse_nodes[i])
                        / (coarse_nodes[k] - coarse_nodes[i])
                    )
            weights_row.append(factor)
        interp_table.append(weights_row)
    widths = [step_length * (fine_nodes[m + 1] - fine_nodes[m]) for m in range(4)]
    return (spread_table, grouped_table, interp_table, widths)


def to_even_odd(a):
    return jnp.concatenate([a[..., 0::2, :], a[..., 1::2, :]], axis=-2)


def from_even_odd(a):
    half = a.shape[-2] // 2
    woven = jnp.stack([a[..., :half, :], a[..., half:, :]], axis=-2)
    return woven.reshape(a.shape)


def crop(field, h):
    a, have = field
    d = have - h
    assert d >= 0
    if d == 0:
        return a
    return lax.slice_in_dim(a, d, a.shape[-3] - d, axis=a.ndim - 3)


def space_halo(a, h):
    if h == 0:
        return a
    size = lax.axis_size("space")
    rows = a.shape[-3]
    assert h <= rows
    up = [(i, (i + 1) % size) for i in range(size)]
    down = [((i + 1) % size, i) for i in range(size)]
    before = lax.ppermute(lax.slice_in_dim(a, rows - h, rows, axis=a.ndim - 3), "space", up)
    after = lax.ppermute(lax.slice_in_dim(a, 0, h, axis=a.ndim - 3), "space", down)
    return jnp.concatenate([before, a, after], axis=a.ndim - 3)


def from_previous_slice(a, h):
    slices = lax.axis_size("tm")
    size = lax.axis_size("space")
    rows = a.shape[-3]
    axes = ("tm", "space")

    def moved(piece, shift):
        pairs = [
            (t * size + s, (t + 1) * size + (s + shift) % size)
            for t in range(slices - 1)
            for s in range(size)
        ]
        return lax.ppermute(piece, axes, pairs)

    centre = moved(a, 0)
    if h == 0:
        return centre
    before = moved(lax.slice_in_dim(a, rows - h, rows, axis=a.ndim - 3), 1)
    after = moved(lax.slice_in_dim(a, 0, h, axis=a.ndim - 3), -1)
    return jnp.concatenate([before, centre, after], axis=a.ndim - 3)


def react_terms(field, laplace, diffusivity, source):
    first_part = field[0]
    second_part = field[1]
    product = first_part * second_part * second_part
    return jnp.stack(
        [
            diffusivity[0] * laplace[0] - product + source[0],
            diffusivity[1] * laplace[1] + product + source[1],
        ],
        axis=0,
    )


def fine_laplace(a):
    centre = a[..., 1:-1, :, :]
    pair_x = a[..., 2:, :, :] + a[..., :-2, :, :]
    half = centre.shape[-2] // 2
    even = centre[..., :half, :]
    odd = centre[..., half:, :]
    pair_y = jnp.concatenate(
        [odd + jnp.roll(odd, 1, -2), jnp.roll(even, -1, -2) + even], axis=-2
    )
    pair_z = jnp.roll(centre, -1, -1) + jnp.roll(centre, 1, -1)
    return pair_x + pair_y + pair_z - 6.0 * centre


def coarse_laplace(a):
    centre = a[..., 1:-1, :, :]
    pair_x = a[..., 2:, :, :] + a[..., :-2, :, :]
    pair_y = jnp.roll(centre, -1, -2) + jnp.roll(centre, 1, -2)
    pair_z = jnp.roll(centre, -1, -1) + jnp.roll(centre, 1, -1)
    return (pair_x - 2.0 * centre) * 0.25 + (pair_y - 2.0 * centre) * 0.25 + (
        pair_z - 2.0 * centre
    )


def restrict(field):
    a, h = field
    h2 = h - h % 2
    a = crop(field, h2)
    rows = a.shape[-3]
    half = a.shape[-2] // 2
    pairs = a.reshape(a.shape[:-3] + (rows // 2, 2) + a.shape[-2:])
    even = pairs[..., :half, :]
    odd = pairs[..., half:, :]
    upper = even[..., 0, :, :] + even[..., 1, :, :]
    lower = odd[..., 0, :, :] + odd[..., 1, :, :]
    return (upper + lower) * 0.25, h2 // 2


def prolong(a):
    rows = jnp.repeat(a, 2, axis=a.ndim - 3)
    return jnp.concatenate([rows, rows], axis=-2)


def per_device(initial, decay_rate, source, diffusivity):
    spread_table, grouped_table, interp_table, widths = node_tables()
    first_slice = lax.axis_index("tm") == 0
    hs = START_HALO
    hfix = hs + (hs % 2)

    own_start = to_even_odd(initial[0])
    decay_own = to_even_odd(decay_rate)
    source_own = to_even_odd(source)
    fixed = space_halo(jnp.stack([decay_own, source_own]), hfix)
    decay = (fixed[0], hfix)
    src = (fixed[1], hfix)
    rate_c = restrict(decay)
    source_c = restrict(src)

    def fine_E(field):
        a, h = field
        laplace = fine_laplace(a)
        return react_terms(a[..., 1:-1, :, :], laplace, diffusivity, crop(src, h - 1)), h - 1

    def coarse_E(field):
        a, h = field
        laplace = coarse_laplace(a)
        return react_terms(a[..., 1:-1, :, :], laplace, diffusivity, crop(source_c, h - 1)), h - 1

    def exchange(field):
        a, h = field
        return space_halo(crop(field, 0), 1 if h == 0 else h), max(h, 1)

    def full(field, field_E):
        h = min(field[1], field_E[1])
        return crop(field_E, h) - crop(decay, h) * crop(field, h), h

    def advance(begin, states):
        cache = {}

        def terms_of(f):
            if id(f) not in cache:
                cache[id(f)] = fine_E(f)
            return cache[id(f)]

        old_terms = [terms_of(f) for f in states]
        old_full = [full(states[j], old_terms[j]) for j in range(5)]
        swept = [begin]
        new_terms = [fine_E(begin)]
        for m in range(4):
            h = min(new_terms[m][1], old_terms[m][1], states[m + 1][1], old_full[0][1])
            summed = spread_table[m][0] * crop(old_full[0], h)
            for j in range(1, 5):
                summed = summed + spread_table[m][j] * crop(old_full[j], h)
            dec = crop(decay, h)
            numerator = (
                crop(swept[m], h)
                + widths[m] * (crop(new_terms[m], h) - crop(old_terms[m], h))
                + widths[m] * dec * crop(states[m + 1], h)
                + summed
            )
            nxt = (numerator / (1.0 + widths[m] * dec), h)
            if h == 0 and m < 3:
                nxt = exchange(nxt)
            swept.append(nxt)
            if m < 3:
                new_terms.append(fine_E(nxt))
        if swept[4][1] == 0:
            swept[4] = exchange(swept[4])
        new_terms.append(fine_E(swept[4]))
        new_full = [full(swept[j], new_terms[j]) for j in range(5)]
        hf = min(f[1] for f in new_full)
        coarse_vals = [restrict(swept[0]), restrict(swept[2]), restrict(swept[4])]
        integrated = []
        for c in range(2):
            summed = grouped_table[c][0] * crop(new_full[0], hf)
            for j in range(1, 5):
                summed = summed + grouped_table[c][j] * crop(new_full[j], hf)
            integrated.append(restrict((summed, hf)))
        half_step = 0.5 * step_length
        hz = min(integrated[0][1], coarse_vals[0][1], coarse_vals[1][1])
        rc = crop(rate_c, hz)
        coarse_one = (
            crop(coarse_vals[0], hz) + half_step * rc * crop(coarse_vals[1], hz) + crop(integrated[0], hz)
        ) / (1.0 + half_step * rc)
        one = (coarse_one, hz)
        mid = coarse_vals[1]
        if hz == 0:
            one = exchange(one)
        if mid[1] == 0:
            mid = exchange(mid)
        mid_terms = coarse_E((crop(mid, 1), 1))
        one_terms = coarse_E((crop(one, 1), 1))
        rc = crop(rate_c, 0)
        coarse_two = (
            crop(one, 0)
            + half_step * (one_terms[0] - mid_terms[0])
            + half_step * rc * crop(coarse_vals[2], 0)
            + crop(integrated[1], 0)
        ) / (1.0 + half_step * rc)
        delta_one = crop(one, 0) - crop(coarse_vals[1], 0)
        delta_two = coarse_two - crop(coarse_vals[2], 0)
        result = [swept[0]]
        for m in range(1, 5):
            result.append(
                (
                    crop(swept[m], 0)
                    + prolong(interp_table[m][1] * delta_one + interp_table[m][2] * delta_two),
                    0,
                )
            )
        return result

    own_ext = space_halo(own_start, hs)
    begin_ext = jnp.where(first_slice, own_ext, from_previous_slice(own_start, hs))
    state = (own_ext, hs)
    states = [state] * 5
    begin = (begin_ext, hs)
    for k in range(ROUNDS):
        states = advance(begin, states)
        if k + 1 < ROUNDS:
            last = states[4][0]
            moved = space_halo(jnp.stack([s[0] for s in states[1:]]), hs)
            prior = from_previous_slice(last, hs)
            states = [(crop(states[0], hs), hs)] + [(moved[j], hs) for j in range(4)]
            begin = (jnp.where(first_slice, own_ext, prior), hs)
    return from_even_odd(states[4][0])[None]


def solution(mesh):
    placed = (
        P("tm", None, "space", None, None),
        P(None, "space", None, None),
        P(None, "space", None, None),
        P(),
    )
    return jax.shard_map(
        per_device,
        mesh=mesh,
        in_specs=placed,
        out_specs=P("tm", None, "space", None, None),
        check_vma=False,
    )
```

```python
import math

import jax
import jax.numpy as jnp
from jax import lax
from jax.sharding import PartitionSpec as P

ROUNDS = 3

START_HALO = 5

step_length = 0.5


def lagrange_integral(nodes, j, upper_end):
    coeffs = [1.0]
    scale_down = 1.0
    for i in range(len(nodes)):
        if i != j:
            grown = [0.0] * (len(coeffs) + 1)
            for p in range(len(coeffs)):
                grown[p + 1] = grown[p + 1] + coeffs[p]
                grown[p] = grown[p] - nodes[i] * coeffs[p]
            coeffs = grown
            scale_down = scale_down * (nodes[j] - nodes[i])
    summed_up = 0.0
    for p in range(len(coeffs)):
        summed_up = summed_up + coeffs[p] * upper_end ** (p + 1) / (p + 1)
    return summed_up / scale_down


def node_tables():
    radical = math.sqrt(3.0 / 7.0)
    fine_nodes = [0.0, 0.5 * (1.0 - radical), 0.5, 0.5 * (1.0 + radical), 1.0]
    coarse_nodes = [0.0, 0.5, 1.0]
    integrals = [
        [lagrange_integral(fine_nodes, j, fine_nodes[m]) for j in range(5)] for m in range(5)
    ]
    spread_table = [
        [float(step_length * (integrals[m + 1][j] - integrals[m][j])) for j in range(5)]
        for m in range(4)
    ]
    grouped_table = [
        [spread_table[2 * c][j] + spread_table[2 * c + 1][j] for j in range(5)] for c in range(2)
    ]
    interp_table = []
    for m in range(5):
        weights_row = []
        for k in range(3):
            factor = 1.0
            for i in range(3):
                if i != k:
                    factor = (
                        factor
                        * (fine_nodes[m] - coarse_nodes[i])
                        / (coarse_nodes[k] - coarse_nodes[i])
                    )
            weights_row.append(factor)
        interp_table.append(weights_row)
    widths = [step_length * (fine_nodes[m + 1] - fine_nodes[m]) for m in range(4)]
    return (spread_table, grouped_table, interp_table, widths)


def to_even_odd(a):
    return jnp.concatenate([a[..., 0::2, :], a[..., 1::2, :]], axis=-2)


def from_even_odd(a):
    half = a.shape[-2] // 2
    woven = jnp.stack([a[..., :half, :], a[..., half:, :]], axis=-2)
    return woven.reshape(a.shape)


def crop(field, h):
    a, have = field
    d = have - h
    assert d >= 0
    if d == 0:
        return a
    return lax.slice_in_dim(a, d, a.shape[-3] - d, axis=a.ndim - 3)


def space_halo(a, h):
    if h == 0:
        return a
    size = lax.axis_size("space")
    rows = a.shape[-3]
    assert h <= rows
    up = [(i, (i + 1) % size) for i in range(size)]
    down = [((i + 1) % size, i) for i in range(size)]
    before = lax.ppermute(lax.slice_in_dim(a, rows - h, rows, axis=a.ndim - 3), "space", up)
    after = lax.ppermute(lax.slice_in_dim(a, 0, h, axis=a.ndim - 3), "space", down)
    return jnp.concatenate([before, a, after], axis=a.ndim - 3)


def from_previous_slice(a, h):
    slices = lax.axis_size("tm")
    size = lax.axis_size("space")
    rows = a.shape[-3]
    axes = ("tm", "space")

    def moved(piece, shift):
        pairs = [
            (t * size + s, (t + 1) * size + (s + shift) % size)
            for t in range(slices - 1)
            for s in range(size)
        ]
        return lax.ppermute(piece, axes, pairs)

    centre = moved(a, 0)
    if h == 0:
        return centre
    before = moved(lax.slice_in_dim(a, rows - h, rows, axis=a.ndim - 3), 1)
    after = moved(lax.slice_in_dim(a, 0, h, axis=a.ndim - 3), -1)
    return jnp.concatenate([before, centre, after], axis=a.ndim - 3)


def react_terms(field, laplace, diffusivity, source):
    first_part = field[0]
    second_part = field[1]
    product = first_part * second_part * second_part
    return jnp.stack(
        [
            diffusivity[0] * laplace[0] - product + source[0],
            diffusivity[1] * laplace[1] + product + source[1],
        ],
        axis=0,
    )


def fine_laplace(a):
    centre = a[..., 1:-1, :, :]
    pair_x = a[..., 2:, :, :] + a[..., :-2, :, :]
    half = centre.shape[-2] // 2
    even = centre[..., :half, :]
    odd = centre[..., half:, :]
    pair_y = jnp.concatenate(
        [odd + jnp.roll(odd, 1, -2), jnp.roll(even, -1, -2) + even], axis=-2
    )
    pair_z = jnp.roll(centre, -1, -1) + jnp.roll(centre, 1, -1)
    return pair_x + pair_y + pair_z - 6.0 * centre


def coarse_laplace(a):
    centre = a[..., 1:-1, :, :]
    pair_x = a[..., 2:, :, :] + a[..., :-2, :, :]
    pair_y = jnp.roll(centre, -1, -2) + jnp.roll(centre, 1, -2)
    pair_z = jnp.roll(centre, -1, -1) + jnp.roll(centre, 1, -1)
    return (pair_x - 2.0 * centre) * 0.25 + (pair_y - 2.0 * centre) * 0.25 + (
        pair_z - 2.0 * centre
    )


def restrict(field):
    a, h = field
    h2 = h - h % 2
    a = crop(field, h2)
    rows = a.shape[-3]
    half = a.shape[-2] // 2
    pairs = a.reshape(a.shape[:-3] + (rows // 2, 2) + a.shape[-2:])
    even = pairs[..., :half, :]
    odd = pairs[..., half:, :]
    upper = even[..., 0, :, :] + even[..., 1, :, :]
    lower = odd[..., 0, :, :] + odd[..., 1, :, :]
    return (upper + lower) * 0.25, h2 // 2


def prolong(a):
    rows = jnp.repeat(a, 2, axis=a.ndim - 3)
    return jnp.concatenate([rows, rows], axis=-2)


def packed_halo(fields):
    size = lax.axis_size("space")
    rows = fields[0][0].shape[-3]
    axis = fields[0][0].ndim - 3
    up = [(i, (i + 1) % size) for i in range(size)]
    down = [((i + 1) % size, i) for i in range(size)]
    lasts = jnp.concatenate(
        [lax.slice_in_dim(a, rows - w, rows, axis=axis) for a, w in fields], axis=axis
    )
    firsts = jnp.concatenate([lax.slice_in_dim(a, 0, w, axis=axis) for a, w in fields], axis=axis)
    before = lax.ppermute(lasts, "space", up)
    after = lax.ppermute(firsts, "space", down)
    out = []
    offset = 0
    for a, w in fields:
        out.append(
            (
                jnp.concatenate(
                    [
                        lax.slice_in_dim(before, offset, offset + w, axis=axis),
                        a,
                        lax.slice_in_dim(after, offset, offset + w, axis=axis),
                    ],
                    axis=axis,
                ),
                w,
            )
        )
        offset += w
    return out


def per_device(initial, decay_rate, source, diffusivity):
    spread_table, grouped_table, interp_table, widths = node_tables()
    first_slice = lax.axis_index("tm") == 0
    hs = START_HALO
    assert hs == 5 and initial.shape[-3] >= hs
    hfix = hs - 1

    own_start = to_even_odd(initial[0])
    fixed = space_halo(jnp.stack([to_even_odd(decay_rate), to_even_odd(source)]), hfix)
    decay = (fixed[0], hfix)
    src = (fixed[1], hfix)
    rate_c = restrict(decay)
    source_c = restrict(src)

    def fine_E(field):
        a, h = field
        laplace = fine_laplace(a)
        return react_terms(a[..., 1:-1, :, :], laplace, diffusivity, crop(src, h - 1)), h - 1

    def coarse_E(field):
        a, h = field
        laplace = coarse_laplace(a)
        return react_terms(a[..., 1:-1, :, :], laplace, diffusivity, crop(source_c, h - 1)), h - 1

    def full(field, field_E):
        h = min(field[1], field_E[1])
        return crop(field_E, h) - crop(decay, h) * crop(field, h), h

    def step_terms(states, terms):
        fulls = [full(states[j], terms[j]) for j in range(5)]
        hf = min(f[1] for f in fulls)
        out = []
        for m in range(4):
            h = min(hf, terms[m][1], states[m + 1][1])
            summed = spread_table[m][0] * crop(fulls[0], h)
            for j in range(1, 5):
                summed = summed + spread_table[m][j] * crop(fulls[j], h)
            own = (
                widths[m] * crop(decay, h) * crop(states[m + 1], h)
                - widths[m] * crop(terms[m], h)
            ) + summed
            out.append((own, h))
        return out

    def advance(begin, step_parts, last):
        swept = [begin]
        new_terms = [fine_E(begin)]
        for m in range(4):
            h = min(new_terms[m][1], step_parts[m][1])
            numerator = (
                crop(swept[m], h) + widths[m] * crop(new_terms[m], h)
            ) + crop(step_parts[m], h)
            swept.append((numerator / (1.0 + widths[m] * crop(decay, h)), h))
            new_terms.append(fine_E(swept[m + 1]))
        assert new_terms[4][1] >= 0
        new_full = [full(swept[j], new_terms[j]) for j in range(5)]
        hf = min(f[1] for f in new_full)
        coarse_vals = [restrict(swept[0]), restrict(swept[2]), restrict(swept[4])]
        integrated = []
        for c in range(2):
            summed = grouped_table[c][0] * crop(new_full[0], hf)
            for j in range(1, 5):
                summed = summed + grouped_table[c][j] * crop(new_full[j], hf)
            integrated.append(restrict((summed, hf)))
        half_step = 0.5 * step_length
        rc = crop(rate_c, 0)
        coarse_one = (
            crop(coarse_vals[0], 0)
            + half_step * rc * crop(coarse_vals[1], 0)
            + crop(integrated[0], 0)
        ) / (1.0 + half_step * rc)
        if last:
            ho = 0
            one, mid = packed_halo([(coarse_one, 1), (crop(coarse_vals[1], 0), 1)])
            low, late = coarse_vals[2], integrated[1]
        else:
            ho = 1
            one, mid, low, late = packed_halo(
                [
                    (coarse_one, 2),
                    (crop(coarse_vals[1], 0), 2),
                    (crop(coarse_vals[2], 0), 1),
                    (crop(integrated[1], 0), 1),
                ]
            )
        one_terms = coarse_E((crop(one, ho + 1), ho + 1))
        mid_terms = coarse_E((crop(mid, ho + 1), ho + 1))
        rc = crop(rate_c, ho)
        coarse_two = (
            crop(one, ho)
            + half_step * (one_terms[0] - mid_terms[0])
            + half_step * rc * crop(low, ho)
            + crop(late, ho)
        ) / (1.0 + half_step * rc)
        delta_one = crop(one, ho) - crop(mid, ho)
        delta_two = coarse_two - crop(low, ho)
        result = [swept[0]]
        for m in range(1, 5):
            if last and m < 4:
                result.append(None)
                continue
            fine = prolong(interp_table[m][1] * delta_one + interp_table[m][2] * delta_two)
            result.append((crop(swept[m], ho) + crop((fine, 2 * ho), ho), ho))
        return result, new_terms[0]

    own_ext = space_halo(own_start, hs)
    begin = (jnp.where(first_slice, own_ext, from_previous_slice(own_start, hs)), hs)
    state = (own_ext, hs)
    state_terms = fine_E(state)
    step_parts = step_terms([state] * 5, [state_terms] * 5)
    for k in range(ROUNDS):
        last = k + 1 == ROUNDS
        states, begin_terms = advance(begin, step_parts, last)
        if not last:
            terms = [begin_terms] + [fine_E(states[m]) for m in range(1, 5)]
            own_parts = step_terms(states, terms)
            step_parts = packed_halo(
                [(crop(own_parts[m], 0), hs - 1 - m) for m in range(4)]
            )
            prior = from_previous_slice(crop(states[4], 0), hs)
            begin = (jnp.where(first_slice, own_ext, prior), hs)
    return from_even_odd(crop(states[4], 0))[None]


def solution(mesh):
    placed = (
        P("tm", None, "space", None, None),
        P(None, "space", None, None),
        P(None, "space", None, None),
        P(),
    )
    return jax.shard_map(
        per_device,
        mesh=mesh,
        in_specs=placed,
        out_specs=P("tm", None, "space", None, None),
        check_vma=False,
    )
```

```python
import math

import jax
import jax.numpy as jnp
from jax import lax
from jax.experimental import pallas as pl
from jax.experimental.pallas import tpu as pltpu
from jax.sharding import PartitionSpec as P

ROUNDS = 3

START_HALO = 5

step_length = 0.5


def lagrange_integral(nodes, j, upper_end):
    coeffs = [1.0]
    scale_down = 1.0
    for i in range(len(nodes)):
        if i != j:
            grown = [0.0] * (len(coeffs) + 1)
            for p in range(len(coeffs)):
                grown[p + 1] = grown[p + 1] + coeffs[p]
                grown[p] = grown[p] - nodes[i] * coeffs[p]
            coeffs = grown
            scale_down = scale_down * (nodes[j] - nodes[i])
    summed_up = 0.0
    for p in range(len(coeffs)):
        summed_up = summed_up + coeffs[p] * upper_end ** (p + 1) / (p + 1)
    return summed_up / scale_down


def node_tables():
    radical = math.sqrt(3.0 / 7.0)
    fine_nodes = [0.0, 0.5 * (1.0 - radical), 0.5, 0.5 * (1.0 + radical), 1.0]
    coarse_nodes = [0.0, 0.5, 1.0]
    integrals = [
        [lagrange_integral(fine_nodes, j, fine_nodes[m]) for j in range(5)] for m in range(5)
    ]
    spread_table = [
        [float(step_length * (integrals[m + 1][j] - integrals[m][j])) for j in range(5)]
        for m in range(4)
    ]
    grouped_table = [
        [spread_table[2 * c][j] + spread_table[2 * c + 1][j] for j in range(5)] for c in range(2)
    ]
    interp_table = []
    for m in range(5):
        weights_row = []
        for k in range(3):
            factor = 1.0
            for i in range(3):
                if i != k:
                    factor = (
                        factor
                        * (fine_nodes[m] - coarse_nodes[i])
                        / (coarse_nodes[k] - coarse_nodes[i])
                    )
            weights_row.append(factor)
        interp_table.append(weights_row)
    widths = [step_length * (fine_nodes[m + 1] - fine_nodes[m]) for m in range(4)]
    return (spread_table, grouped_table, interp_table, widths)


def to_even_odd(a):
    return jnp.concatenate([a[..., 0::2, :], a[..., 1::2, :]], axis=-2)


def from_even_odd(a):
    half = a.shape[-2] // 2
    woven = jnp.stack([a[..., :half, :], a[..., half:, :]], axis=-2)
    return woven.reshape(a.shape)


def crop(field, h):
    a, have = field
    d = have - h
    assert d >= 0
    if d == 0:
        return a
    return lax.slice_in_dim(a, d, a.shape[-3] - d, axis=a.ndim - 3)


def space_halo(a, h):
    if h == 0:
        return a
    size = lax.axis_size("space")
    rows = a.shape[-3]
    assert h <= rows
    up = [(i, (i + 1) % size) for i in range(size)]
    down = [((i + 1) % size, i) for i in range(size)]
    before = lax.ppermute(lax.slice_in_dim(a, rows - h, rows, axis=a.ndim - 3), "space", up)
    after = lax.ppermute(lax.slice_in_dim(a, 0, h, axis=a.ndim - 3), "space", down)
    return jnp.concatenate([before, a, after], axis=a.ndim - 3)


def from_previous_slice(a, h):
    slices = lax.axis_size("tm")
    size = lax.axis_size("space")
    rows = a.shape[-3]
    axes = ("tm", "space")

    def moved(piece, shift):
        pairs = [
            (t * size + s, (t + 1) * size + (s + shift) % size)
            for t in range(slices - 1)
            for s in range(size)
        ]
        return lax.ppermute(piece, axes, pairs)

    centre = moved(a, 0)
    if h == 0:
        return centre
    before = moved(lax.slice_in_dim(a, rows - h, rows, axis=a.ndim - 3), 1)
    after = moved(lax.slice_in_dim(a, 0, h, axis=a.ndim - 3), -1)
    return jnp.concatenate([before, centre, after], axis=a.ndim - 3)


def react_terms(field, laplace, diffusivity, source):
    first_part = field[0]
    second_part = field[1]
    product = first_part * second_part * second_part
    return jnp.stack(
        [
            diffusivity[0] * laplace[0] - product + source[0],
            diffusivity[1] * laplace[1] + product + source[1],
        ],
        axis=0,
    )


def fine_laplace(a):
    centre = a[..., 1:-1, :, :]
    pair_x = a[..., 2:, :, :] + a[..., :-2, :, :]
    half = centre.shape[-2] // 2
    even = centre[..., :half, :]
    odd = centre[..., half:, :]
    pair_y = jnp.concatenate(
        [odd + jnp.roll(odd, 1, -2), jnp.roll(even, -1, -2) + even], axis=-2
    )
    pair_z = jnp.roll(centre, -1, -1) + jnp.roll(centre, 1, -1)
    return pair_x + pair_y + pair_z - 6.0 * centre


def coarse_laplace(a):
    centre = a[..., 1:-1, :, :]
    pair_x = a[..., 2:, :, :] + a[..., :-2, :, :]
    pair_y = jnp.roll(centre, -1, -2) + jnp.roll(centre, 1, -2)
    pair_z = jnp.roll(centre, -1, -1) + jnp.roll(centre, 1, -1)
    return (pair_x - 2.0 * centre) * 0.25 + (pair_y - 2.0 * centre) * 0.25 + (
        pair_z - 2.0 * centre
    )


def restrict(field):
    a, h = field
    h2 = h - h % 2
    a = crop(field, h2)
    rows = a.shape[-3]
    half = a.shape[-2] // 2
    pairs = a.reshape(a.shape[:-3] + (rows // 2, 2) + a.shape[-2:])
    even = pairs[..., :half, :]
    odd = pairs[..., half:, :]
    upper = even[..., 0, :, :] + even[..., 1, :, :]
    lower = odd[..., 0, :, :] + odd[..., 1, :, :]
    return (upper + lower) * 0.25, h2 // 2


def prolong(a):
    rows = jnp.repeat(a, 2, axis=a.ndim - 3)
    return jnp.concatenate([rows, rows], axis=-2)


def kernel_laplace(f):
    centre = f[:, 1:-1]
    pair_x = f[:, 2:] + f[:, :-2]
    half = centre.shape[2] // 2
    even = centre[:, :, :half]
    odd = centre[:, :, half:]
    pair_y = jnp.concatenate(
        [odd + pltpu.roll(odd, 1, 2), pltpu.roll(even, half - 1, 2) + even], axis=2
    )
    lanes = centre.shape[3]
    pair_z = pltpu.roll(centre, lanes - 1, 3) + pltpu.roll(centre, 1, 3)
    return pair_x + pair_y + pair_z - 6.0 * centre


def sweep_kernel(diff_ref, b_ref, a0_ref, a1_ref, a2_ref, a3_ref, dec_ref, src_ref,
                 n1_ref, n2_ref, n3_ref, n4_ref, e0_ref, s0_ref, s1_ref):
    spread_table, grouped_table, interp_table, widths = node_tables()
    rows = e0_ref.shape[1]
    hs = (b_ref.shape[1] - rows) // 2
    hd = (dec_ref.shape[1] - rows) // 2
    d0 = diff_ref[0]
    d1 = diff_ref[1]

    def at(ref, h):
        off = hd - h
        return ref[:, off:off + rows + 2 * h]

    def cut(v, have, h):
        d = have - h
        return v[:, d:v.shape[1] - d]

    def terms(f, h):
        laplace = kernel_laplace(f)
        centre = f[:, 1:-1]
        s = at(src_ref, h - 1)
        product = centre[0] * centre[1] * centre[1]
        return jnp.stack([d0 * laplace[0] - product + s[0], d1 * laplace[1] + product + s[1]])

    parts = [a0_ref, a1_ref, a2_ref, a3_ref]
    swept = [b_ref[...]]
    found = []
    for m in range(4):
        have = hs - m
        e = terms(swept[m], have)
        found.append(e)
        h = have - 1
        numerator = (cut(swept[m], have, h) + widths[m] * e) + parts[m][...]
        swept.append(numerator / (1.0 + widths[m] * at(dec_ref, h)))
    found.append(terms(swept[4], hs - 4))
    dec0 = at(dec_ref, 0)
    fulls = [cut(found[j], hs - 1 - j, 0) - dec0 * cut(swept[j], hs - j, 0) for j in range(5)]
    for c, out in ((0, s0_ref), (1, s1_ref)):
        summed = grouped_table[c][0] * fulls[0]
        for j in range(1, 5):
            summed = summed + grouped_table[c][j] * fulls[j]
        out[...] = summed
    for m, out in ((1, n1_ref), (2, n2_ref), (3, n3_ref), (4, n4_ref)):
        out[...] = cut(swept[m], hs - m, 1)
    e0_ref[...] = cut(found[0], hs - 1, 0)


def fine_sweep(diffusivity, begin, parts, decay, src):
    rows = begin.shape[1] - 2 * START_HALO
    shape = begin.shape
    wide = jax.ShapeDtypeStruct((shape[0], rows + 2) + shape[2:], jnp.float32)
    own = jax.ShapeDtypeStruct((shape[0], rows) + shape[2:], jnp.float32)
    vmem = pl.BlockSpec(memory_space=pltpu.VMEM)
    return pl.pallas_call(
        sweep_kernel,
        out_shape=(wide, wide, wide, wide, own, own, own),
        in_specs=[pl.BlockSpec(memory_space=pltpu.SMEM)] + [vmem] * 7,
        out_specs=(vmem,) * 7,
    )(diffusivity, begin, *parts, decay, src)


def packed_halo(fields):
    size = lax.axis_size("space")
    rows = fields[0][0].shape[-3]
    axis = fields[0][0].ndim - 3
    up = [(i, (i + 1) % size) for i in range(size)]
    down = [((i + 1) % size, i) for i in range(size)]
    lasts = jnp.concatenate(
        [lax.slice_in_dim(a, rows - w, rows, axis=axis) for a, w in fields], axis=axis
    )
    firsts = jnp.concatenate([lax.slice_in_dim(a, 0, w, axis=axis) for a, w in fields], axis=axis)
    before = lax.ppermute(lasts, "space", up)
    after = lax.ppermute(firsts, "space", down)
    out = []
    offset = 0
    for a, w in fields:
        out.append(
            (
                jnp.concatenate(
                    [
                        lax.slice_in_dim(before, offset, offset + w, axis=axis),
                        a,
                        lax.slice_in_dim(after, offset, offset + w, axis=axis),
                    ],
                    axis=axis,
                ),
                w,
            )
        )
        offset += w
    return out


def per_device(initial, decay_rate, source, diffusivity):
    spread_table, grouped_table, interp_table, widths = node_tables()
    first_slice = lax.axis_index("tm") == 0
    hs = START_HALO
    assert hs == 5 and initial.shape[-3] >= hs
    hfix = hs - 1

    own_start = to_even_odd(initial[0])
    fixed = space_halo(jnp.stack([to_even_odd(decay_rate), to_even_odd(source)]), hfix)
    decay = (fixed[0], hfix)
    src = (fixed[1], hfix)
    rate_c = restrict(decay)
    source_c = restrict(src)

    def fine_E(field):
        a, h = field
        laplace = fine_laplace(a)
        return react_terms(a[..., 1:-1, :, :], laplace, diffusivity, crop(src, h - 1)), h - 1

    def coarse_E(field):
        a, h = field
        laplace = coarse_laplace(a)
        return react_terms(a[..., 1:-1, :, :], laplace, diffusivity, crop(source_c, h - 1)), h - 1

    def full(field, field_E):
        h = min(field[1], field_E[1])
        return crop(field_E, h) - crop(decay, h) * crop(field, h), h

    def step_terms(states, terms):
        fulls = [full(states[j], terms[j]) for j in range(5)]
        hf = min(f[1] for f in fulls)
        out = []
        for m in range(4):
            h = min(hf, terms[m][1], states[m + 1][1])
            summed = spread_table[m][0] * crop(fulls[0], h)
            for j in range(1, 5):
                summed = summed + spread_table[m][j] * crop(fulls[j], h)
            own = (
                widths[m] * crop(decay, h) * crop(states[m + 1], h)
                - widths[m] * crop(terms[m], h)
            ) + summed
            out.append((own, h))
        return out

    def advance(begin, step_parts, last):
        parts = [crop(step_parts[m], hs - 1 - m) for m in range(4)]
        n1, n2, n3, n4, e0, s0, s1 = fine_sweep(
            diffusivity, begin[0], parts, decay[0], src[0]
        )
        swept = [begin, (n1, 1), (n2, 1), (n3, 1), (n4, 1)]
        begin_terms = (e0, 0)
        integrated = [restrict((s0, 0)), restrict((s1, 0))]
        coarse_vals = [restrict(swept[0]), restrict(swept[2]), restrict(swept[4])]
        half_step = 0.5 * step_length
        rc = crop(rate_c, 0)
        coarse_one = (
            crop(coarse_vals[0], 0)
            + half_step * rc * crop(coarse_vals[1], 0)
            + crop(integrated[0], 0)
        ) / (1.0 + half_step * rc)
        if last:
            ho = 0
            one, mid = packed_halo([(coarse_one, 1), (crop(coarse_vals[1], 0), 1)])
            low, late = coarse_vals[2], integrated[1]
        else:
            ho = 1
            one, mid, low, late = packed_halo(
                [
                    (coarse_one, 2),
                    (crop(coarse_vals[1], 0), 2),
                    (crop(coarse_vals[2], 0), 1),
                    (crop(integrated[1], 0), 1),
                ]
            )
        one_terms = coarse_E((crop(one, ho + 1), ho + 1))
        mid_terms = coarse_E((crop(mid, ho + 1), ho + 1))
        rc = crop(rate_c, ho)
        coarse_two = (
            crop(one, ho)
            + half_step * (one_terms[0] - mid_terms[0])
            + half_step * rc * crop(low, ho)
            + crop(late, ho)
        ) / (1.0 + half_step * rc)
        delta_one = crop(one, ho) - crop(mid, ho)
        delta_two = coarse_two - crop(low, ho)
        result = [swept[0]]
        for m in range(1, 5):
            if last and m < 4:
                result.append(None)
                continue
            fine = prolong(interp_table[m][1] * delta_one + interp_table[m][2] * delta_two)
            result.append((crop(swept[m], ho) + crop((fine, 2 * ho), ho), ho))
        return result, begin_terms

    own_ext = space_halo(own_start, hs)
    begin = (jnp.where(first_slice, own_ext, from_previous_slice(own_start, hs)), hs)
    state = (own_ext, hs)
    state_terms = fine_E(state)
    step_parts = step_terms([state] * 5, [state_terms] * 5)
    for k in range(ROUNDS):
        last = k + 1 == ROUNDS
        states, begin_terms = advance(begin, step_parts, last)
        if not last:
            terms = [begin_terms] + [fine_E(states[m]) for m in range(1, 5)]
            own_parts = step_terms(states, terms)
            step_parts = packed_halo(
                [(crop(own_parts[m], 0), hs - 1 - m) for m in range(4)]
            )
            prior = from_previous_slice(crop(states[4], 0), hs)
            begin = (jnp.where(first_slice, own_ext, prior), hs)
    return from_even_odd(crop(states[4], 0))[None]


def solution(mesh):
    placed = (
        P("tm", None, "space", None, None),
        P(None, "space", None, None),
        P(None, "space", None, None),
        P(),
    )
    return jax.shard_map(
        per_device,
        mesh=mesh,
        in_specs=placed,
        out_specs=P("tm", None, "space", None, None),
        check_vma=False,
    )
```

```python
import math

import jax
import jax.numpy as jnp
from jax import lax
from jax.experimental import pallas as pl
from jax.experimental.pallas import tpu as pltpu
from jax.sharding import PartitionSpec as P

ROUNDS = 3

START_HALO = 5

step_length = 0.5


def lagrange_integral(nodes, j, upper_end):
    coeffs = [1.0]
    scale_down = 1.0
    for i in range(len(nodes)):
        if i != j:
            grown = [0.0] * (len(coeffs) + 1)
            for p in range(len(coeffs)):
                grown[p + 1] = grown[p + 1] + coeffs[p]
                grown[p] = grown[p] - nodes[i] * coeffs[p]
            coeffs = grown
            scale_down = scale_down * (nodes[j] - nodes[i])
    summed_up = 0.0
    for p in range(len(coeffs)):
        summed_up = summed_up + coeffs[p] * upper_end ** (p + 1) / (p + 1)
    return summed_up / scale_down


def node_tables():
    radical = math.sqrt(3.0 / 7.0)
    fine_nodes = [0.0, 0.5 * (1.0 - radical), 0.5, 0.5 * (1.0 + radical), 1.0]
    coarse_nodes = [0.0, 0.5, 1.0]
    integrals = [
        [lagrange_integral(fine_nodes, j, fine_nodes[m]) for j in range(5)] for m in range(5)
    ]
    spread_table = [
        [float(step_length * (integrals[m + 1][j] - integrals[m][j])) for j in range(5)]
        for m in range(4)
    ]
    grouped_table = [
        [spread_table[2 * c][j] + spread_table[2 * c + 1][j] for j in range(5)] for c in range(2)
    ]
    interp_table = []
    for m in range(5):
        weights_row = []
        for k in range(3):
            factor = 1.0
            for i in range(3):
                if i != k:
                    factor = (
                        factor
                        * (fine_nodes[m] - coarse_nodes[i])
                        / (coarse_nodes[k] - coarse_nodes[i])
                    )
            weights_row.append(factor)
        interp_table.append(weights_row)
    widths = [step_length * (fine_nodes[m + 1] - fine_nodes[m]) for m in range(4)]
    return (spread_table, grouped_table, interp_table, widths)


def to_even_odd(a):
    return jnp.concatenate([a[..., 0::2, :], a[..., 1::2, :]], axis=-2)


def from_even_odd(a):
    half = a.shape[-2] // 2
    woven = jnp.stack([a[..., :half, :], a[..., half:, :]], axis=-2)
    return woven.reshape(a.shape)


def crop(field, h):
    a, have = field
    d = have - h
    assert d >= 0
    if d == 0:
        return a
    return lax.slice_in_dim(a, d, a.shape[-3] - d, axis=a.ndim - 3)


def space_halo(a, h):
    if h == 0:
        return a
    size = lax.axis_size("space")
    rows = a.shape[-3]
    assert h <= rows
    up = [(i, (i + 1) % size) for i in range(size)]
    down = [((i + 1) % size, i) for i in range(size)]
    before = lax.ppermute(lax.slice_in_dim(a, rows - h, rows, axis=a.ndim - 3), "space", up)
    after = lax.ppermute(lax.slice_in_dim(a, 0, h, axis=a.ndim - 3), "space", down)
    return jnp.concatenate([before, a, after], axis=a.ndim - 3)


def from_previous_slice(a, h):
    slices = lax.axis_size("tm")
    size = lax.axis_size("space")
    rows = a.shape[-3]
    axes = ("tm", "space")

    def moved(piece, shift):
        pairs = [
            (t * size + s, (t + 1) * size + (s + shift) % size)
            for t in range(slices - 1)
            for s in range(size)
        ]
        return lax.ppermute(piece, axes, pairs)

    centre = moved(a, 0)
    if h == 0:
        return centre
    before = moved(lax.slice_in_dim(a, rows - h, rows, axis=a.ndim - 3), 1)
    after = moved(lax.slice_in_dim(a, 0, h, axis=a.ndim - 3), -1)
    return jnp.concatenate([before, centre, after], axis=a.ndim - 3)


def react_terms(field, laplace, diffusivity, source):
    first_part = field[0]
    second_part = field[1]
    product = first_part * second_part * second_part
    return jnp.stack(
        [
            diffusivity[0] * laplace[0] - product + source[0],
            diffusivity[1] * laplace[1] + product + source[1],
        ],
        axis=0,
    )


def fine_laplace(a):
    centre = a[..., 1:-1, :, :]
    pair_x = a[..., 2:, :, :] + a[..., :-2, :, :]
    half = centre.shape[-2] // 2
    even = centre[..., :half, :]
    odd = centre[..., half:, :]
    pair_y = jnp.concatenate(
        [odd + jnp.roll(odd, 1, -2), jnp.roll(even, -1, -2) + even], axis=-2
    )
    pair_z = jnp.roll(centre, -1, -1) + jnp.roll(centre, 1, -1)
    return pair_x + pair_y + pair_z - 6.0 * centre


def coarse_laplace(a):
    centre = a[..., 1:-1, :, :]
    pair_x = a[..., 2:, :, :] + a[..., :-2, :, :]
    pair_y = jnp.roll(centre, -1, -2) + jnp.roll(centre, 1, -2)
    pair_z = jnp.roll(centre, -1, -1) + jnp.roll(centre, 1, -1)
    return (pair_x - 2.0 * centre) * 0.25 + (pair_y - 2.0 * centre) * 0.25 + (
        pair_z - 2.0 * centre
    )


def restrict(field):
    a, h = field
    h2 = h - h % 2
    a = crop(field, h2)
    rows = a.shape[-3]
    half = a.shape[-2] // 2
    pairs = a.reshape(a.shape[:-3] + (rows // 2, 2) + a.shape[-2:])
    even = pairs[..., :half, :]
    odd = pairs[..., half:, :]
    upper = even[..., 0, :, :] + even[..., 1, :, :]
    lower = odd[..., 0, :, :] + odd[..., 1, :, :]
    return (upper + lower) * 0.25, h2 // 2


def prolong(a):
    rows = jnp.repeat(a, 2, axis=a.ndim - 3)
    return jnp.concatenate([rows, rows], axis=-2)


def kernel_laplace(f):
    centre = f[:, 1:-1]
    pair_x = f[:, 2:] + f[:, :-2]
    half = centre.shape[2] // 2
    even = centre[:, :, :half]
    odd = centre[:, :, half:]
    pair_y = jnp.concatenate(
        [odd + pltpu.roll(odd, 1, 2), pltpu.roll(even, half - 1, 2) + even], axis=2
    )
    lanes = centre.shape[3]
    pair_z = pltpu.roll(centre, lanes - 1, 3) + pltpu.roll(centre, 1, 3)
    return pair_x + pair_y + pair_z - 6.0 * centre


def sweep_kernel(diff_ref, b_ref, own_ref, before_ref, after_ref, dec_ref, src_ref,
                 n1_ref, n2_ref, n3_ref, n4_ref, e0_ref, s0_ref, s1_ref):
    spread_table, grouped_table, interp_table, widths = node_tables()
    rows = e0_ref.shape[1]
    hs = (b_ref.shape[1] - rows) // 2
    hd = (dec_ref.shape[1] - rows) // 2
    d0 = diff_ref[0]
    d1 = diff_ref[1]

    def at(ref, h):
        off = hd - h
        return ref[:, off:off + rows + 2 * h]

    def cut(v, have, h):
        d = have - h
        return v[:, d:v.shape[1] - d]

    def terms(f, h):
        laplace = kernel_laplace(f)
        centre = f[:, 1:-1]
        s = at(src_ref, h - 1)
        product = centre[0] * centre[1] * centre[1]
        return jnp.stack([d0 * laplace[0] - product + s[0], d1 * laplace[1] + product + s[1]])

    parts = []
    offset = 0
    for m in range(4):
        w = hs - 1 - m
        parts.append(
            jnp.concatenate(
                [before_ref[:, offset:offset + w], own_ref[m], after_ref[:, offset:offset + w]],
                axis=1,
            )
        )
        offset += w
    swept = [b_ref[...]]
    found = []
    for m in range(4):
        have = hs - m
        e = terms(swept[m], have)
        found.append(e)
        h = have - 1
        numerator = (cut(swept[m], have, h) + widths[m] * e) + parts[m]
        swept.append(numerator / (1.0 + widths[m] * at(dec_ref, h)))
    found.append(terms(swept[4], hs - 4))
    dec0 = at(dec_ref, 0)
    fulls = [cut(found[j], hs - 1 - j, 0) - dec0 * cut(swept[j], hs - j, 0) for j in range(5)]
    for c, out in ((0, s0_ref), (1, s1_ref)):
        summed = grouped_table[c][0] * fulls[0]
        for j in range(1, 5):
            summed = summed + grouped_table[c][j] * fulls[j]
        out[...] = summed
    for m, out in ((1, n1_ref), (2, n2_ref), (3, n3_ref), (4, n4_ref)):
        out[...] = cut(swept[m], hs - m, 1)
    e0_ref[...] = cut(found[0], hs - 1, 0)


def fine_sweep(diffusivity, begin, parts, decay, src):
    rows = begin.shape[1] - 2 * START_HALO
    shape = begin.shape
    wide = jax.ShapeDtypeStruct((shape[0], rows + 2) + shape[2:], jnp.float32)
    own = jax.ShapeDtypeStruct((shape[0], rows) + shape[2:], jnp.float32)
    vmem = pl.BlockSpec(memory_space=pltpu.VMEM)
    return pl.pallas_call(
        sweep_kernel,
        out_shape=(wide, wide, wide, wide, own, own, own),
        in_specs=[pl.BlockSpec(memory_space=pltpu.SMEM)] + [vmem] * 6,
        out_specs=(vmem,) * 7,
    )(diffusivity, begin, *parts, decay, src)


def coarse_kernel_laplace(f):
    centre = f[:, 1:-1]
    pair_x = f[:, 2:] + f[:, :-2]
    ny = centre.shape[2]
    lanes = centre.shape[3]
    pair_y = pltpu.roll(centre, ny - 1, 2) + pltpu.roll(centre, 1, 2)
    pair_z = pltpu.roll(centre, lanes - 1, 3) + pltpu.roll(centre, 1, 3)
    return (pair_x - 2.0 * centre) * 0.25 + (pair_y - 2.0 * centre) * 0.25 + (
        pair_z - 2.0 * centre
    )


def finish_kernel(diff_ref, one_ref, mid_ref, low_ref, late_ref, rate_ref, csrc_ref,
                  n1_ref, n2_ref, n3_ref, n4_ref, b_ref, e0_ref, dec_ref, src_ref, *outs):
    spread_table, grouped_table, interp_table, widths = node_tables()
    last = len(outs) == 1
    rows = e0_ref.shape[1]
    crows = rows // 2
    ho = (low_ref.shape[1] - crows) // 2
    hcr = (rate_ref.shape[1] - crows) // 2
    hd = (dec_ref.shape[1] - rows) // 2
    hs = (b_ref.shape[1] - rows) // 2
    d0 = diff_ref[0]
    d1 = diff_ref[1]

    def at(ref, h, size, have):
        off = have - h
        return ref[:, off:off + size + 2 * h]

    def cut(v, have, h):
        d = have - h
        return v[:, d:v.shape[1] - d]

    def react(centre, laplace, s):
        product = centre[0] * centre[1] * centre[1]
        return jnp.stack([d0 * laplace[0] - product + s[0], d1 * laplace[1] + product + s[1]])

    def coarse_terms(v):
        return react(v[:, 1:-1], coarse_kernel_laplace(v), at(csrc_ref, ho, crows, hcr))

    half_step = 0.5 * step_length
    one = one_ref[...]
    mid = mid_ref[...]
    rc = at(rate_ref, ho, crows, hcr)
    coarse_two = (
        cut(one, ho + 1, ho)
        + half_step * (coarse_terms(one) - coarse_terms(mid))
        + half_step * rc * low_ref[...]
        + late_ref[...]
    ) / (1.0 + half_step * rc)
    delta_one = cut(one, ho + 1, ho) - cut(mid, ho + 1, ho)
    delta_two = coarse_two - low_ref[...]

    def prolonged(c):
        shape = c.shape
        doubled = jnp.broadcast_to(c[:, :, None], (shape[0], shape[1], 2) + shape[2:])
        doubled = doubled.reshape((shape[0], 2 * shape[1]) + shape[2:])
        return jnp.concatenate([doubled, doubled], axis=2)

    news = {}
    for m, ref in ((1, n1_ref), (2, n2_ref), (3, n3_ref), (4, n4_ref)):
        if last and m < 4:
            continue
        fine = prolonged(interp_table[m][1] * delta_one + interp_table[m][2] * delta_two)
        news[m] = cut(ref[...], 1, ho) + cut(fine, 2 * ho, ho)
    if last:
        outs[0][...] = news[4]
        return
    own_out, lasts_out, firsts_out, u4_out = outs
    src1 = at(src_ref, 0, rows, hd)
    dec0 = at(dec_ref, 0, rows, hd)
    states = [at(b_ref, 0, rows, hs)] + [cut(news[m], 1, 0) for m in range(1, 5)]
    terms = [e0_ref[...]] + [
        react(cut(news[m], 1, 0), kernel_laplace(news[m]), src1) for m in range(1, 5)
    ]
    fulls = [terms[j] - dec0 * states[j] for j in range(5)]
    offset = 0
    for m in range(4):
        summed = spread_table[m][0] * fulls[0]
        for j in range(1, 5):
            summed = summed + spread_table[m][j] * fulls[j]
        part = (widths[m] * dec0 * states[m + 1] - widths[m] * terms[m]) + summed
        own_out[m] = part
        w = hs - 1 - m
        lasts_out[:, offset:offset + w] = part[:, rows - w:]
        firsts_out[:, offset:offset + w] = part[:, :w]
        offset += w
    u4_out[...] = states[4]


def finish_round(diffusivity, coarse, rate_c, source_c, swept, e0, decay, src, last):
    begin = swept[0]
    shape = begin.shape
    rows = e0.shape[1]
    field = jax.ShapeDtypeStruct((shape[0], rows) + shape[2:], jnp.float32)
    if last:
        out_shape = (field,)
    else:
        sent = sum(START_HALO - 1 - m for m in range(4))
        edge = jax.ShapeDtypeStruct((shape[0], sent) + shape[2:], jnp.float32)
        out_shape = (jax.ShapeDtypeStruct((4,) + field.shape, jnp.float32), edge, edge, field)
    vmem = pl.BlockSpec(memory_space=pltpu.VMEM)
    args = (diffusivity, *coarse, rate_c, source_c, *swept[1:], begin, e0, decay, src)
    return pl.pallas_call(
        finish_kernel,
        out_shape=out_shape,
        in_specs=[pl.BlockSpec(memory_space=pltpu.SMEM)] + [vmem] * (len(args) - 1),
        out_specs=(vmem,) * len(out_shape),
    )(*args)


def packed_halo(fields):
    size = lax.axis_size("space")
    rows = fields[0][0].shape[-3]
    axis = fields[0][0].ndim - 3
    up = [(i, (i + 1) % size) for i in range(size)]
    down = [((i + 1) % size, i) for i in range(size)]
    lasts = jnp.concatenate(
        [lax.slice_in_dim(a, rows - w, rows, axis=axis) for a, w in fields], axis=axis
    )
    firsts = jnp.concatenate([lax.slice_in_dim(a, 0, w, axis=axis) for a, w in fields], axis=axis)
    before = lax.ppermute(lasts, "space", up)
    after = lax.ppermute(firsts, "space", down)
    out = []
    offset = 0
    for a, w in fields:
        out.append(
            (
                jnp.concatenate(
                    [
                        lax.slice_in_dim(before, offset, offset + w, axis=axis),
                        a,
                        lax.slice_in_dim(after, offset, offset + w, axis=axis),
                    ],
                    axis=axis,
                ),
                w,
            )
        )
        offset += w
    return out


def per_device(initial, decay_rate, source, diffusivity):
    spread_table, grouped_table, interp_table, widths = node_tables()
    first_slice = lax.axis_index("tm") == 0
    hs = START_HALO
    assert hs == 5 and initial.shape[-3] >= hs
    hfix = hs - 1

    own_start = to_even_odd(initial[0])
    fixed = space_halo(jnp.stack([to_even_odd(decay_rate), to_even_odd(source)]), hfix)
    decay = (fixed[0], hfix)
    src = (fixed[1], hfix)
    rate_c = restrict(decay)
    source_c = restrict(src)

    def fine_E(field):
        a, h = field
        laplace = fine_laplace(a)
        return react_terms(a[..., 1:-1, :, :], laplace, diffusivity, crop(src, h - 1)), h - 1

    def coarse_E(field):
        a, h = field
        laplace = coarse_laplace(a)
        return react_terms(a[..., 1:-1, :, :], laplace, diffusivity, crop(source_c, h - 1)), h - 1

    def full(field, field_E):
        h = min(field[1], field_E[1])
        return crop(field_E, h) - crop(decay, h) * crop(field, h), h

    def step_terms(states, terms):
        fulls = [full(states[j], terms[j]) for j in range(5)]
        hf = min(f[1] for f in fulls)
        out = []
        for m in range(4):
            h = min(hf, terms[m][1], states[m + 1][1])
            summed = spread_table[m][0] * crop(fulls[0], h)
            for j in range(1, 5):
                summed = summed + spread_table[m][j] * crop(fulls[j], h)
            own = (
                widths[m] * crop(decay, h) * crop(states[m + 1], h)
                - widths[m] * crop(terms[m], h)
            ) + summed
            out.append((own, h))
        return out

    def advance(begin, pieces, last):
        n1, n2, n3, n4, e0, s0, s1 = fine_sweep(diffusivity, begin[0], pieces, decay[0], src[0])
        coarse_vals = [restrict(begin), restrict((n2, 1)), restrict((n4, 1))]
        coarse_vals = [crop(v, 0) for v in coarse_vals]
        integrated = [crop(restrict((s0, 0)), 0), crop(restrict((s1, 0)), 0)]
        half_step = 0.5 * step_length
        rc = crop(rate_c, 0)
        coarse_one = (
            coarse_vals[0] + half_step * rc * coarse_vals[1] + integrated[0]
        ) / (1.0 + half_step * rc)
        if last:
            one, mid = packed_halo([(coarse_one, 1), (coarse_vals[1], 1)])
            coarse = (one[0], mid[0], coarse_vals[2], integrated[1])
        else:
            one, mid, low, late = packed_halo(
                [(coarse_one, 2), (coarse_vals[1], 2), (coarse_vals[2], 1), (integrated[1], 1)]
            )
            coarse = (one[0], mid[0], low[0], late[0])
        return finish_round(
            diffusivity, coarse, rate_c[0], source_c[0],
            (begin[0], n1, n2, n3, n4), e0, decay[0], src[0], last,
        )

    size = lax.axis_size("space")
    up = [(i, (i + 1) % size) for i in range(size)]
    down = [((i + 1) % size, i) for i in range(size)]
    rows = own_start.shape[-3]
    own_ext = space_halo(own_start, hs)
    begin = (jnp.where(first_slice, own_ext, from_previous_slice(own_start, hs)), hs)
    state = (own_ext, hs)
    state_terms = fine_E(state)
    parts = step_terms([state] * 5, [state_terms] * 5)
    wide = [crop(parts[m], hs - 1) for m in range(4)]
    edge = hs - 1
    pieces = (
        jnp.stack([lax.slice_in_dim(p, edge, edge + rows, axis=1) for p in wide]),
        jnp.concatenate(
            [lax.slice_in_dim(p, m, edge, axis=1) for m, p in enumerate(wide)], axis=1
        ),
        jnp.concatenate(
            [lax.slice_in_dim(p, edge + rows, edge + rows + edge - m, axis=1)
             for m, p in enumerate(wide)], axis=1
        ),
    )
    for k in range(ROUNDS):
        last = k + 1 == ROUNDS
        outs = advance(begin, pieces, last)
        if not last:
            own4, lasts, firsts, u4 = outs
            pieces = (
                own4,
                lax.ppermute(lasts, "space", up),
                lax.ppermute(firsts, "space", down),
            )
            prior = from_previous_slice(u4, hs)
            begin = (jnp.where(first_slice, own_ext, prior), hs)
    return from_even_odd(outs[0])[None]


def solution(mesh):
    placed = (
        P("tm", None, "space", None, None),
        P(None, "space", None, None),
        P(None, "space", None, None),
        P(),
    )
    return jax.shard_map(
        per_device,
        mesh=mesh,
        in_specs=placed,
        out_specs=P("tm", None, "space", None, None),
        check_vma=False,
    )
```

```python
import functools
import math

import jax
import jax.numpy as jnp
from jax import lax
from jax.experimental import pallas as pl
from jax.experimental.pallas import tpu as pltpu
from jax.sharding import PartitionSpec as P

ROUNDS = 3

START_HALO = 5

step_length = 0.5


def lagrange_integral(nodes, j, upper_end):
    coeffs = [1.0]
    scale_down = 1.0
    for i in range(len(nodes)):
        if i != j:
            grown = [0.0] * (len(coeffs) + 1)
            for p in range(len(coeffs)):
                grown[p + 1] = grown[p + 1] + coeffs[p]
                grown[p] = grown[p] - nodes[i] * coeffs[p]
            coeffs = grown
            scale_down = scale_down * (nodes[j] - nodes[i])
    summed_up = 0.0
    for p in range(len(coeffs)):
        summed_up = summed_up + coeffs[p] * upper_end ** (p + 1) / (p + 1)
    return summed_up / scale_down


def node_tables():
    radical = math.sqrt(3.0 / 7.0)
    fine_nodes = [0.0, 0.5 * (1.0 - radical), 0.5, 0.5 * (1.0 + radical), 1.0]
    coarse_nodes = [0.0, 0.5, 1.0]
    integrals = [
        [lagrange_integral(fine_nodes, j, fine_nodes[m]) for j in range(5)] for m in range(5)
    ]
    spread_table = [
        [float(step_length * (integrals[m + 1][j] - integrals[m][j])) for j in range(5)]
        for m in range(4)
    ]
    grouped_table = [
        [spread_table[2 * c][j] + spread_table[2 * c + 1][j] for j in range(5)] for c in range(2)
    ]
    interp_table = []
    for m in range(5):
        weights_row = []
        for k in range(3):
            factor = 1.0
            for i in range(3):
                if i != k:
                    factor = (
                        factor
                        * (fine_nodes[m] - coarse_nodes[i])
                        / (coarse_nodes[k] - coarse_nodes[i])
                    )
            weights_row.append(factor)
        interp_table.append(weights_row)
    widths = [step_length * (fine_nodes[m + 1] - fine_nodes[m]) for m in range(4)]
    return (spread_table, grouped_table, interp_table, widths)


def to_even_odd(a):
    return jnp.concatenate([a[..., 0::2, :], a[..., 1::2, :]], axis=-2)


def from_even_odd(a):
    half = a.shape[-2] // 2
    woven = jnp.stack([a[..., :half, :], a[..., half:, :]], axis=-2)
    return woven.reshape(a.shape)


def crop(field, h):
    a, have = field
    d = have - h
    assert d >= 0
    if d == 0:
        return a
    return lax.slice_in_dim(a, d, a.shape[-3] - d, axis=a.ndim - 3)


def space_halo(a, h):
    if h == 0:
        return a
    size = lax.axis_size("space")
    rows = a.shape[-3]
    assert h <= rows
    up = [(i, (i + 1) % size) for i in range(size)]
    down = [((i + 1) % size, i) for i in range(size)]
    before = lax.ppermute(lax.slice_in_dim(a, rows - h, rows, axis=a.ndim - 3), "space", up)
    after = lax.ppermute(lax.slice_in_dim(a, 0, h, axis=a.ndim - 3), "space", down)
    return jnp.concatenate([before, a, after], axis=a.ndim - 3)


def from_previous_slice(a, h):
    slices = lax.axis_size("tm")
    size = lax.axis_size("space")
    rows = a.shape[-3]
    axes = ("tm", "space")

    def moved(piece, shift):
        pairs = [
            (t * size + s, (t + 1) * size + (s + shift) % size)
            for t in range(slices - 1)
            for s in range(size)
        ]
        return lax.ppermute(piece, axes, pairs)

    centre = moved(a, 0)
    if h == 0:
        return centre
    before = moved(lax.slice_in_dim(a, rows - h, rows, axis=a.ndim - 3), 1)
    after = moved(lax.slice_in_dim(a, 0, h, axis=a.ndim - 3), -1)
    return jnp.concatenate([before, centre, after], axis=a.ndim - 3)


def react_terms(field, laplace, diffusivity, source):
    first_part = field[0]
    second_part = field[1]
    product = first_part * second_part * second_part
    return jnp.stack(
        [
            diffusivity[0] * laplace[0] - product + source[0],
            diffusivity[1] * laplace[1] + product + source[1],
        ],
        axis=0,
    )


def fine_laplace(a):
    centre = a[..., 1:-1, :, :]
    pair_x = a[..., 2:, :, :] + a[..., :-2, :, :]
    half = centre.shape[-2] // 2
    even = centre[..., :half, :]
    odd = centre[..., half:, :]
    pair_y = jnp.concatenate(
        [odd + jnp.roll(odd, 1, -2), jnp.roll(even, -1, -2) + even], axis=-2
    )
    pair_z = jnp.roll(centre, -1, -1) + jnp.roll(centre, 1, -1)
    return pair_x + pair_y + pair_z - 6.0 * centre


def coarse_laplace(a):
    centre = a[..., 1:-1, :, :]
    pair_x = a[..., 2:, :, :] + a[..., :-2, :, :]
    pair_y = jnp.roll(centre, -1, -2) + jnp.roll(centre, 1, -2)
    pair_z = jnp.roll(centre, -1, -1) + jnp.roll(centre, 1, -1)
    return (pair_x - 2.0 * centre) * 0.25 + (pair_y - 2.0 * centre) * 0.25 + (
        pair_z - 2.0 * centre
    )


def restrict(field):
    a, h = field
    h2 = h - h % 2
    a = crop(field, h2)
    rows = a.shape[-3]
    half = a.shape[-2] // 2
    pairs = a.reshape(a.shape[:-3] + (rows // 2, 2) + a.shape[-2:])
    even = pairs[..., :half, :]
    odd = pairs[..., half:, :]
    upper = even[..., 0, :, :] + even[..., 1, :, :]
    lower = odd[..., 0, :, :] + odd[..., 1, :, :]
    return (upper + lower) * 0.25, h2 // 2


def prolong(a):
    rows = jnp.repeat(a, 2, axis=a.ndim - 3)
    return jnp.concatenate([rows, rows], axis=-2)


def kernel_laplace(f):
    centre = f[:, 1:-1]
    pair_x = f[:, 2:] + f[:, :-2]
    half = centre.shape[2] // 2
    even = centre[:, :, :half]
    odd = centre[:, :, half:]
    pair_y = jnp.concatenate(
        [odd + pltpu.roll(odd, 1, 2), pltpu.roll(even, half - 1, 2) + even], axis=2
    )
    lanes = centre.shape[3]
    pair_z = pltpu.roll(centre, lanes - 1, 3) + pltpu.roll(centre, 1, 3)
    return pair_x + pair_y + pair_z - 6.0 * centre


def kernel_restrict(v):
    shape = v.shape
    pairs = v.reshape((shape[0], shape[1] // 2, 2) + shape[2:])
    half = shape[2] // 2
    even = pairs[:, :, :, :half]
    odd = pairs[:, :, :, half:]
    upper = even[:, :, 0] + even[:, :, 1]
    lower = odd[:, :, 0] + odd[:, :, 1]
    return (upper + lower) * 0.25


def sweep_kernel(widths_sent, diff_ref, b_ref, own_ref, before_ref, after_ref, dec_ref, src_ref,
                 rate_ref, n1_ref, n2_ref, n3_ref, n4_ref, e0_ref, cown_ref, clasts_ref,
                 cfirsts_ref):
    spread_table, grouped_table, interp_table, widths = node_tables()
    rows = e0_ref.shape[1]
    hs = (b_ref.shape[1] - rows) // 2
    hd = (dec_ref.shape[1] - rows) // 2
    d0 = diff_ref[0]
    d1 = diff_ref[1]

    def at(ref, h):
        off = hd - h
        return ref[:, off:off + rows + 2 * h]

    def cut(v, have, h):
        d = have - h
        return v[:, d:v.shape[1] - d]

    def terms(f, h):
        laplace = kernel_laplace(f)
        centre = f[:, 1:-1]
        s = at(src_ref, h - 1)
        product = centre[0] * centre[1] * centre[1]
        return jnp.stack([d0 * laplace[0] - product + s[0], d1 * laplace[1] + product + s[1]])

    parts = []
    offset = 0
    for m in range(4):
        w = hs - 1 - m
        parts.append(
            jnp.concatenate(
                [before_ref[:, offset:offset + w], own_ref[m], after_ref[:, offset:offset + w]],
                axis=1,
            )
        )
        offset += w
    swept = [b_ref[...]]
    found = []
    for m in range(4):
        have = hs - m
        e = terms(swept[m], have)
        found.append(e)
        h = have - 1
        numerator = (cut(swept[m], have, h) + widths[m] * e) + parts[m]
        swept.append(numerator / (1.0 + widths[m] * at(dec_ref, h)))
    found.append(terms(swept[4], hs - 4))
    dec0 = at(dec_ref, 0)
    fulls = [cut(found[j], hs - 1 - j, 0) - dec0 * cut(swept[j], hs - j, 0) for j in range(5)]
    integrated = []
    for c in range(2):
        summed = grouped_table[c][0] * fulls[0]
        for j in range(1, 5):
            summed = summed + grouped_table[c][j] * fulls[j]
        integrated.append(kernel_restrict(summed))
    crows = rows // 2
    hcr = (rate_ref.shape[1] - crows) // 2
    rc = rate_ref[:, hcr:hcr + crows]
    coarse_vals = [kernel_restrict(cut(swept[j], hs - j, 0)) for j in (0, 2, 4)]
    half_step = 0.5 * step_length
    coarse_one = (
        coarse_vals[0] + half_step * rc * coarse_vals[1] + integrated[0]
    ) / (1.0 + half_step * rc)
    sent = [coarse_one, coarse_vals[1], coarse_vals[2], integrated[1]]
    offset = 0
    for i, piece in enumerate(sent):
        cown_ref[i] = piece
        w = widths_sent[i]
        if w:
            clasts_ref[:, offset:offset + w] = piece[:, crows - w:]
            cfirsts_ref[:, offset:offset + w] = piece[:, :w]
        offset += w
    for m, out in ((1, n1_ref), (2, n2_ref), (3, n3_ref), (4, n4_ref)):
        out[...] = cut(swept[m], hs - m, 1)
    e0_ref[...] = cut(found[0], hs - 1, 0)


def fine_sweep(diffusivity, begin, parts, decay, src, rate_c, widths_sent):
    rows = begin.shape[1] - 2 * START_HALO
    shape = begin.shape
    wide = jax.ShapeDtypeStruct((shape[0], rows + 2) + shape[2:], jnp.float32)
    own = jax.ShapeDtypeStruct((shape[0], rows) + shape[2:], jnp.float32)
    cshape = (shape[0], rows // 2, shape[2] // 2, shape[3])
    cown = jax.ShapeDtypeStruct((4,) + cshape, jnp.float32)
    cedge = jax.ShapeDtypeStruct((shape[0], sum(widths_sent)) + cshape[2:], jnp.float32)
    vmem = pl.BlockSpec(memory_space=pltpu.VMEM)
    return pl.pallas_call(
        functools.partial(sweep_kernel, widths_sent),
        out_shape=(wide, wide, wide, wide, own, cown, cedge, cedge),
        in_specs=[pl.BlockSpec(memory_space=pltpu.SMEM)] + [vmem] * 7,
        out_specs=(vmem,) * 8,
    )(diffusivity, begin, *parts, decay, src, rate_c)


def coarse_kernel_laplace(f):
    centre = f[:, 1:-1]
    pair_x = f[:, 2:] + f[:, :-2]
    ny = centre.shape[2]
    lanes = centre.shape[3]
    pair_y = pltpu.roll(centre, ny - 1, 2) + pltpu.roll(centre, 1, 2)
    pair_z = pltpu.roll(centre, lanes - 1, 3) + pltpu.roll(centre, 1, 3)
    return (pair_x - 2.0 * centre) * 0.25 + (pair_y - 2.0 * centre) * 0.25 + (
        pair_z - 2.0 * centre
    )


def finish_kernel(widths_sent, diff_ref, cown_ref, cbefore_ref, cafter_ref, rate_ref, csrc_ref,
                  n1_ref, n2_ref, n3_ref, n4_ref, b_ref, e0_ref, dec_ref, src_ref, *outs):
    spread_table, grouped_table, interp_table, widths = node_tables()
    last = len(outs) == 1
    rows = e0_ref.shape[1]
    crows = rows // 2
    ho = widths_sent[2]
    joined = []
    offset = 0
    for i in range(4):
        w = widths_sent[i]
        if w:
            joined.append(
                jnp.concatenate(
                    [cbefore_ref[:, offset:offset + w], cown_ref[i], cafter_ref[:, offset:offset + w]],
                    axis=1,
                )
            )
        else:
            joined.append(cown_ref[i])
        offset += w
    one, mid, low, late = joined
    hcr = (rate_ref.shape[1] - crows) // 2
    hd = (dec_ref.shape[1] - rows) // 2
    hs = (b_ref.shape[1] - rows) // 2
    d0 = diff_ref[0]
    d1 = diff_ref[1]

    def at(ref, h, size, have):
        off = have - h
        return ref[:, off:off + size + 2 * h]

    def cut(v, have, h):
        d = have - h
        return v[:, d:v.shape[1] - d]

    def react(centre, laplace, s):
        product = centre[0] * centre[1] * centre[1]
        return jnp.stack([d0 * laplace[0] - product + s[0], d1 * laplace[1] + product + s[1]])

    def coarse_terms(v):
        return react(v[:, 1:-1], coarse_kernel_laplace(v), at(csrc_ref, ho, crows, hcr))

    half_step = 0.5 * step_length
    rc = at(rate_ref, ho, crows, hcr)
    coarse_two = (
        cut(one, ho + 1, ho)
        + half_step * (coarse_terms(one) - coarse_terms(mid))
        + half_step * rc * low
        + late
    ) / (1.0 + half_step * rc)
    delta_one = cut(one, ho + 1, ho) - cut(mid, ho + 1, ho)
    delta_two = coarse_two - low

    def prolonged(c):
        shape = c.shape
        doubled = jnp.broadcast_to(c[:, :, None], (shape[0], shape[1], 2) + shape[2:])
        doubled = doubled.reshape((shape[0], 2 * shape[1]) + shape[2:])
        return jnp.concatenate([doubled, doubled], axis=2)

    news = {}
    for m, ref in ((1, n1_ref), (2, n2_ref), (3, n3_ref), (4, n4_ref)):
        if last and m < 4:
            continue
        fine = prolonged(interp_table[m][1] * delta_one + interp_table[m][2] * delta_two)
        news[m] = cut(ref[...], 1, ho) + cut(fine, 2 * ho, ho)
    if last:
        outs[0][...] = news[4]
        return
    own_out, lasts_out, firsts_out, u4_out = outs
    src1 = at(src_ref, 0, rows, hd)
    dec0 = at(dec_ref, 0, rows, hd)
    states = [at(b_ref, 0, rows, hs)] + [cut(news[m], 1, 0) for m in range(1, 5)]
    terms = [e0_ref[...]] + [
        react(cut(news[m], 1, 0), kernel_laplace(news[m]), src1) for m in range(1, 5)
    ]
    fulls = [terms[j] - dec0 * states[j] for j in range(5)]
    offset = 0
    for m in range(4):
        summed = spread_table[m][0] * fulls[0]
        for j in range(1, 5):
            summed = summed + spread_table[m][j] * fulls[j]
        part = (widths[m] * dec0 * states[m + 1] - widths[m] * terms[m]) + summed
        own_out[m] = part
        w = hs - 1 - m
        lasts_out[:, offset:offset + w] = part[:, rows - w:]
        firsts_out[:, offset:offset + w] = part[:, :w]
        offset += w
    u4_out[...] = states[4]


def finish_round(diffusivity, coarse, rate_c, source_c, swept, e0, decay, src, last, widths_sent):
    begin = swept[0]
    shape = begin.shape
    rows = e0.shape[1]
    field = jax.ShapeDtypeStruct((shape[0], rows) + shape[2:], jnp.float32)
    if last:
        out_shape = (field,)
    else:
        sent = sum(START_HALO - 1 - m for m in range(4))
        edge = jax.ShapeDtypeStruct((shape[0], sent) + shape[2:], jnp.float32)
        out_shape = (jax.ShapeDtypeStruct((4,) + field.shape, jnp.float32), edge, edge, field)
    vmem = pl.BlockSpec(memory_space=pltpu.VMEM)
    args = (diffusivity, *coarse, rate_c, source_c, *swept[1:], begin, e0, decay, src)
    return pl.pallas_call(
        functools.partial(finish_kernel, widths_sent),
        out_shape=out_shape,
        in_specs=[pl.BlockSpec(memory_space=pltpu.SMEM)] + [vmem] * (len(args) - 1),
        out_specs=(vmem,) * len(out_shape),
    )(*args)


def packed_halo(fields):
    size = lax.axis_size("space")
    rows = fields[0][0].shape[-3]
    axis = fields[0][0].ndim - 3
    up = [(i, (i + 1) % size) for i in range(size)]
    down = [((i + 1) % size, i) for i in range(size)]
    lasts = jnp.concatenate(
        [lax.slice_in_dim(a, rows - w, rows, axis=axis) for a, w in fields], axis=axis
    )
    firsts = jnp.concatenate([lax.slice_in_dim(a, 0, w, axis=axis) for a, w in fields], axis=axis)
    before = lax.ppermute(lasts, "space", up)
    after = lax.ppermute(firsts, "space", down)
    out = []
    offset = 0
    for a, w in fields:
        out.append(
            (
                jnp.concatenate(
                    [
                        lax.slice_in_dim(before, offset, offset + w, axis=axis),
                        a,
                        lax.slice_in_dim(after, offset, offset + w, axis=axis),
                    ],
                    axis=axis,
                ),
                w,
            )
        )
        offset += w
    return out


def per_device(initial, decay_rate, source, diffusivity):
    spread_table, grouped_table, interp_table, widths = node_tables()
    first_slice = lax.axis_index("tm") == 0
    hs = START_HALO
    assert hs == 5 and initial.shape[-3] >= hs
    hfix = hs - 1

    own_start = to_even_odd(initial[0])
    fixed = space_halo(jnp.stack([to_even_odd(decay_rate), to_even_odd(source)]), hfix)
    decay = (fixed[0], hfix)
    src = (fixed[1], hfix)
    rate_c = restrict(decay)
    source_c = restrict(src)

    def fine_E(field):
        a, h = field
        laplace = fine_laplace(a)
        return react_terms(a[..., 1:-1, :, :], laplace, diffusivity, crop(src, h - 1)), h - 1

    def coarse_E(field):
        a, h = field
        laplace = coarse_laplace(a)
        return react_terms(a[..., 1:-1, :, :], laplace, diffusivity, crop(source_c, h - 1)), h - 1

    def full(field, field_E):
        h = min(field[1], field_E[1])
        return crop(field_E, h) - crop(decay, h) * crop(field, h), h

    def step_terms(states, terms):
        fulls = [full(states[j], terms[j]) for j in range(5)]
        hf = min(f[1] for f in fulls)
        out = []
        for m in range(4):
            h = min(hf, terms[m][1], states[m + 1][1])
            summed = spread_table[m][0] * crop(fulls[0], h)
            for j in range(1, 5):
                summed = summed + spread_table[m][j] * crop(fulls[j], h)
            own = (
                widths[m] * crop(decay, h) * crop(states[m + 1], h)
                - widths[m] * crop(terms[m], h)
            ) + summed
            out.append((own, h))
        return out

    def advance(begin, pieces, last):
        widths_sent = (1, 1, 0, 0) if last else (2, 2, 1, 1)
        n1, n2, n3, n4, e0, cown, clasts, cfirsts = fine_sweep(
            diffusivity, begin[0], pieces, decay[0], src[0], rate_c[0], widths_sent
        )
        coarse = (
            cown,
            lax.ppermute(clasts, "space", up),
            lax.ppermute(cfirsts, "space", down),
        )
        return finish_round(
            diffusivity, coarse, rate_c[0], source_c[0],
            (begin[0], n1, n2, n3, n4), e0, decay[0], src[0], last, widths_sent,
        )

    size = lax.axis_size("space")
    up = [(i, (i + 1) % size) for i in range(size)]
    down = [((i + 1) % size, i) for i in range(size)]
    rows = own_start.shape[-3]
    own_ext = space_halo(own_start, hs)
    begin = (jnp.where(first_slice, own_ext, from_previous_slice(own_start, hs)), hs)
    state = (own_ext, hs)
    state_terms = fine_E(state)
    parts = step_terms([state] * 5, [state_terms] * 5)
    wide = [crop(parts[m], hs - 1) for m in range(4)]
    edge = hs - 1
    pieces = (
        jnp.stack([lax.slice_in_dim(p, edge, edge + rows, axis=1) for p in wide]),
        jnp.concatenate(
            [lax.slice_in_dim(p, m, edge, axis=1) for m, p in enumerate(wide)], axis=1
        ),
        jnp.concatenate(
            [lax.slice_in_dim(p, edge + rows, edge + rows + edge - m, axis=1)
             for m, p in enumerate(wide)], axis=1
        ),
    )
    for k in range(ROUNDS):
        last = k + 1 == ROUNDS
        outs = advance(begin, pieces, last)
        if not last:
            own4, lasts, firsts, u4 = outs
            pieces = (
                own4,
                lax.ppermute(lasts, "space", up),
                lax.ppermute(firsts, "space", down),
            )
            prior = from_previous_slice(u4, hs)
            begin = (jnp.where(first_slice, own_ext, prior), hs)
    return from_even_odd(outs[0])[None]


def solution(mesh):
    placed = (
        P("tm", None, "space", None, None),
        P(None, "space", None, None),
        P(None, "space", None, None),
        P(),
    )
    return jax.shard_map(
        per_device,
        mesh=mesh,
        in_specs=placed,
        out_specs=P("tm", None, "space", None, None),
        check_vma=False,
    )
```

```python
import functools
import math

import jax
import jax.numpy as jnp
from jax import lax
from jax.experimental import pallas as pl
from jax.experimental.pallas import tpu as pltpu
from jax.sharding import PartitionSpec as P

ROUNDS = 3

START_HALO = 5

step_length = 0.5


def lagrange_integral(nodes, j, upper_end):
    coeffs = [1.0]
    scale_down = 1.0
    for i in range(len(nodes)):
        if i != j:
            grown = [0.0] * (len(coeffs) + 1)
            for p in range(len(coeffs)):
                grown[p + 1] = grown[p + 1] + coeffs[p]
                grown[p] = grown[p] - nodes[i] * coeffs[p]
            coeffs = grown
            scale_down = scale_down * (nodes[j] - nodes[i])
    summed_up = 0.0
    for p in range(len(coeffs)):
        summed_up = summed_up + coeffs[p] * upper_end ** (p + 1) / (p + 1)
    return summed_up / scale_down


def node_tables():
    radical = math.sqrt(3.0 / 7.0)
    fine_nodes = [0.0, 0.5 * (1.0 - radical), 0.5, 0.5 * (1.0 + radical), 1.0]
    coarse_nodes = [0.0, 0.5, 1.0]
    integrals = [
        [lagrange_integral(fine_nodes, j, fine_nodes[m]) for j in range(5)] for m in range(5)
    ]
    spread_table = [
        [float(step_length * (integrals[m + 1][j] - integrals[m][j])) for j in range(5)]
        for m in range(4)
    ]
    grouped_table = [
        [spread_table[2 * c][j] + spread_table[2 * c + 1][j] for j in range(5)] for c in range(2)
    ]
    interp_table = []
    for m in range(5):
        weights_row = []
        for k in range(3):
            factor = 1.0
            for i in range(3):
                if i != k:
                    factor = (
                        factor
                        * (fine_nodes[m] - coarse_nodes[i])
                        / (coarse_nodes[k] - coarse_nodes[i])
                    )
            weights_row.append(factor)
        interp_table.append(weights_row)
    widths = [step_length * (fine_nodes[m + 1] - fine_nodes[m]) for m in range(4)]
    return (spread_table, grouped_table, interp_table, widths)


def to_even_odd(a):
    return jnp.concatenate([a[..., 0::2, :], a[..., 1::2, :]], axis=-2)


def from_even_odd(a):
    half = a.shape[-2] // 2
    woven = jnp.stack([a[..., :half, :], a[..., half:, :]], axis=-2)
    return woven.reshape(a.shape)


def crop(field, h):
    a, have = field
    d = have - h
    assert d >= 0
    if d == 0:
        return a
    return lax.slice_in_dim(a, d, a.shape[-3] - d, axis=a.ndim - 3)


def space_halo(a, h):
    if h == 0:
        return a
    size = lax.axis_size("space")
    rows = a.shape[-3]
    assert h <= rows
    up = [(i, (i + 1) % size) for i in range(size)]
    down = [((i + 1) % size, i) for i in range(size)]
    before = lax.ppermute(lax.slice_in_dim(a, rows - h, rows, axis=a.ndim - 3), "space", up)
    after = lax.ppermute(lax.slice_in_dim(a, 0, h, axis=a.ndim - 3), "space", down)
    return jnp.concatenate([before, a, after], axis=a.ndim - 3)


def from_previous_slice(pieces):
    slices = lax.axis_size("tm")
    size = lax.axis_size("space")
    axes = ("tm", "space")

    def moved(piece, shift):
        pairs = [
            (t * size + s, (t + 1) * size + (s + shift) % size)
            for t in range(slices - 1)
            for s in range(size)
        ]
        return lax.ppermute(piece, axes, pairs)

    own, lasts, firsts = pieces
    return moved(own, 0), moved(lasts, 1), moved(firsts, -1)


def react_terms(field, laplace, diffusivity, source):
    first_part = field[0]
    second_part = field[1]
    product = first_part * second_part * second_part
    return jnp.stack(
        [
            diffusivity[0] * laplace[0] - product + source[0],
            diffusivity[1] * laplace[1] + product + source[1],
        ],
        axis=0,
    )


def fine_laplace(a):
    centre = a[..., 1:-1, :, :]
    pair_x = a[..., 2:, :, :] + a[..., :-2, :, :]
    half = centre.shape[-2] // 2
    even = centre[..., :half, :]
    odd = centre[..., half:, :]
    pair_y = jnp.concatenate(
        [odd + jnp.roll(odd, 1, -2), jnp.roll(even, -1, -2) + even], axis=-2
    )
    pair_z = jnp.roll(centre, -1, -1) + jnp.roll(centre, 1, -1)
    return pair_x + pair_y + pair_z - 6.0 * centre


def coarse_laplace(a):
    centre = a[..., 1:-1, :, :]
    pair_x = a[..., 2:, :, :] + a[..., :-2, :, :]
    pair_y = jnp.roll(centre, -1, -2) + jnp.roll(centre, 1, -2)
    pair_z = jnp.roll(centre, -1, -1) + jnp.roll(centre, 1, -1)
    return (pair_x - 2.0 * centre) * 0.25 + (pair_y - 2.0 * centre) * 0.25 + (
        pair_z - 2.0 * centre
    )


def restrict(field):
    a, h = field
    h2 = h - h % 2
    a = crop(field, h2)
    rows = a.shape[-3]
    half = a.shape[-2] // 2
    pairs = a.reshape(a.shape[:-3] + (rows // 2, 2) + a.shape[-2:])
    even = pairs[..., :half, :]
    odd = pairs[..., half:, :]
    upper = even[..., 0, :, :] + even[..., 1, :, :]
    lower = odd[..., 0, :, :] + odd[..., 1, :, :]
    return (upper + lower) * 0.25, h2 // 2


def prolong(a):
    rows = jnp.repeat(a, 2, axis=a.ndim - 3)
    return jnp.concatenate([rows, rows], axis=-2)


def kernel_laplace(f):
    centre = f[:, 1:-1]
    pair_x = f[:, 2:] + f[:, :-2]
    half = centre.shape[2] // 2
    even = centre[:, :, :half]
    odd = centre[:, :, half:]
    pair_y = jnp.concatenate(
        [odd + pltpu.roll(odd, 1, 2), pltpu.roll(even, half - 1, 2) + even], axis=2
    )
    lanes = centre.shape[3]
    pair_z = pltpu.roll(centre, lanes - 1, 3) + pltpu.roll(centre, 1, 3)
    return pair_x + pair_y + pair_z - 6.0 * centre


def kernel_restrict(v):
    shape = v.shape
    pairs = v.reshape((shape[0], shape[1] // 2, 2) + shape[2:])
    half = shape[2] // 2
    even = pairs[:, :, :, :half]
    odd = pairs[:, :, :, half:]
    upper = even[:, :, 0] + even[:, :, 1]
    lower = odd[:, :, 0] + odd[:, :, 1]
    return (upper + lower) * 0.25


def sweep_kernel(widths_sent, diff_ref, flag_ref, start_ref, centre_ref, bbefore_ref, bafter_ref,
                 own_ref, before_ref, after_ref, dec_ref, src_ref,
                 rate_ref, n1_ref, n2_ref, n3_ref, n4_ref, e0_ref, b0_ref, cown_ref, clasts_ref,
                 cfirsts_ref):
    spread_table, grouped_table, interp_table, widths = node_tables()
    rows = e0_ref.shape[1]
    hs = (start_ref.shape[1] - rows) // 2
    hd = (dec_ref.shape[1] - rows) // 2
    d0 = diff_ref[0]
    d1 = diff_ref[1]

    def at(ref, h):
        off = hd - h
        return ref[:, off:off + rows + 2 * h]

    def cut(v, have, h):
        d = have - h
        return v[:, d:v.shape[1] - d]

    def terms(f, h):
        laplace = kernel_laplace(f)
        centre = f[:, 1:-1]
        s = at(src_ref, h - 1)
        product = centre[0] * centre[1] * centre[1]
        return jnp.stack([d0 * laplace[0] - product + s[0], d1 * laplace[1] + product + s[1]])

    parts = []
    offset = 0
    for m in range(4):
        w = hs - 1 - m
        parts.append(
            jnp.concatenate(
                [before_ref[:, offset:offset + w], own_ref[m], after_ref[:, offset:offset + w]],
                axis=1,
            )
        )
        offset += w
    joined = jnp.concatenate([bbefore_ref[...], centre_ref[...], bafter_ref[...]], axis=1)
    swept = [jnp.where(flag_ref[0] == 1, start_ref[...], joined)]
    found = []
    for m in range(4):
        have = hs - m
        e = terms(swept[m], have)
        found.append(e)
        h = have - 1
        numerator = (cut(swept[m], have, h) + widths[m] * e) + parts[m]
        swept.append(numerator / (1.0 + widths[m] * at(dec_ref, h)))
    found.append(terms(swept[4], hs - 4))
    dec0 = at(dec_ref, 0)
    fulls = [cut(found[j], hs - 1 - j, 0) - dec0 * cut(swept[j], hs - j, 0) for j in range(5)]
    integrated = []
    for c in range(2):
        summed = grouped_table[c][0] * fulls[0]
        for j in range(1, 5):
            summed = summed + grouped_table[c][j] * fulls[j]
        integrated.append(kernel_restrict(summed))
    crows = rows // 2
    hcr = (rate_ref.shape[1] - crows) // 2
    rc = rate_ref[:, hcr:hcr + crows]
    coarse_vals = [kernel_restrict(cut(swept[j], hs - j, 0)) for j in (0, 2, 4)]
    half_step = 0.5 * step_length
    coarse_one = (
        coarse_vals[0] + half_step * rc * coarse_vals[1] + integrated[0]
    ) / (1.0 + half_step * rc)
    sent = [coarse_one, coarse_vals[1], coarse_vals[2], integrated[1]]
    offset = 0
    for i, piece in enumerate(sent):
        cown_ref[i] = piece
        w = widths_sent[i]
        if w:
            clasts_ref[:, offset:offset + w] = piece[:, crows - w:]
            cfirsts_ref[:, offset:offset + w] = piece[:, :w]
        offset += w
    for m, out in ((1, n1_ref), (2, n2_ref), (3, n3_ref), (4, n4_ref)):
        out[...] = cut(swept[m], hs - m, 1)
    e0_ref[...] = cut(found[0], hs - 1, 0)
    b0_ref[...] = cut(swept[0], hs, 0)


def fine_sweep(diffusivity, flag, start, prior, parts, decay, src, rate_c, widths_sent):
    rows = start.shape[1] - 2 * START_HALO
    shape = start.shape
    wide = jax.ShapeDtypeStruct((shape[0], rows + 2) + shape[2:], jnp.float32)
    own = jax.ShapeDtypeStruct((shape[0], rows) + shape[2:], jnp.float32)
    cshape = (shape[0], rows // 2, shape[2] // 2, shape[3])
    cown = jax.ShapeDtypeStruct((4,) + cshape, jnp.float32)
    cedge = jax.ShapeDtypeStruct((shape[0], sum(widths_sent)) + cshape[2:], jnp.float32)
    vmem = pl.BlockSpec(memory_space=pltpu.VMEM)
    return pl.pallas_call(
        functools.partial(sweep_kernel, widths_sent),
        out_shape=(wide, wide, wide, wide, own, own, cown, cedge, cedge),
        in_specs=[pl.BlockSpec(memory_space=pltpu.SMEM)] * 2 + [vmem] * 10,
        out_specs=(vmem,) * 9,
    )(diffusivity, flag, start, *prior, *parts, decay, src, rate_c)


def coarse_kernel_laplace(f):
    centre = f[:, 1:-1]
    pair_x = f[:, 2:] + f[:, :-2]
    ny = centre.shape[2]
    lanes = centre.shape[3]
    pair_y = pltpu.roll(centre, ny - 1, 2) + pltpu.roll(centre, 1, 2)
    pair_z = pltpu.roll(centre, lanes - 1, 3) + pltpu.roll(centre, 1, 3)
    return (pair_x - 2.0 * centre) * 0.25 + (pair_y - 2.0 * centre) * 0.25 + (
        pair_z - 2.0 * centre
    )


def finish_kernel(widths_sent, diff_ref, cown_ref, cbefore_ref, cafter_ref, rate_ref, csrc_ref,
                  n1_ref, n2_ref, n3_ref, n4_ref, b_ref, e0_ref, dec_ref, src_ref, *outs):
    spread_table, grouped_table, interp_table, widths = node_tables()
    last = len(outs) == 1
    rows = e0_ref.shape[1]
    crows = rows // 2
    ho = widths_sent[2]
    joined = []
    offset = 0
    for i in range(4):
        w = widths_sent[i]
        if w:
            joined.append(
                jnp.concatenate(
                    [cbefore_ref[:, offset:offset + w], cown_ref[i], cafter_ref[:, offset:offset + w]],
                    axis=1,
                )
            )
        else:
            joined.append(cown_ref[i])
        offset += w
    one, mid, low, late = joined
    hcr = (rate_ref.shape[1] - crows) // 2
    hd = (dec_ref.shape[1] - rows) // 2
    hs = START_HALO
    d0 = diff_ref[0]
    d1 = diff_ref[1]

    def at(ref, h, size, have):
        off = have - h
        return ref[:, off:off + size + 2 * h]

    def cut(v, have, h):
        d = have - h
        return v[:, d:v.shape[1] - d]

    def react(centre, laplace, s):
        product = centre[0] * centre[1] * centre[1]
        return jnp.stack([d0 * laplace[0] - product + s[0], d1 * laplace[1] + product + s[1]])

    def coarse_terms(v):
        return react(v[:, 1:-1], coarse_kernel_laplace(v), at(csrc_ref, ho, crows, hcr))

    half_step = 0.5 * step_length
    rc = at(rate_ref, ho, crows, hcr)
    coarse_two = (
        cut(one, ho + 1, ho)
        + half_step * (coarse_terms(one) - coarse_terms(mid))
        + half_step * rc * low
        + late
    ) / (1.0 + half_step * rc)
    delta_one = cut(one, ho + 1, ho) - cut(mid, ho + 1, ho)
    delta_two = coarse_two - low

    def prolonged(c):
        shape = c.shape
        doubled = jnp.broadcast_to(c[:, :, None], (shape[0], shape[1], 2) + shape[2:])
        doubled = doubled.reshape((shape[0], 2 * shape[1]) + shape[2:])
        return jnp.concatenate([doubled, doubled], axis=2)

    news = {}
    for m, ref in ((1, n1_ref), (2, n2_ref), (3, n3_ref), (4, n4_ref)):
        if last and m < 4:
            continue
        fine = prolonged(interp_table[m][1] * delta_one + interp_table[m][2] * delta_two)
        news[m] = cut(ref[...], 1, ho) + cut(fine, 2 * ho, ho)
    if last:
        outs[0][...] = news[4]
        return
    own_out, lasts_out, firsts_out, u4_out, u4_last_out, u4_first_out = outs
    src1 = at(src_ref, 0, rows, hd)
    dec0 = at(dec_ref, 0, rows, hd)
    states = [b_ref[...]] + [cut(news[m], 1, 0) for m in range(1, 5)]
    terms = [e0_ref[...]] + [
        react(cut(news[m], 1, 0), kernel_laplace(news[m]), src1) for m in range(1, 5)
    ]
    fulls = [terms[j] - dec0 * states[j] for j in range(5)]
    offset = 0
    for m in range(4):
        summed = spread_table[m][0] * fulls[0]
        for j in range(1, 5):
            summed = summed + spread_table[m][j] * fulls[j]
        part = (widths[m] * dec0 * states[m + 1] - widths[m] * terms[m]) + summed
        own_out[m] = part
        w = hs - 1 - m
        lasts_out[:, offset:offset + w] = part[:, rows - w:]
        firsts_out[:, offset:offset + w] = part[:, :w]
        offset += w
    u4_out[...] = states[4]
    u4_last_out[...] = states[4][:, rows - hs:]
    u4_first_out[...] = states[4][:, :hs]


def finish_round(diffusivity, coarse, rate_c, source_c, swept, e0, decay, src, last, widths_sent):
    begin = swept[0]
    shape = begin.shape
    rows = e0.shape[1]
    field = jax.ShapeDtypeStruct((shape[0], rows) + shape[2:], jnp.float32)
    if last:
        out_shape = (field,)
    else:
        sent = sum(START_HALO - 1 - m for m in range(4))
        edge = jax.ShapeDtypeStruct((shape[0], sent) + shape[2:], jnp.float32)
        rim = jax.ShapeDtypeStruct((shape[0], START_HALO) + shape[2:], jnp.float32)
        out_shape = (jax.ShapeDtypeStruct((4,) + field.shape, jnp.float32), edge, edge, field, rim, rim)
    vmem = pl.BlockSpec(memory_space=pltpu.VMEM)
    args = (diffusivity, *coarse, rate_c, source_c, *swept[1:], begin, e0, decay, src)
    return pl.pallas_call(
        functools.partial(finish_kernel, widths_sent),
        out_shape=out_shape,
        in_specs=[pl.BlockSpec(memory_space=pltpu.SMEM)] + [vmem] * (len(args) - 1),
        out_specs=(vmem,) * len(out_shape),
    )(*args)


def packed_halo(fields):
    size = lax.axis_size("space")
    rows = fields[0][0].shape[-3]
    axis = fields[0][0].ndim - 3
    up = [(i, (i + 1) % size) for i in range(size)]
    down = [((i + 1) % size, i) for i in range(size)]
    lasts = jnp.concatenate(
        [lax.slice_in_dim(a, rows - w, rows, axis=axis) for a, w in fields], axis=axis
    )
    firsts = jnp.concatenate([lax.slice_in_dim(a, 0, w, axis=axis) for a, w in fields], axis=axis)
    before = lax.ppermute(lasts, "space", up)
    after = lax.ppermute(firsts, "space", down)
    out = []
    offset = 0
    for a, w in fields:
        out.append(
            (
                jnp.concatenate(
                    [
                        lax.slice_in_dim(before, offset, offset + w, axis=axis),
                        a,
                        lax.slice_in_dim(after, offset, offset + w, axis=axis),
                    ],
                    axis=axis,
                ),
                w,
            )
        )
        offset += w
    return out


def per_device(initial, decay_rate, source, diffusivity):
    spread_table, grouped_table, interp_table, widths = node_tables()
    first_slice = lax.axis_index("tm") == 0
    hs = START_HALO
    assert hs == 5 and initial.shape[-3] >= hs

    own_start = to_even_odd(initial[0])
    fixed = space_halo(
        jnp.stack([own_start, to_even_odd(decay_rate), to_even_odd(source)]), hs
    )
    own_ext = fixed[0]
    decay = (fixed[1], hs)
    src = (fixed[2], hs)
    rate_c = restrict(decay)
    source_c = restrict(src)

    def fine_E(field):
        a, h = field
        laplace = fine_laplace(a)
        return react_terms(a[..., 1:-1, :, :], laplace, diffusivity, crop(src, h - 1)), h - 1

    def coarse_E(field):
        a, h = field
        laplace = coarse_laplace(a)
        return react_terms(a[..., 1:-1, :, :], laplace, diffusivity, crop(source_c, h - 1)), h - 1

    def full(field, field_E):
        h = min(field[1], field_E[1])
        return crop(field_E, h) - crop(decay, h) * crop(field, h), h

    def step_terms(states, terms):
        fulls = [full(states[j], terms[j]) for j in range(5)]
        hf = min(f[1] for f in fulls)
        out = []
        for m in range(4):
            h = min(hf, terms[m][1], states[m + 1][1])
            summed = spread_table[m][0] * crop(fulls[0], h)
            for j in range(1, 5):
                summed = summed + spread_table[m][j] * crop(fulls[j], h)
            own = (
                widths[m] * crop(decay, h) * crop(states[m + 1], h)
                - widths[m] * crop(terms[m], h)
            ) + summed
            out.append((own, h))
        return out

    def advance(prior, pieces, last):
        widths_sent = (1, 1, 0, 0) if last else (2, 2, 1, 1)
        n1, n2, n3, n4, e0, b0, cown, clasts, cfirsts = fine_sweep(
            diffusivity, flag, own_ext, prior, pieces, decay[0], src[0], rate_c[0], widths_sent
        )
        coarse = (
            cown,
            lax.ppermute(clasts, "space", up),
            lax.ppermute(cfirsts, "space", down),
        )
        return finish_round(
            diffusivity, coarse, rate_c[0], source_c[0],
            (b0, n1, n2, n3, n4), e0, decay[0], src[0], last, widths_sent,
        )

    size = lax.axis_size("space")
    up = [(i, (i + 1) % size) for i in range(size)]
    down = [((i + 1) % size, i) for i in range(size)]
    rows = own_start.shape[-3]
    flag = jnp.where(first_slice, 1, 0).astype(jnp.int32).reshape(1)
    state = (own_ext, hs)
    state_terms = fine_E(state)
    parts = step_terms([state] * 5, [state_terms] * 5)
    wide = [crop(parts[m], hs - 1) for m in range(4)]
    edge = hs - 1
    pieces = (
        jnp.stack([lax.slice_in_dim(p, edge, edge + rows, axis=1) for p in wide]),
        jnp.concatenate(
            [lax.slice_in_dim(p, m, edge, axis=1) for m, p in enumerate(wide)], axis=1
        ),
        jnp.concatenate(
            [lax.slice_in_dim(p, edge + rows, edge + rows + edge - m, axis=1)
             for m, p in enumerate(wide)], axis=1
        ),
    )
    prior = from_previous_slice(
        (own_start, own_start[:, rows - hs:], own_start[:, :hs])
    )
    for k in range(ROUNDS):
        last = k + 1 == ROUNDS
        outs = advance(prior, pieces, last)
        if not last:
            own4, lasts, firsts, u4, u4_last, u4_first = outs
            pieces = (
                own4,
                lax.ppermute(lasts, "space", up),
                lax.ppermute(firsts, "space", down),
            )
            prior = from_previous_slice((u4, u4_last, u4_first))
    return from_even_odd(outs[0])[None]


def solution(mesh):
    placed = (
        P("tm", None, "space", None, None),
        P(None, "space", None, None),
        P(None, "space", None, None),
        P(),
    )
    return jax.shard_map(
        per_device,
        mesh=mesh,
        in_specs=placed,
        out_specs=P("tm", None, "space", None, None),
        check_vma=False,
    )
```

```python
import functools
import math

import jax
import jax.numpy as jnp
from jax import lax
from jax.experimental import pallas as pl
from jax.experimental.pallas import tpu as pltpu
from jax.sharding import PartitionSpec as P

ROUNDS = 3

START_HALO = 5

step_length = 0.5


def lagrange_integral(nodes, j, upper_end):
    coeffs = [1.0]
    scale_down = 1.0
    for i in range(len(nodes)):
        if i != j:
            grown = [0.0] * (len(coeffs) + 1)
            for p in range(len(coeffs)):
                grown[p + 1] = grown[p + 1] + coeffs[p]
                grown[p] = grown[p] - nodes[i] * coeffs[p]
            coeffs = grown
            scale_down = scale_down * (nodes[j] - nodes[i])
    summed_up = 0.0
    for p in range(len(coeffs)):
        summed_up = summed_up + coeffs[p] * upper_end ** (p + 1) / (p + 1)
    return summed_up / scale_down


def node_tables():
    radical = math.sqrt(3.0 / 7.0)
    fine_nodes = [0.0, 0.5 * (1.0 - radical), 0.5, 0.5 * (1.0 + radical), 1.0]
    coarse_nodes = [0.0, 0.5, 1.0]
    integrals = [
        [lagrange_integral(fine_nodes, j, fine_nodes[m]) for j in range(5)] for m in range(5)
    ]
    spread_table = [
        [float(step_length * (integrals[m + 1][j] - integrals[m][j])) for j in range(5)]
        for m in range(4)
    ]
    grouped_table = [
        [spread_table[2 * c][j] + spread_table[2 * c + 1][j] for j in range(5)] for c in range(2)
    ]
    interp_table = []
    for m in range(5):
        weights_row = []
        for k in range(3):
            factor = 1.0
            for i in range(3):
                if i != k:
                    factor = (
                        factor
                        * (fine_nodes[m] - coarse_nodes[i])
                        / (coarse_nodes[k] - coarse_nodes[i])
                    )
            weights_row.append(factor)
        interp_table.append(weights_row)
    widths = [step_length * (fine_nodes[m + 1] - fine_nodes[m]) for m in range(4)]
    return (spread_table, grouped_table, interp_table, widths)


def to_even_odd(a):
    return jnp.concatenate([a[..., 0::2, :], a[..., 1::2, :]], axis=-2)


def from_even_odd(a):
    half = a.shape[-2] // 2
    woven = jnp.stack([a[..., :half, :], a[..., half:, :]], axis=-2)
    return woven.reshape(a.shape)


def crop(field, h):
    a, have = field
    d = have - h
    assert d >= 0
    if d == 0:
        return a
    return lax.slice_in_dim(a, d, a.shape[-3] - d, axis=a.ndim - 3)


def space_halo(a, h):
    if h == 0:
        return a
    size = lax.axis_size("space")
    rows = a.shape[-3]
    assert h <= rows
    up = [(i, (i + 1) % size) for i in range(size)]
    down = [((i + 1) % size, i) for i in range(size)]
    before = lax.ppermute(lax.slice_in_dim(a, rows - h, rows, axis=a.ndim - 3), "space", up)
    after = lax.ppermute(lax.slice_in_dim(a, 0, h, axis=a.ndim - 3), "space", down)
    return jnp.concatenate([before, a, after], axis=a.ndim - 3)


def from_previous_slice(pieces):
    slices = lax.axis_size("tm")
    size = lax.axis_size("space")
    axes = ("tm", "space")

    def moved(piece, shift):
        pairs = [
            (t * size + s, (t + 1) * size + (s + shift) % size)
            for t in range(slices - 1)
            for s in range(size)
        ]
        return lax.ppermute(piece, axes, pairs)

    own, lasts, firsts = pieces
    return moved(own, 0), moved(lasts, 1), moved(firsts, -1)


def react_terms(field, laplace, diffusivity, source):
    first_part = field[0]
    second_part = field[1]
    product = first_part * second_part * second_part
    return jnp.stack(
        [
            diffusivity[0] * laplace[0] - product + source[0],
            diffusivity[1] * laplace[1] + product + source[1],
        ],
        axis=0,
    )


def fine_laplace(a):
    centre = a[..., 1:-1, :, :]
    pair_x = a[..., 2:, :, :] + a[..., :-2, :, :]
    half = centre.shape[-2] // 2
    even = centre[..., :half, :]
    odd = centre[..., half:, :]
    pair_y = jnp.concatenate(
        [odd + jnp.roll(odd, 1, -2), jnp.roll(even, -1, -2) + even], axis=-2
    )
    pair_z = jnp.roll(centre, -1, -1) + jnp.roll(centre, 1, -1)
    return pair_x + pair_y + pair_z - 6.0 * centre


def coarse_laplace(a):
    centre = a[..., 1:-1, :, :]
    pair_x = a[..., 2:, :, :] + a[..., :-2, :, :]
    pair_y = jnp.roll(centre, -1, -2) + jnp.roll(centre, 1, -2)
    pair_z = jnp.roll(centre, -1, -1) + jnp.roll(centre, 1, -1)
    return (pair_x - 2.0 * centre) * 0.25 + (pair_y - 2.0 * centre) * 0.25 + (
        pair_z - 2.0 * centre
    )


def restrict(field):
    a, h = field
    h2 = h - h % 2
    a = crop(field, h2)
    rows = a.shape[-3]
    half = a.shape[-2] // 2
    pairs = a.reshape(a.shape[:-3] + (rows // 2, 2) + a.shape[-2:])
    even = pairs[..., :half, :]
    odd = pairs[..., half:, :]
    upper = even[..., 0, :, :] + even[..., 1, :, :]
    lower = odd[..., 0, :, :] + odd[..., 1, :, :]
    return (upper + lower) * 0.25, h2 // 2


def prolong(a):
    rows = jnp.repeat(a, 2, axis=a.ndim - 3)
    return jnp.concatenate([rows, rows], axis=-2)


def kernel_laplace(f):
    centre = f[:, 1:-1]
    pair_x = f[:, 2:] + f[:, :-2]
    half = centre.shape[2] // 2
    even = centre[:, :, :half]
    odd = centre[:, :, half:]
    pair_y = jnp.concatenate(
        [odd + pltpu.roll(odd, 1, 2), pltpu.roll(even, half - 1, 2) + even], axis=2
    )
    lanes = centre.shape[3]
    pair_z = pltpu.roll(centre, lanes - 1, 3) + pltpu.roll(centre, 1, 3)
    return pair_x + pair_y + pair_z - 6.0 * centre


def kernel_restrict(v):
    shape = v.shape
    pairs = v.reshape((shape[0], shape[1] // 2, 2) + shape[2:])
    half = shape[2] // 2
    even = pairs[:, :, :, :half]
    odd = pairs[:, :, :, half:]
    upper = even[:, :, 0] + even[:, :, 1]
    lower = odd[:, :, 0] + odd[:, :, 1]
    return (upper + lower) * 0.25


def sweep_kernel(widths_sent, diff_ref, flag_ref, start_ref, centre_ref, bbefore_ref, bafter_ref,
                 own_ref, before_ref, after_ref, dec_ref, src_ref,
                 rate_ref, n1_ref, n2_ref, n3_ref, n4_ref, e0_ref, b0_ref, cown_ref, clasts_ref,
                 cfirsts_ref):
    spread_table, grouped_table, interp_table, widths = node_tables()
    rows = e0_ref.shape[1]
    hs = (start_ref.shape[1] - rows) // 2
    hd = (dec_ref.shape[1] - rows) // 2
    d0 = diff_ref[0]
    d1 = diff_ref[1]

    def at(ref, h):
        off = hd - h
        return ref[:, off:off + rows + 2 * h]

    def cut(v, have, h):
        d = have - h
        return v[:, d:v.shape[1] - d]

    def terms(f, h):
        laplace = kernel_laplace(f)
        centre = f[:, 1:-1]
        s = at(src_ref, h - 1)
        product = centre[0] * centre[1] * centre[1]
        return jnp.stack([d0 * laplace[0] - product + s[0], d1 * laplace[1] + product + s[1]])

    parts = []
    offset = 0
    for m in range(4):
        w = hs - 1 - m
        parts.append(
            jnp.concatenate(
                [before_ref[:, offset:offset + w], own_ref[m], after_ref[:, offset:offset + w]],
                axis=1,
            )
        )
        offset += w
    joined = jnp.concatenate([bbefore_ref[...], centre_ref[...], bafter_ref[...]], axis=1)
    swept = [jnp.where(flag_ref[0] == 1, start_ref[...], joined)]
    found = []
    for m in range(4):
        have = hs - m
        e = terms(swept[m], have)
        found.append(e)
        h = have - 1
        numerator = (cut(swept[m], have, h) + widths[m] * e) + parts[m]
        swept.append(numerator / (1.0 + widths[m] * at(dec_ref, h)))
    found.append(terms(swept[4], hs - 4))
    dec0 = at(dec_ref, 0)
    fulls = [cut(found[j], hs - 1 - j, 0) - dec0 * cut(swept[j], hs - j, 0) for j in range(5)]
    integrated = []
    for c in range(2):
        summed = grouped_table[c][0] * fulls[0]
        for j in range(1, 5):
            summed = summed + grouped_table[c][j] * fulls[j]
        integrated.append(kernel_restrict(summed))
    crows = rows // 2
    hcr = (rate_ref.shape[1] - crows) // 2
    rc = rate_ref[:, hcr:hcr + crows]
    coarse_vals = [kernel_restrict(cut(swept[j], hs - j, 0)) for j in (0, 2, 4)]
    half_step = 0.5 * step_length
    coarse_one = (
        coarse_vals[0] + half_step * rc * coarse_vals[1] + integrated[0]
    ) / (1.0 + half_step * rc)
    sent = [coarse_one, coarse_vals[1], coarse_vals[2], integrated[1]]
    offset = 0
    for i, piece in enumerate(sent):
        cown_ref[i] = piece
        w = widths_sent[i]
        if w:
            clasts_ref[:, offset:offset + w] = piece[:, crows - w:]
            cfirsts_ref[:, offset:offset + w] = piece[:, :w]
        offset += w
    for m, out in ((1, n1_ref), (2, n2_ref), (3, n3_ref), (4, n4_ref)):
        out[...] = cut(swept[m], hs - m, 1)
    e0_ref[...] = cut(found[0], hs - 1, 0)
    b0_ref[...] = cut(swept[0], hs, 0)


def fine_sweep(diffusivity, flag, start, prior, parts, decay, src, rate_c, widths_sent):
    rows = start.shape[1] - 2 * START_HALO
    shape = start.shape
    wide = jax.ShapeDtypeStruct((shape[0], rows + 2) + shape[2:], jnp.float32)
    own = jax.ShapeDtypeStruct((shape[0], rows) + shape[2:], jnp.float32)
    cshape = (shape[0], rows // 2, shape[2] // 2, shape[3])
    cown = jax.ShapeDtypeStruct((4,) + cshape, jnp.float32)
    cedge = jax.ShapeDtypeStruct((shape[0], sum(widths_sent)) + cshape[2:], jnp.float32)
    vmem = pl.BlockSpec(memory_space=pltpu.VMEM)
    return pl.pallas_call(
        functools.partial(sweep_kernel, widths_sent),
        out_shape=(wide, wide, wide, wide, own, own, cown, cedge, cedge),
        in_specs=[pl.BlockSpec(memory_space=pltpu.SMEM)] * 2 + [vmem] * 10,
        out_specs=(vmem,) * 9,
    )(diffusivity, flag, start, *prior, *parts, decay, src, rate_c)


def coarse_kernel_laplace(f):
    centre = f[:, 1:-1]
    pair_x = f[:, 2:] + f[:, :-2]
    ny = centre.shape[2]
    lanes = centre.shape[3]
    pair_y = pltpu.roll(centre, ny - 1, 2) + pltpu.roll(centre, 1, 2)
    pair_z = pltpu.roll(centre, lanes - 1, 3) + pltpu.roll(centre, 1, 3)
    return (pair_x - 2.0 * centre) * 0.25 + (pair_y - 2.0 * centre) * 0.25 + (
        pair_z - 2.0 * centre
    )


def finish_kernel(widths_sent, diff_ref, cown_ref, cbefore_ref, cafter_ref, rate_ref, csrc_ref,
                  n1_ref, n2_ref, n3_ref, n4_ref, b_ref, e0_ref, dec_ref, src_ref, *outs):
    spread_table, grouped_table, interp_table, widths = node_tables()
    last = len(outs) == 1
    rows = e0_ref.shape[1]
    crows = rows // 2
    ho = widths_sent[2]
    joined = []
    offset = 0
    for i in range(4):
        w = widths_sent[i]
        if w:
            joined.append(
                jnp.concatenate(
                    [cbefore_ref[:, offset:offset + w], cown_ref[i], cafter_ref[:, offset:offset + w]],
                    axis=1,
                )
            )
        else:
            joined.append(cown_ref[i])
        offset += w
    one, mid, low, late = joined
    hcr = (rate_ref.shape[1] - crows) // 2
    hd = (dec_ref.shape[1] - rows) // 2
    hs = START_HALO
    d0 = diff_ref[0]
    d1 = diff_ref[1]

    def at(ref, h, size, have):
        off = have - h
        return ref[:, off:off + size + 2 * h]

    def cut(v, have, h):
        d = have - h
        return v[:, d:v.shape[1] - d]

    def react(centre, laplace, s):
        product = centre[0] * centre[1] * centre[1]
        return jnp.stack([d0 * laplace[0] - product + s[0], d1 * laplace[1] + product + s[1]])

    def coarse_terms(v):
        return react(v[:, 1:-1], coarse_kernel_laplace(v), at(csrc_ref, ho, crows, hcr))

    half_step = 0.5 * step_length
    rc = at(rate_ref, ho, crows, hcr)
    coarse_two = (
        cut(one, ho + 1, ho)
        + half_step * (coarse_terms(one) - coarse_terms(mid))
        + half_step * rc * low
        + late
    ) / (1.0 + half_step * rc)
    delta_one = cut(one, ho + 1, ho) - cut(mid, ho + 1, ho)
    delta_two = coarse_two - low

    def prolonged(c):
        shape = c.shape
        doubled = jnp.broadcast_to(c[:, :, None], (shape[0], shape[1], 2) + shape[2:])
        doubled = doubled.reshape((shape[0], 2 * shape[1]) + shape[2:])
        return jnp.concatenate([doubled, doubled], axis=2)

    news = {}
    for m, ref in ((1, n1_ref), (2, n2_ref), (3, n3_ref), (4, n4_ref)):
        if last and m < 4:
            continue
        fine = prolonged(interp_table[m][1] * delta_one + interp_table[m][2] * delta_two)
        news[m] = cut(ref[...], 1, ho) + cut(fine, 2 * ho, ho)
    if last:
        outs[0][...] = news[4]
        return
    own_out, lasts_out, firsts_out, u4_out, u4_last_out, u4_first_out = outs
    src1 = at(src_ref, 0, rows, hd)
    dec0 = at(dec_ref, 0, rows, hd)
    states = [b_ref[...]] + [cut(news[m], 1, 0) for m in range(1, 5)]
    terms = [e0_ref[...]] + [
        react(cut(news[m], 1, 0), kernel_laplace(news[m]), src1) for m in range(1, 5)
    ]
    fulls = [terms[j] - dec0 * states[j] for j in range(5)]
    offset = 0
    for m in range(4):
        summed = spread_table[m][0] * fulls[0]
        for j in range(1, 5):
            summed = summed + spread_table[m][j] * fulls[j]
        part = (widths[m] * dec0 * states[m + 1] - widths[m] * terms[m]) + summed
        own_out[m] = part
        w = hs - 1 - m
        lasts_out[:, offset:offset + w] = part[:, rows - w:]
        firsts_out[:, offset:offset + w] = part[:, :w]
        offset += w
    u4_out[...] = states[4]
    u4_last_out[...] = states[4][:, rows - hs:]
    u4_first_out[...] = states[4][:, :hs]


def finish_round(diffusivity, coarse, rate_c, source_c, swept, e0, decay, src, last, widths_sent):
    begin = swept[0]
    shape = begin.shape
    rows = e0.shape[1]
    field = jax.ShapeDtypeStruct((shape[0], rows) + shape[2:], jnp.float32)
    if last:
        out_shape = (field,)
    else:
        sent = sum(START_HALO - 1 - m for m in range(4))
        edge = jax.ShapeDtypeStruct((shape[0], sent) + shape[2:], jnp.float32)
        rim = jax.ShapeDtypeStruct((shape[0], START_HALO) + shape[2:], jnp.float32)
        out_shape = (jax.ShapeDtypeStruct((4,) + field.shape, jnp.float32), edge, edge, field, rim, rim)
    vmem = pl.BlockSpec(memory_space=pltpu.VMEM)
    args = (diffusivity, *coarse, rate_c, source_c, *swept[1:], begin, e0, decay, src)
    return pl.pallas_call(
        functools.partial(finish_kernel, widths_sent),
        out_shape=out_shape,
        in_specs=[pl.BlockSpec(memory_space=pltpu.SMEM)] + [vmem] * (len(args) - 1),
        out_specs=(vmem,) * len(out_shape),
    )(*args)


def start_kernel(diff_ref, init_ref, dec_ref, src_ref, own_ref, before_ref, after_ref,
                 rate_ref, csrc_ref):
    spread_table, grouped_table, interp_table, widths = node_tables()
    rows = own_ref.shape[2]
    hs = (init_ref.shape[1] - rows) // 2
    d0 = diff_ref[0]
    d1 = diff_ref[1]
    state = init_ref[...]
    inner = state[:, 1:-1]
    dec = dec_ref[:, 1:-1]
    s = src_ref[:, 1:-1]
    laplace = kernel_laplace(state)
    product = inner[0] * inner[1] * inner[1]
    terms = jnp.stack([d0 * laplace[0] - product + s[0], d1 * laplace[1] + product + s[1]])
    full = terms - dec * inner
    edge = hs - 1
    offset = 0
    for m in range(4):
        summed = spread_table[m][0] * full
        for j in range(1, 5):
            summed = summed + spread_table[m][j] * full
        part = (widths[m] * dec * inner - widths[m] * terms) + summed
        own_ref[m] = part[:, edge:edge + rows]
        w = edge - m
        before_ref[:, offset:offset + w] = part[:, m:edge]
        after_ref[:, offset:offset + w] = part[:, edge + rows:edge + rows + w]
        offset += w
    rate_ref[...] = kernel_restrict(dec)
    csrc_ref[...] = kernel_restrict(s)


def start_terms(diffusivity, own_ext, decay, src):
    shape = own_ext.shape
    rows = shape[1] - 2 * START_HALO
    sent = sum(START_HALO - 1 - m for m in range(4))
    edge = jax.ShapeDtypeStruct((shape[0], sent) + shape[2:], jnp.float32)
    cshape = (shape[0], (rows + 2 * (START_HALO - 1)) // 2, shape[2] // 2, shape[3])
    coarse = jax.ShapeDtypeStruct(cshape, jnp.float32)
    vmem = pl.BlockSpec(memory_space=pltpu.VMEM)
    return pl.pallas_call(
        start_kernel,
        out_shape=(
            jax.ShapeDtypeStruct((4, shape[0], rows) + shape[2:], jnp.float32),
            edge, edge, coarse, coarse,
        ),
        in_specs=[pl.BlockSpec(memory_space=pltpu.SMEM)] + [vmem] * 3,
        out_specs=(vmem,) * 5,
    )(diffusivity, own_ext, decay, src)


def packed_halo(fields):
    size = lax.axis_size("space")
    rows = fields[0][0].shape[-3]
    axis = fields[0][0].ndim - 3
    up = [(i, (i + 1) % size) for i in range(size)]
    down = [((i + 1) % size, i) for i in range(size)]
    lasts = jnp.concatenate(
        [lax.slice_in_dim(a, rows - w, rows, axis=axis) for a, w in fields], axis=axis
    )
    firsts = jnp.concatenate([lax.slice_in_dim(a, 0, w, axis=axis) for a, w in fields], axis=axis)
    before = lax.ppermute(lasts, "space", up)
    after = lax.ppermute(firsts, "space", down)
    out = []
    offset = 0
    for a, w in fields:
        out.append(
            (
                jnp.concatenate(
                    [
                        lax.slice_in_dim(before, offset, offset + w, axis=axis),
                        a,
                        lax.slice_in_dim(after, offset, offset + w, axis=axis),
                    ],
                    axis=axis,
                ),
                w,
            )
        )
        offset += w
    return out


def per_device(initial, decay_rate, source, diffusivity):
    spread_table, grouped_table, interp_table, widths = node_tables()
    first_slice = lax.axis_index("tm") == 0
    hs = START_HALO
    assert hs == 5 and initial.shape[-3] >= hs

    own_start = to_even_odd(initial[0])
    own_ext = space_halo(own_start, hs)
    fixed = space_halo(jnp.stack([to_even_odd(decay_rate), to_even_odd(source)]), hs)
    decay = (fixed[0], hs)
    src = (fixed[1], hs)
    own4, before4, after4, rate_own, csrc_own = start_terms(diffusivity, own_ext, decay[0], src[0])
    rate_c = (rate_own, (hs - 1) // 2)
    source_c = (csrc_own, (hs - 1) // 2)

    def fine_E(field):
        a, h = field
        laplace = fine_laplace(a)
        return react_terms(a[..., 1:-1, :, :], laplace, diffusivity, crop(src, h - 1)), h - 1

    def coarse_E(field):
        a, h = field
        laplace = coarse_laplace(a)
        return react_terms(a[..., 1:-1, :, :], laplace, diffusivity, crop(source_c, h - 1)), h - 1

    def full(field, field_E):
        h = min(field[1], field_E[1])
        return crop(field_E, h) - crop(decay, h) * crop(field, h), h

    def step_terms(states, terms):
        fulls = [full(states[j], terms[j]) for j in range(5)]
        hf = min(f[1] for f in fulls)
        out = []
        for m in range(4):
            h = min(hf, terms[m][1], states[m + 1][1])
            summed = spread_table[m][0] * crop(fulls[0], h)
            for j in range(1, 5):
                summed = summed + spread_table[m][j] * crop(fulls[j], h)
            own = (
                widths[m] * crop(decay, h) * crop(states[m + 1], h)
                - widths[m] * crop(terms[m], h)
            ) + summed
            out.append((own, h))
        return out

    def advance(prior, pieces, last):
        widths_sent = (1, 1, 0, 0) if last else (2, 2, 1, 1)
        n1, n2, n3, n4, e0, b0, cown, clasts, cfirsts = fine_sweep(
            diffusivity, flag, own_ext, prior, pieces, decay[0], src[0], rate_c[0], widths_sent
        )
        coarse = (
            cown,
            lax.ppermute(clasts, "space", up),
            lax.ppermute(cfirsts, "space", down),
        )
        return finish_round(
            diffusivity, coarse, rate_c[0], source_c[0],
            (b0, n1, n2, n3, n4), e0, decay[0], src[0], last, widths_sent,
        )

    size = lax.axis_size("space")
    up = [(i, (i + 1) % size) for i in range(size)]
    down = [((i + 1) % size, i) for i in range(size)]
    rows = own_start.shape[-3]
    flag = jnp.where(first_slice, 1, 0).astype(jnp.int32).reshape(1)
    pieces = (own4, before4, after4)
    prior = from_previous_slice(
        (own_start, own_start[:, rows - hs:], own_start[:, :hs])
    )
    for k in range(ROUNDS):
        last = k + 1 == ROUNDS
        outs = advance(prior, pieces, last)
        if not last:
            own4, lasts, firsts, u4, u4_last, u4_first = outs
            pieces = (
                own4,
                lax.ppermute(lasts, "space", up),
                lax.ppermute(firsts, "space", down),
            )
            prior = from_previous_slice((u4, u4_last, u4_first))
    return from_even_odd(outs[0])[None]


def solution(mesh):
    placed = (
        P("tm", None, "space", None, None),
        P(None, "space", None, None),
        P(None, "space", None, None),
        P(),
    )
    return jax.shard_map(
        per_device,
        mesh=mesh,
        in_specs=placed,
        out_specs=P("tm", None, "space", None, None),
        check_vma=False,
    )
```

```python
import functools
import math

import jax
import jax.numpy as jnp
from jax import lax
from jax.experimental import pallas as pl
from jax.experimental.pallas import tpu as pltpu
from jax.sharding import PartitionSpec as P

ROUNDS = 3

START_HALO = 5

step_length = 0.5


def lagrange_integral(nodes, j, upper_end):
    coeffs = [1.0]
    scale_down = 1.0
    for i in range(len(nodes)):
        if i != j:
            grown = [0.0] * (len(coeffs) + 1)
            for p in range(len(coeffs)):
                grown[p + 1] = grown[p + 1] + coeffs[p]
                grown[p] = grown[p] - nodes[i] * coeffs[p]
            coeffs = grown
            scale_down = scale_down * (nodes[j] - nodes[i])
    summed_up = 0.0
    for p in range(len(coeffs)):
        summed_up = summed_up + coeffs[p] * upper_end ** (p + 1) / (p + 1)
    return summed_up / scale_down


def node_tables():
    radical = math.sqrt(3.0 / 7.0)
    fine_nodes = [0.0, 0.5 * (1.0 - radical), 0.5, 0.5 * (1.0 + radical), 1.0]
    coarse_nodes = [0.0, 0.5, 1.0]
    integrals = [
        [lagrange_integral(fine_nodes, j, fine_nodes[m]) for j in range(5)] for m in range(5)
    ]
    spread_table = [
        [float(step_length * (integrals[m + 1][j] - integrals[m][j])) for j in range(5)]
        for m in range(4)
    ]
    grouped_table = [
        [spread_table[2 * c][j] + spread_table[2 * c + 1][j] for j in range(5)] for c in range(2)
    ]
    interp_table = []
    for m in range(5):
        weights_row = []
        for k in range(3):
            factor = 1.0
            for i in range(3):
                if i != k:
                    factor = (
                        factor
                        * (fine_nodes[m] - coarse_nodes[i])
                        / (coarse_nodes[k] - coarse_nodes[i])
                    )
            weights_row.append(factor)
        interp_table.append(weights_row)
    widths = [step_length * (fine_nodes[m + 1] - fine_nodes[m]) for m in range(4)]
    return (spread_table, grouped_table, interp_table, widths)


def to_even_odd(a):
    return jnp.concatenate([a[..., 0::2, :], a[..., 1::2, :]], axis=-2)


def from_even_odd(a):
    half = a.shape[-2] // 2
    woven = jnp.stack([a[..., :half, :], a[..., half:, :]], axis=-2)
    return woven.reshape(a.shape)


def crop(field, h):
    a, have = field
    d = have - h
    assert d >= 0
    if d == 0:
        return a
    return lax.slice_in_dim(a, d, a.shape[-3] - d, axis=a.ndim - 3)


def space_halo(a, h):
    if h == 0:
        return a
    size = lax.axis_size("space")
    rows = a.shape[-3]
    assert h <= rows
    up = [(i, (i + 1) % size) for i in range(size)]
    down = [((i + 1) % size, i) for i in range(size)]
    before = lax.ppermute(lax.slice_in_dim(a, rows - h, rows, axis=a.ndim - 3), "space", up)
    after = lax.ppermute(lax.slice_in_dim(a, 0, h, axis=a.ndim - 3), "space", down)
    return jnp.concatenate([before, a, after], axis=a.ndim - 3)


def from_previous_slice(pieces):
    slices = lax.axis_size("tm")
    size = lax.axis_size("space")
    axes = ("tm", "space")

    def moved(piece, shift):
        pairs = [
            (t * size + s, (t + 1) * size + (s + shift) % size)
            for t in range(slices - 1)
            for s in range(size)
        ]
        return lax.ppermute(piece, axes, pairs)

    own, lasts, firsts = pieces
    return moved(own, 0), moved(lasts, 1), moved(firsts, -1)


def react_terms(field, laplace, diffusivity, source):
    first_part = field[0]
    second_part = field[1]
    product = first_part * second_part * second_part
    return jnp.stack(
        [
            diffusivity[0] * laplace[0] - product + source[0],
            diffusivity[1] * laplace[1] + product + source[1],
        ],
        axis=0,
    )


def fine_laplace(a):
    centre = a[..., 1:-1, :, :]
    pair_x = a[..., 2:, :, :] + a[..., :-2, :, :]
    half = centre.shape[-2] // 2
    even = centre[..., :half, :]
    odd = centre[..., half:, :]
    pair_y = jnp.concatenate(
        [odd + jnp.roll(odd, 1, -2), jnp.roll(even, -1, -2) + even], axis=-2
    )
    pair_z = jnp.roll(centre, -1, -1) + jnp.roll(centre, 1, -1)
    return pair_x + pair_y + pair_z - 6.0 * centre


def coarse_laplace(a):
    centre = a[..., 1:-1, :, :]
    pair_x = a[..., 2:, :, :] + a[..., :-2, :, :]
    pair_y = jnp.roll(centre, -1, -2) + jnp.roll(centre, 1, -2)
    pair_z = jnp.roll(centre, -1, -1) + jnp.roll(centre, 1, -1)
    return (pair_x - 2.0 * centre) * 0.25 + (pair_y - 2.0 * centre) * 0.25 + (
        pair_z - 2.0 * centre
    )


def restrict(field):
    a, h = field
    h2 = h - h % 2
    a = crop(field, h2)
    rows = a.shape[-3]
    half = a.shape[-2] // 2
    pairs = a.reshape(a.shape[:-3] + (rows // 2, 2) + a.shape[-2:])
    even = pairs[..., :half, :]
    odd = pairs[..., half:, :]
    upper = even[..., 0, :, :] + even[..., 1, :, :]
    lower = odd[..., 0, :, :] + odd[..., 1, :, :]
    return (upper + lower) * 0.25, h2 // 2


def prolong(a):
    rows = jnp.repeat(a, 2, axis=a.ndim - 3)
    return jnp.concatenate([rows, rows], axis=-2)


def even_odd_load(ref, index=()):
    view = ref.at[index] if index else ref
    lead = (slice(None),) * (len(view.shape) - 2)
    half = view.shape[-2] // 2
    even = view[lead + (pl.ds(0, half, stride=2), slice(None))]
    odd = view[lead + (pl.ds(1, half, stride=2), slice(None))]
    return jnp.concatenate([even, odd], axis=-2)


def kernel_laplace(f):
    centre = f[:, 1:-1]
    pair_x = f[:, 2:] + f[:, :-2]
    half = centre.shape[2] // 2
    even = centre[:, :, :half]
    odd = centre[:, :, half:]
    pair_y = jnp.concatenate(
        [odd + pltpu.roll(odd, 1, 2), pltpu.roll(even, half - 1, 2) + even], axis=2
    )
    lanes = centre.shape[3]
    pair_z = pltpu.roll(centre, lanes - 1, 3) + pltpu.roll(centre, 1, 3)
    return pair_x + pair_y + pair_z - 6.0 * centre


def kernel_restrict(v):
    shape = v.shape
    pairs = v.reshape((shape[0], shape[1] // 2, 2) + shape[2:])
    half = shape[2] // 2
    even = pairs[:, :, :, :half]
    odd = pairs[:, :, :, half:]
    upper = even[:, :, 0] + even[:, :, 1]
    lower = odd[:, :, 0] + odd[:, :, 1]
    return (upper + lower) * 0.25


def sweep_kernel(widths_sent, natural_prior, diff_ref, flag_ref, start_ref, centre_ref, bbefore_ref, bafter_ref,
                 own_ref, before_ref, after_ref, dec_ref, src_ref,
                 rate_ref, n1_ref, n2_ref, n3_ref, n4_ref, e0_ref, b0_ref, cown_ref, clasts_ref,
                 cfirsts_ref):
    spread_table, grouped_table, interp_table, widths = node_tables()
    rows = e0_ref.shape[1]
    hs = (start_ref.shape[1] - rows) // 2
    hd = (dec_ref.shape[1] - rows) // 2
    d0 = diff_ref[0]
    d1 = diff_ref[1]

    def at(ref, h):
        off = hd - h
        return ref[:, off:off + rows + 2 * h]

    def cut(v, have, h):
        d = have - h
        return v[:, d:v.shape[1] - d]

    def terms(f, h):
        laplace = kernel_laplace(f)
        centre = f[:, 1:-1]
        s = at(src_ref, h - 1)
        product = centre[0] * centre[1] * centre[1]
        return jnp.stack([d0 * laplace[0] - product + s[0], d1 * laplace[1] + product + s[1]])

    parts = []
    offset = 0
    for m in range(4):
        w = hs - 1 - m
        parts.append(
            jnp.concatenate(
                [before_ref[:, offset:offset + w], own_ref[m], after_ref[:, offset:offset + w]],
                axis=1,
            )
        )
        offset += w
    if natural_prior:
        pieces = [even_odd_load(r) for r in (bbefore_ref, centre_ref, bafter_ref)]
    else:
        pieces = [r[...] for r in (bbefore_ref, centre_ref, bafter_ref)]
    joined = jnp.concatenate(pieces, axis=1)
    swept = [jnp.where(flag_ref[0] == 1, start_ref[...], joined)]
    found = []
    for m in range(4):
        have = hs - m
        e = terms(swept[m], have)
        found.append(e)
        h = have - 1
        numerator = (cut(swept[m], have, h) + widths[m] * e) + parts[m]
        swept.append(numerator / (1.0 + widths[m] * at(dec_ref, h)))
    found.append(terms(swept[4], hs - 4))
    dec0 = at(dec_ref, 0)
    fulls = [cut(found[j], hs - 1 - j, 0) - dec0 * cut(swept[j], hs - j, 0) for j in range(5)]
    integrated = []
    for c in range(2):
        summed = grouped_table[c][0] * fulls[0]
        for j in range(1, 5):
            summed = summed + grouped_table[c][j] * fulls[j]
        integrated.append(kernel_restrict(summed))
    crows = rows // 2
    hcr = (rate_ref.shape[1] - crows) // 2
    rc = rate_ref[:, hcr:hcr + crows]
    coarse_vals = [kernel_restrict(cut(swept[j], hs - j, 0)) for j in (0, 2, 4)]
    half_step = 0.5 * step_length
    coarse_one = (
        coarse_vals[0] + half_step * rc * coarse_vals[1] + integrated[0]
    ) / (1.0 + half_step * rc)
    sent = [coarse_one, coarse_vals[1], coarse_vals[2], integrated[1]]
    offset = 0
    for i, piece in enumerate(sent):
        cown_ref[i] = piece
        w = widths_sent[i]
        if w:
            clasts_ref[:, offset:offset + w] = piece[:, crows - w:]
            cfirsts_ref[:, offset:offset + w] = piece[:, :w]
        offset += w
    for m, out in ((1, n1_ref), (2, n2_ref), (3, n3_ref), (4, n4_ref)):
        out[...] = cut(swept[m], hs - m, 1)
    e0_ref[...] = cut(found[0], hs - 1, 0)
    b0_ref[...] = cut(swept[0], hs, 0)


def fine_sweep(diffusivity, flag, start, prior, parts, decay, src, rate_c, widths_sent,
               natural_prior):
    rows = start.shape[1] - 2 * START_HALO
    shape = start.shape
    wide = jax.ShapeDtypeStruct((shape[0], rows + 2) + shape[2:], jnp.float32)
    own = jax.ShapeDtypeStruct((shape[0], rows) + shape[2:], jnp.float32)
    cshape = (shape[0], rows // 2, shape[2] // 2, shape[3])
    cown = jax.ShapeDtypeStruct((4,) + cshape, jnp.float32)
    cedge = jax.ShapeDtypeStruct((shape[0], sum(widths_sent)) + cshape[2:], jnp.float32)
    vmem = pl.BlockSpec(memory_space=pltpu.VMEM)
    return pl.pallas_call(
        functools.partial(sweep_kernel, widths_sent, natural_prior),
        out_shape=(wide, wide, wide, wide, own, own, cown, cedge, cedge),
        in_specs=[pl.BlockSpec(memory_space=pltpu.SMEM)] * 2 + [vmem] * 10,
        out_specs=(vmem,) * 9,
    )(diffusivity, flag, start, *prior, *parts, decay, src, rate_c)


def coarse_kernel_laplace(f):
    centre = f[:, 1:-1]
    pair_x = f[:, 2:] + f[:, :-2]
    ny = centre.shape[2]
    lanes = centre.shape[3]
    pair_y = pltpu.roll(centre, ny - 1, 2) + pltpu.roll(centre, 1, 2)
    pair_z = pltpu.roll(centre, lanes - 1, 3) + pltpu.roll(centre, 1, 3)
    return (pair_x - 2.0 * centre) * 0.25 + (pair_y - 2.0 * centre) * 0.25 + (
        pair_z - 2.0 * centre
    )


def finish_kernel(widths_sent, diff_ref, cown_ref, cbefore_ref, cafter_ref, rate_ref, csrc_ref,
                  n1_ref, n2_ref, n3_ref, n4_ref, b_ref, e0_ref, dec_ref, src_ref, *outs):
    spread_table, grouped_table, interp_table, widths = node_tables()
    last = len(outs) == 1
    rows = e0_ref.shape[1]
    crows = rows // 2
    ho = widths_sent[2]
    joined = []
    offset = 0
    for i in range(4):
        w = widths_sent[i]
        if w:
            joined.append(
                jnp.concatenate(
                    [cbefore_ref[:, offset:offset + w], cown_ref[i], cafter_ref[:, offset:offset + w]],
                    axis=1,
                )
            )
        else:
            joined.append(cown_ref[i])
        offset += w
    one, mid, low, late = joined
    hcr = (rate_ref.shape[1] - crows) // 2
    hd = (dec_ref.shape[1] - rows) // 2
    hs = START_HALO
    d0 = diff_ref[0]
    d1 = diff_ref[1]

    def at(ref, h, size, have):
        off = have - h
        return ref[:, off:off + size + 2 * h]

    def cut(v, have, h):
        d = have - h
        return v[:, d:v.shape[1] - d]

    def react(centre, laplace, s):
        product = centre[0] * centre[1] * centre[1]
        return jnp.stack([d0 * laplace[0] - product + s[0], d1 * laplace[1] + product + s[1]])

    def coarse_terms(v):
        return react(v[:, 1:-1], coarse_kernel_laplace(v), at(csrc_ref, ho, crows, hcr))

    half_step = 0.5 * step_length
    rc = at(rate_ref, ho, crows, hcr)
    coarse_two = (
        cut(one, ho + 1, ho)
        + half_step * (coarse_terms(one) - coarse_terms(mid))
        + half_step * rc * low
        + late
    ) / (1.0 + half_step * rc)
    delta_one = cut(one, ho + 1, ho) - cut(mid, ho + 1, ho)
    delta_two = coarse_two - low

    def prolonged(c):
        shape = c.shape
        doubled = jnp.broadcast_to(c[:, :, None], (shape[0], shape[1], 2) + shape[2:])
        doubled = doubled.reshape((shape[0], 2 * shape[1]) + shape[2:])
        return jnp.concatenate([doubled, doubled], axis=2)

    news = {}
    for m, ref in ((1, n1_ref), (2, n2_ref), (3, n3_ref), (4, n4_ref)):
        if last and m < 4:
            continue
        fine = prolonged(interp_table[m][1] * delta_one + interp_table[m][2] * delta_two)
        news[m] = cut(ref[...], 1, ho) + cut(fine, 2 * ho, ho)
    if last:
        half = news[4].shape[2] // 2
        outs[0][:, :, pl.ds(0, half, stride=2), :] = news[4][:, :, :half]
        outs[0][:, :, pl.ds(1, half, stride=2), :] = news[4][:, :, half:]
        return
    own_out, lasts_out, firsts_out, u4_out, u4_last_out, u4_first_out = outs
    src1 = at(src_ref, 0, rows, hd)
    dec0 = at(dec_ref, 0, rows, hd)
    states = [b_ref[...]] + [cut(news[m], 1, 0) for m in range(1, 5)]
    terms = [e0_ref[...]] + [
        react(cut(news[m], 1, 0), kernel_laplace(news[m]), src1) for m in range(1, 5)
    ]
    fulls = [terms[j] - dec0 * states[j] for j in range(5)]
    offset = 0
    for m in range(4):
        summed = spread_table[m][0] * fulls[0]
        for j in range(1, 5):
            summed = summed + spread_table[m][j] * fulls[j]
        part = (widths[m] * dec0 * states[m + 1] - widths[m] * terms[m]) + summed
        own_out[m] = part
        w = hs - 1 - m
        lasts_out[:, offset:offset + w] = part[:, rows - w:]
        firsts_out[:, offset:offset + w] = part[:, :w]
        offset += w
    u4_out[...] = states[4]
    u4_last_out[...] = states[4][:, rows - hs:]
    u4_first_out[...] = states[4][:, :hs]


def finish_round(diffusivity, coarse, rate_c, source_c, swept, e0, decay, src, last, widths_sent):
    begin = swept[0]
    shape = begin.shape
    rows = e0.shape[1]
    field = jax.ShapeDtypeStruct((shape[0], rows) + shape[2:], jnp.float32)
    if last:
        out_shape = (field,)
    else:
        sent = sum(START_HALO - 1 - m for m in range(4))
        edge = jax.ShapeDtypeStruct((shape[0], sent) + shape[2:], jnp.float32)
        rim = jax.ShapeDtypeStruct((shape[0], START_HALO) + shape[2:], jnp.float32)
        out_shape = (jax.ShapeDtypeStruct((4,) + field.shape, jnp.float32), edge, edge, field, rim, rim)
    vmem = pl.BlockSpec(memory_space=pltpu.VMEM)
    args = (diffusivity, *coarse, rate_c, source_c, *swept[1:], begin, e0, decay, src)
    return pl.pallas_call(
        functools.partial(finish_kernel, widths_sent),
        out_shape=out_shape,
        in_specs=[pl.BlockSpec(memory_space=pltpu.SMEM)] + [vmem] * (len(args) - 1),
        out_specs=(vmem,) * len(out_shape),
    )(*args)


def start_kernel(diff_ref, stacked_ref, own_ref, before_ref, after_ref, rate_ref, csrc_ref,
                 ext_ref, dec_ref, src_ref):
    spread_table, grouped_table, interp_table, widths = node_tables()
    rows = own_ref.shape[2]
    hs = (stacked_ref.shape[2] - rows) // 2
    d0 = diff_ref[0]
    d1 = diff_ref[1]
    state = even_odd_load(stacked_ref, (0,))
    decay = even_odd_load(stacked_ref, (1,))
    source = even_odd_load(stacked_ref, (2,))
    ext_ref[...] = state
    dec_ref[...] = decay
    src_ref[...] = source
    inner = state[:, 1:-1]
    dec = decay[:, 1:-1]
    s = source[:, 1:-1]
    laplace = kernel_laplace(state)
    product = inner[0] * inner[1] * inner[1]
    terms = jnp.stack([d0 * laplace[0] - product + s[0], d1 * laplace[1] + product + s[1]])
    full = terms - dec * inner
    edge = hs - 1
    offset = 0
    for m in range(4):
        summed = spread_table[m][0] * full
        for j in range(1, 5):
            summed = summed + spread_table[m][j] * full
        part = (widths[m] * dec * inner - widths[m] * terms) + summed
        own_ref[m] = part[:, edge:edge + rows]
        w = edge - m
        before_ref[:, offset:offset + w] = part[:, m:edge]
        after_ref[:, offset:offset + w] = part[:, edge + rows:edge + rows + w]
        offset += w
    rate_ref[...] = kernel_restrict(dec)
    csrc_ref[...] = kernel_restrict(s)


def start_terms(diffusivity, stacked):
    shape = stacked.shape[1:]
    rows = shape[1] - 2 * START_HALO
    sent = sum(START_HALO - 1 - m for m in range(4))
    edge = jax.ShapeDtypeStruct((shape[0], sent) + shape[2:], jnp.float32)
    cshape = (shape[0], (rows + 2 * (START_HALO - 1)) // 2, shape[2] // 2, shape[3])
    coarse = jax.ShapeDtypeStruct(cshape, jnp.float32)
    vmem = pl.BlockSpec(memory_space=pltpu.VMEM)
    return pl.pallas_call(
        start_kernel,
        out_shape=(
            jax.ShapeDtypeStruct((4, shape[0], rows) + shape[2:], jnp.float32),
            edge, edge, coarse, coarse,
            jax.ShapeDtypeStruct(shape, jnp.float32),
            jax.ShapeDtypeStruct(shape, jnp.float32),
            jax.ShapeDtypeStruct(shape, jnp.float32),
        ),
        in_specs=[pl.BlockSpec(memory_space=pltpu.SMEM)] + [vmem],
        out_specs=(vmem,) * 8,
    )(diffusivity, stacked)


def packed_halo(fields):
    size = lax.axis_size("space")
    rows = fields[0][0].shape[-3]
    axis = fields[0][0].ndim - 3
    up = [(i, (i + 1) % size) for i in range(size)]
    down = [((i + 1) % size, i) for i in range(size)]
    lasts = jnp.concatenate(
        [lax.slice_in_dim(a, rows - w, rows, axis=axis) for a, w in fields], axis=axis
    )
    firsts = jnp.concatenate([lax.slice_in_dim(a, 0, w, axis=axis) for a, w in fields], axis=axis)
    before = lax.ppermute(lasts, "space", up)
    after = lax.ppermute(firsts, "space", down)
    out = []
    offset = 0
    for a, w in fields:
        out.append(
            (
                jnp.concatenate(
                    [
                        lax.slice_in_dim(before, offset, offset + w, axis=axis),
                        a,
                        lax.slice_in_dim(after, offset, offset + w, axis=axis),
                    ],
                    axis=axis,
                ),
                w,
            )
        )
        offset += w
    return out


def per_device(initial, decay_rate, source, diffusivity):
    spread_table, grouped_table, interp_table, widths = node_tables()
    first_slice = lax.axis_index("tm") == 0
    hs = START_HALO
    assert hs == 5 and initial.shape[-3] >= hs

    own_start = initial[0]
    stacked = space_halo(jnp.stack([own_start, decay_rate, source]), hs)
    own4, before4, after4, rate_own, csrc_own, own_ext, dec_ext, src_ext = start_terms(
        diffusivity, stacked
    )
    decay = (dec_ext, hs)
    src = (src_ext, hs)
    rate_c = (rate_own, (hs - 1) // 2)
    source_c = (csrc_own, (hs - 1) // 2)

    def fine_E(field):
        a, h = field
        laplace = fine_laplace(a)
        return react_terms(a[..., 1:-1, :, :], laplace, diffusivity, crop(src, h - 1)), h - 1

    def coarse_E(field):
        a, h = field
        laplace = coarse_laplace(a)
        return react_terms(a[..., 1:-1, :, :], laplace, diffusivity, crop(source_c, h - 1)), h - 1

    def full(field, field_E):
        h = min(field[1], field_E[1])
        return crop(field_E, h) - crop(decay, h) * crop(field, h), h

    def step_terms(states, terms):
        fulls = [full(states[j], terms[j]) for j in range(5)]
        hf = min(f[1] for f in fulls)
        out = []
        for m in range(4):
            h = min(hf, terms[m][1], states[m + 1][1])
            summed = spread_table[m][0] * crop(fulls[0], h)
            for j in range(1, 5):
                summed = summed + spread_table[m][j] * crop(fulls[j], h)
            own = (
                widths[m] * crop(decay, h) * crop(states[m + 1], h)
                - widths[m] * crop(terms[m], h)
            ) + summed
            out.append((own, h))
        return out

    def advance(prior, pieces, last, natural):
        widths_sent = (1, 1, 0, 0) if last else (2, 2, 1, 1)
        n1, n2, n3, n4, e0, b0, cown, clasts, cfirsts = fine_sweep(
            diffusivity, flag, own_ext, prior, pieces, decay[0], src[0], rate_c[0], widths_sent,
            natural,
        )
        coarse = (
            cown,
            lax.ppermute(clasts, "space", up),
            lax.ppermute(cfirsts, "space", down),
        )
        return finish_round(
            diffusivity, coarse, rate_c[0], source_c[0],
            (b0, n1, n2, n3, n4), e0, decay[0], src[0], last, widths_sent,
        )

    size = lax.axis_size("space")
    up = [(i, (i + 1) % size) for i in range(size)]
    down = [((i + 1) % size, i) for i in range(size)]
    rows = own_start.shape[-3]
    flag = jnp.where(first_slice, 1, 0).astype(jnp.int32).reshape(1)
    pieces = (own4, before4, after4)
    prior = from_previous_slice(
        (own_start, own_start[:, rows - hs:], own_start[:, :hs])
    )
    for k in range(ROUNDS):
        last = k + 1 == ROUNDS
        outs = advance(prior, pieces, last, k == 0)
        if not last:
            own4, lasts, firsts, u4, u4_last, u4_first = outs
            pieces = (
                own4,
                lax.ppermute(lasts, "space", up),
                lax.ppermute(firsts, "space", down),
            )
            prior = from_previous_slice((u4, u4_last, u4_first))
    return outs[0][None]


def solution(mesh):
    placed = (
        P("tm", None, "space", None, None),
        P(None, "space", None, None),
        P(None, "space", None, None),
        P(),
    )
    return jax.shard_map(
        per_device,
        mesh=mesh,
        in_specs=placed,
        out_specs=P("tm", None, "space", None, None),
        check_vma=False,
    )
```

```python
import functools
import math

import jax
import jax.numpy as jnp
from jax import lax
from jax.experimental import pallas as pl
from jax.experimental.pallas import tpu as pltpu
from jax.sharding import PartitionSpec as P

ROUNDS = 3

START_HALO = 5

step_length = 0.5


def lagrange_integral(nodes, j, upper_end):
    coeffs = [1.0]
    scale_down = 1.0
    for i in range(len(nodes)):
        if i != j:
            grown = [0.0] * (len(coeffs) + 1)
            for p in range(len(coeffs)):
                grown[p + 1] = grown[p + 1] + coeffs[p]
                grown[p] = grown[p] - nodes[i] * coeffs[p]
            coeffs = grown
            scale_down = scale_down * (nodes[j] - nodes[i])
    summed_up = 0.0
    for p in range(len(coeffs)):
        summed_up = summed_up + coeffs[p] * upper_end ** (p + 1) / (p + 1)
    return summed_up / scale_down


def node_tables():
    radical = math.sqrt(3.0 / 7.0)
    fine_nodes = [0.0, 0.5 * (1.0 - radical), 0.5, 0.5 * (1.0 + radical), 1.0]
    coarse_nodes = [0.0, 0.5, 1.0]
    integrals = [
        [lagrange_integral(fine_nodes, j, fine_nodes[m]) for j in range(5)] for m in range(5)
    ]
    spread_table = [
        [float(step_length * (integrals[m + 1][j] - integrals[m][j])) for j in range(5)]
        for m in range(4)
    ]
    grouped_table = [
        [spread_table[2 * c][j] + spread_table[2 * c + 1][j] for j in range(5)] for c in range(2)
    ]
    interp_table = []
    for m in range(5):
        weights_row = []
        for k in range(3):
            factor = 1.0
            for i in range(3):
                if i != k:
                    factor = (
                        factor
                        * (fine_nodes[m] - coarse_nodes[i])
                        / (coarse_nodes[k] - coarse_nodes[i])
                    )
            weights_row.append(factor)
        interp_table.append(weights_row)
    widths = [step_length * (fine_nodes[m + 1] - fine_nodes[m]) for m in range(4)]
    return (spread_table, grouped_table, interp_table, widths)


def to_even_odd(a):
    return jnp.concatenate([a[..., 0::2, :], a[..., 1::2, :]], axis=-2)


def from_even_odd(a):
    half = a.shape[-2] // 2
    woven = jnp.stack([a[..., :half, :], a[..., half:, :]], axis=-2)
    return woven.reshape(a.shape)


def crop(field, h):
    a, have = field
    d = have - h
    assert d >= 0
    if d == 0:
        return a
    return lax.slice_in_dim(a, d, a.shape[-3] - d, axis=a.ndim - 3)


def space_halo(a, h):
    if h == 0:
        return a
    size = lax.axis_size("space")
    rows = a.shape[-3]
    assert h <= rows
    up = [(i, (i + 1) % size) for i in range(size)]
    down = [((i + 1) % size, i) for i in range(size)]
    before = lax.ppermute(lax.slice_in_dim(a, rows - h, rows, axis=a.ndim - 3), "space", up)
    after = lax.ppermute(lax.slice_in_dim(a, 0, h, axis=a.ndim - 3), "space", down)
    return jnp.concatenate([before, a, after], axis=a.ndim - 3)


def from_previous_slice(pieces):
    slices = lax.axis_size("tm")
    size = lax.axis_size("space")
    axes = ("tm", "space")

    def moved(piece, shift):
        pairs = [
            (t * size + s, (t + 1) * size + (s + shift) % size)
            for t in range(slices - 1)
            for s in range(size)
        ]
        return lax.ppermute(piece, axes, pairs)

    own, lasts, firsts = pieces
    return moved(own, 0), moved(lasts, 1), moved(firsts, -1)


def react_terms(field, laplace, diffusivity, source):
    first_part = field[0]
    second_part = field[1]
    product = first_part * second_part * second_part
    return jnp.stack(
        [
            diffusivity[0] * laplace[0] - product + source[0],
            diffusivity[1] * laplace[1] + product + source[1],
        ],
        axis=0,
    )


def fine_laplace(a):
    centre = a[..., 1:-1, :, :]
    pair_x = a[..., 2:, :, :] + a[..., :-2, :, :]
    half = centre.shape[-2] // 2
    even = centre[..., :half, :]
    odd = centre[..., half:, :]
    pair_y = jnp.concatenate(
        [odd + jnp.roll(odd, 1, -2), jnp.roll(even, -1, -2) + even], axis=-2
    )
    pair_z = jnp.roll(centre, -1, -1) + jnp.roll(centre, 1, -1)
    return pair_x + pair_y + pair_z - 6.0 * centre


def coarse_laplace(a):
    centre = a[..., 1:-1, :, :]
    pair_x = a[..., 2:, :, :] + a[..., :-2, :, :]
    pair_y = jnp.roll(centre, -1, -2) + jnp.roll(centre, 1, -2)
    pair_z = jnp.roll(centre, -1, -1) + jnp.roll(centre, 1, -1)
    return (pair_x - 2.0 * centre) * 0.25 + (pair_y - 2.0 * centre) * 0.25 + (
        pair_z - 2.0 * centre
    )


def restrict(field):
    a, h = field
    h2 = h - h % 2
    a = crop(field, h2)
    rows = a.shape[-3]
    half = a.shape[-2] // 2
    pairs = a.reshape(a.shape[:-3] + (rows // 2, 2) + a.shape[-2:])
    even = pairs[..., :half, :]
    odd = pairs[..., half:, :]
    upper = even[..., 0, :, :] + even[..., 1, :, :]
    lower = odd[..., 0, :, :] + odd[..., 1, :, :]
    return (upper + lower) * 0.25, h2 // 2


def prolong(a):
    rows = jnp.repeat(a, 2, axis=a.ndim - 3)
    return jnp.concatenate([rows, rows], axis=-2)


def even_odd_load(ref, index=()):
    view = ref.at[index] if index else ref
    lead = (slice(None),) * (len(view.shape) - 2)
    half = view.shape[-2] // 2
    even = view[lead + (pl.ds(0, half, stride=2), slice(None))]
    odd = view[lead + (pl.ds(1, half, stride=2), slice(None))]
    return jnp.concatenate([even, odd], axis=-2)


def kernel_laplace(f):
    centre = f[:, 1:-1]
    pair_x = f[:, 2:] + f[:, :-2]
    half = centre.shape[2] // 2
    even = centre[:, :, :half]
    odd = centre[:, :, half:]
    pair_y = jnp.concatenate(
        [odd + pltpu.roll(odd, 1, 2), pltpu.roll(even, half - 1, 2) + even], axis=2
    )
    lanes = centre.shape[3]
    pair_z = pltpu.roll(centre, lanes - 1, 3) + pltpu.roll(centre, 1, 3)
    return pair_x + pair_y + pair_z - 6.0 * centre


def kernel_restrict(v):
    shape = v.shape
    pairs = v.reshape((shape[0], shape[1] // 2, 2) + shape[2:])
    half = shape[2] // 2
    even = pairs[:, :, :, :half]
    odd = pairs[:, :, :, half:]
    upper = even[:, :, 0] + even[:, :, 1]
    lower = odd[:, :, 0] + odd[:, :, 1]
    return (upper + lower) * 0.25


def sweep_kernel(widths_sent, natural_prior, diff_ref, flag_ref, start_ref, centre_ref, bbefore_ref, bafter_ref,
                 own_ref, before_ref, after_ref, dec_ref, src_ref,
                 rate_ref, recip_ref, n1_ref, n2_ref, n3_ref, n4_ref, e0_ref, b0_ref, cown_ref, clasts_ref,
                 cfirsts_ref):
    spread_table, grouped_table, interp_table, widths = node_tables()
    rows = e0_ref.shape[1]
    hs = (start_ref.shape[1] - rows) // 2
    hd = (dec_ref.shape[1] - rows) // 2
    d0 = diff_ref[0]
    d1 = diff_ref[1]

    def at(ref, h):
        off = hd - h
        return ref[:, off:off + rows + 2 * h]

    def cut(v, have, h):
        d = have - h
        return v[:, d:v.shape[1] - d]

    def terms(f, h):
        laplace = kernel_laplace(f)
        centre = f[:, 1:-1]
        s = at(src_ref, h - 1)
        product = centre[0] * centre[1] * centre[1]
        return jnp.stack([d0 * laplace[0] - product + s[0], d1 * laplace[1] + product + s[1]])

    parts = []
    offset = 0
    for m in range(4):
        w = hs - 1 - m
        parts.append(
            jnp.concatenate(
                [before_ref[:, offset:offset + w], own_ref[m], after_ref[:, offset:offset + w]],
                axis=1,
            )
        )
        offset += w
    if natural_prior:
        pieces = [even_odd_load(r) for r in (bbefore_ref, centre_ref, bafter_ref)]
    else:
        pieces = [r[...] for r in (bbefore_ref, centre_ref, bafter_ref)]
    joined = jnp.concatenate(pieces, axis=1)
    swept = [jnp.where(flag_ref[0] == 1, start_ref[...], joined)]
    found = []
    for m in range(4):
        have = hs - m
        e = terms(swept[m], have)
        found.append(e)
        h = have - 1
        numerator = (cut(swept[m], have, h) + widths[m] * e) + parts[m]
        off = hd - 1 - h
        swept.append(numerator * recip_ref[m, :, off:off + rows + 2 * h])
    found.append(terms(swept[4], hs - 4))
    dec0 = at(dec_ref, 0)
    fulls = [cut(found[j], hs - 1 - j, 0) - dec0 * cut(swept[j], hs - j, 0) for j in range(5)]
    integrated = []
    for c in range(2):
        summed = grouped_table[c][0] * fulls[0]
        for j in range(1, 5):
            summed = summed + grouped_table[c][j] * fulls[j]
        integrated.append(kernel_restrict(summed))
    crows = rows // 2
    hcr = (rate_ref.shape[1] - crows) // 2
    rc = rate_ref[:, hcr:hcr + crows]
    coarse_vals = [kernel_restrict(cut(swept[j], hs - j, 0)) for j in (0, 2, 4)]
    half_step = 0.5 * step_length
    coarse_one = (
        coarse_vals[0] + half_step * rc * coarse_vals[1] + integrated[0]
    ) / (1.0 + half_step * rc)
    sent = [coarse_one, coarse_vals[1], coarse_vals[2], integrated[1]]
    offset = 0
    for i, piece in enumerate(sent):
        cown_ref[i] = piece
        w = widths_sent[i]
        if w:
            clasts_ref[:, offset:offset + w] = piece[:, crows - w:]
            cfirsts_ref[:, offset:offset + w] = piece[:, :w]
        offset += w
    for m, out in ((1, n1_ref), (2, n2_ref), (3, n3_ref), (4, n4_ref)):
        out[...] = cut(swept[m], hs - m, 1)
    e0_ref[...] = cut(found[0], hs - 1, 0)
    b0_ref[...] = cut(swept[0], hs, 0)


def fine_sweep(diffusivity, flag, start, prior, parts, decay, src, rate_c, recip, widths_sent,
               natural_prior):
    rows = start.shape[1] - 2 * START_HALO
    shape = start.shape
    wide = jax.ShapeDtypeStruct((shape[0], rows + 2) + shape[2:], jnp.float32)
    own = jax.ShapeDtypeStruct((shape[0], rows) + shape[2:], jnp.float32)
    cshape = (shape[0], rows // 2, shape[2] // 2, shape[3])
    cown = jax.ShapeDtypeStruct((4,) + cshape, jnp.float32)
    cedge = jax.ShapeDtypeStruct((shape[0], sum(widths_sent)) + cshape[2:], jnp.float32)
    vmem = pl.BlockSpec(memory_space=pltpu.VMEM)
    return pl.pallas_call(
        functools.partial(sweep_kernel, widths_sent, natural_prior),
        out_shape=(wide, wide, wide, wide, own, own, cown, cedge, cedge),
        in_specs=[pl.BlockSpec(memory_space=pltpu.SMEM)] * 2 + [vmem] * 11,
        out_specs=(vmem,) * 9,
    )(diffusivity, flag, start, *prior, *parts, decay, src, rate_c, recip)


def coarse_kernel_laplace(f):
    centre = f[:, 1:-1]
    pair_x = f[:, 2:] + f[:, :-2]
    ny = centre.shape[2]
    lanes = centre.shape[3]
    pair_y = pltpu.roll(centre, ny - 1, 2) + pltpu.roll(centre, 1, 2)
    pair_z = pltpu.roll(centre, lanes - 1, 3) + pltpu.roll(centre, 1, 3)
    return (pair_x - 2.0 * centre) * 0.25 + (pair_y - 2.0 * centre) * 0.25 + (
        pair_z - 2.0 * centre
    )


def finish_kernel(widths_sent, diff_ref, cown_ref, cbefore_ref, cafter_ref, rate_ref, csrc_ref,
                  n1_ref, n2_ref, n3_ref, n4_ref, b_ref, e0_ref, dec_ref, src_ref, *outs):
    spread_table, grouped_table, interp_table, widths = node_tables()
    last = len(outs) == 1
    rows = e0_ref.shape[1]
    crows = rows // 2
    ho = widths_sent[2]
    joined = []
    offset = 0
    for i in range(4):
        w = widths_sent[i]
        if w:
            joined.append(
                jnp.concatenate(
                    [cbefore_ref[:, offset:offset + w], cown_ref[i], cafter_ref[:, offset:offset + w]],
                    axis=1,
                )
            )
        else:
            joined.append(cown_ref[i])
        offset += w
    one, mid, low, late = joined
    hcr = (rate_ref.shape[1] - crows) // 2
    hd = (dec_ref.shape[1] - rows) // 2
    hs = START_HALO
    d0 = diff_ref[0]
    d1 = diff_ref[1]

    def at(ref, h, size, have):
        off = have - h
        return ref[:, off:off + size + 2 * h]

    def cut(v, have, h):
        d = have - h
        return v[:, d:v.shape[1] - d]

    def react(centre, laplace, s):
        product = centre[0] * centre[1] * centre[1]
        return jnp.stack([d0 * laplace[0] - product + s[0], d1 * laplace[1] + product + s[1]])

    def coarse_terms(v):
        return react(v[:, 1:-1], coarse_kernel_laplace(v), at(csrc_ref, ho, crows, hcr))

    half_step = 0.5 * step_length
    rc = at(rate_ref, ho, crows, hcr)
    coarse_two = (
        cut(one, ho + 1, ho)
        + half_step * (coarse_terms(one) - coarse_terms(mid))
        + half_step * rc * low
        + late
    ) / (1.0 + half_step * rc)
    delta_one = cut(one, ho + 1, ho) - cut(mid, ho + 1, ho)
    delta_two = coarse_two - low

    def prolonged(c):
        shape = c.shape
        doubled = jnp.broadcast_to(c[:, :, None], (shape[0], shape[1], 2) + shape[2:])
        doubled = doubled.reshape((shape[0], 2 * shape[1]) + shape[2:])
        return jnp.concatenate([doubled, doubled], axis=2)

    news = {}
    for m, ref in ((1, n1_ref), (2, n2_ref), (3, n3_ref), (4, n4_ref)):
        if last and m < 4:
            continue
        fine = prolonged(interp_table[m][1] * delta_one + interp_table[m][2] * delta_two)
        news[m] = cut(ref[...], 1, ho) + cut(fine, 2 * ho, ho)
    if last:
        half = news[4].shape[2] // 2
        outs[0][:, :, pl.ds(0, half, stride=2), :] = news[4][:, :, :half]
        outs[0][:, :, pl.ds(1, half, stride=2), :] = news[4][:, :, half:]
        return
    own_out, lasts_out, firsts_out, u4_out, u4_last_out, u4_first_out = outs
    src1 = at(src_ref, 0, rows, hd)
    dec0 = at(dec_ref, 0, rows, hd)
    states = [b_ref[...]] + [cut(news[m], 1, 0) for m in range(1, 5)]
    terms = [e0_ref[...]] + [
        react(cut(news[m], 1, 0), kernel_laplace(news[m]), src1) for m in range(1, 5)
    ]
    fulls = [terms[j] - dec0 * states[j] for j in range(5)]
    offset = 0
    for m in range(4):
        summed = spread_table[m][0] * fulls[0]
        for j in range(1, 5):
            summed = summed + spread_table[m][j] * fulls[j]
        part = (widths[m] * dec0 * states[m + 1] - widths[m] * terms[m]) + summed
        own_out[m] = part
        w = hs - 1 - m
        lasts_out[:, offset:offset + w] = part[:, rows - w:]
        firsts_out[:, offset:offset + w] = part[:, :w]
        offset += w
    u4_out[...] = states[4]
    u4_last_out[...] = states[4][:, rows - hs:]
    u4_first_out[...] = states[4][:, :hs]


def finish_round(diffusivity, coarse, rate_c, source_c, swept, e0, decay, src, last, widths_sent):
    begin = swept[0]
    shape = begin.shape
    rows = e0.shape[1]
    field = jax.ShapeDtypeStruct((shape[0], rows) + shape[2:], jnp.float32)
    if last:
        out_shape = (field,)
    else:
        sent = sum(START_HALO - 1 - m for m in range(4))
        edge = jax.ShapeDtypeStruct((shape[0], sent) + shape[2:], jnp.float32)
        rim = jax.ShapeDtypeStruct((shape[0], START_HALO) + shape[2:], jnp.float32)
        out_shape = (jax.ShapeDtypeStruct((4,) + field.shape, jnp.float32), edge, edge, field, rim, rim)
    vmem = pl.BlockSpec(memory_space=pltpu.VMEM)
    args = (diffusivity, *coarse, rate_c, source_c, *swept[1:], begin, e0, decay, src)
    return pl.pallas_call(
        functools.partial(finish_kernel, widths_sent),
        out_shape=out_shape,
        in_specs=[pl.BlockSpec(memory_space=pltpu.SMEM)] + [vmem] * (len(args) - 1),
        out_specs=(vmem,) * len(out_shape),
    )(*args)


def start_kernel(diff_ref, stacked_ref, own_ref, before_ref, after_ref, rate_ref, csrc_ref,
                 ext_ref, dec_ref, src_ref, recip_ref):
    spread_table, grouped_table, interp_table, widths = node_tables()
    rows = own_ref.shape[2]
    hs = (stacked_ref.shape[2] - rows) // 2
    d0 = diff_ref[0]
    d1 = diff_ref[1]
    state = even_odd_load(stacked_ref, (0,))
    decay = even_odd_load(stacked_ref, (1,))
    source = even_odd_load(stacked_ref, (2,))
    ext_ref[...] = state
    dec_ref[...] = decay
    src_ref[...] = source
    inner = state[:, 1:-1]
    dec = decay[:, 1:-1]
    s = source[:, 1:-1]
    laplace = kernel_laplace(state)
    product = inner[0] * inner[1] * inner[1]
    terms = jnp.stack([d0 * laplace[0] - product + s[0], d1 * laplace[1] + product + s[1]])
    full = terms - dec * inner
    edge = hs - 1
    offset = 0
    for m in range(4):
        summed = spread_table[m][0] * full
        for j in range(1, 5):
            summed = summed + spread_table[m][j] * full
        part = (widths[m] * dec * inner - widths[m] * terms) + summed
        own_ref[m] = part[:, edge:edge + rows]
        w = edge - m
        before_ref[:, offset:offset + w] = part[:, m:edge]
        after_ref[:, offset:offset + w] = part[:, edge + rows:edge + rows + w]
        offset += w
    rate_ref[...] = kernel_restrict(dec)
    csrc_ref[...] = kernel_restrict(s)
    for m in range(4):
        recip_ref[m] = 1.0 / (1.0 + widths[m] * dec)


def start_terms(diffusivity, stacked):
    shape = stacked.shape[1:]
    rows = shape[1] - 2 * START_HALO
    sent = sum(START_HALO - 1 - m for m in range(4))
    edge = jax.ShapeDtypeStruct((shape[0], sent) + shape[2:], jnp.float32)
    cshape = (shape[0], (rows + 2 * (START_HALO - 1)) // 2, shape[2] // 2, shape[3])
    coarse = jax.ShapeDtypeStruct(cshape, jnp.float32)
    vmem = pl.BlockSpec(memory_space=pltpu.VMEM)
    return pl.pallas_call(
        start_kernel,
        out_shape=(
            jax.ShapeDtypeStruct((4, shape[0], rows) + shape[2:], jnp.float32),
            edge, edge, coarse, coarse,
            jax.ShapeDtypeStruct(shape, jnp.float32),
            jax.ShapeDtypeStruct(shape, jnp.float32),
            jax.ShapeDtypeStruct(shape, jnp.float32),
            jax.ShapeDtypeStruct((4, shape[0], shape[1] - 2) + shape[2:], jnp.float32),
        ),
        in_specs=[pl.BlockSpec(memory_space=pltpu.SMEM)] + [vmem],
        out_specs=(vmem,) * 9,
    )(diffusivity, stacked)


def packed_halo(fields):
    size = lax.axis_size("space")
    rows = fields[0][0].shape[-3]
    axis = fields[0][0].ndim - 3
    up = [(i, (i + 1) % size) for i in range(size)]
    down = [((i + 1) % size, i) for i in range(size)]
    lasts = jnp.concatenate(
        [lax.slice_in_dim(a, rows - w, rows, axis=axis) for a, w in fields], axis=axis
    )
    firsts = jnp.concatenate([lax.slice_in_dim(a, 0, w, axis=axis) for a, w in fields], axis=axis)
    before = lax.ppermute(lasts, "space", up)
    after = lax.ppermute(firsts, "space", down)
    out = []
    offset = 0
    for a, w in fields:
        out.append(
            (
                jnp.concatenate(
                    [
                        lax.slice_in_dim(before, offset, offset + w, axis=axis),
                        a,
                        lax.slice_in_dim(after, offset, offset + w, axis=axis),
                    ],
                    axis=axis,
                ),
                w,
            )
        )
        offset += w
    return out


def per_device(initial, decay_rate, source, diffusivity):
    spread_table, grouped_table, interp_table, widths = node_tables()
    first_slice = lax.axis_index("tm") == 0
    hs = START_HALO
    assert hs == 5 and initial.shape[-3] >= hs

    own_start = initial[0]
    stacked = space_halo(jnp.stack([own_start, decay_rate, source]), hs)
    own4, before4, after4, rate_own, csrc_own, own_ext, dec_ext, src_ext, recip = start_terms(
        diffusivity, stacked
    )
    decay = (dec_ext, hs)
    src = (src_ext, hs)
    rate_c = (rate_own, (hs - 1) // 2)
    source_c = (csrc_own, (hs - 1) // 2)

    def fine_E(field):
        a, h = field
        laplace = fine_laplace(a)
        return react_terms(a[..., 1:-1, :, :], laplace, diffusivity, crop(src, h - 1)), h - 1

    def coarse_E(field):
        a, h = field
        laplace = coarse_laplace(a)
        return react_terms(a[..., 1:-1, :, :], laplace, diffusivity, crop(source_c, h - 1)), h - 1

    def full(field, field_E):
        h = min(field[1], field_E[1])
        return crop(field_E, h) - crop(decay, h) * crop(field, h), h

    def step_terms(states, terms):
        fulls = [full(states[j], terms[j]) for j in range(5)]
        hf = min(f[1] for f in fulls)
        out = []
        for m in range(4):
            h = min(hf, terms[m][1], states[m + 1][1])
            summed = spread_table[m][0] * crop(fulls[0], h)
            for j in range(1, 5):
                summed = summed + spread_table[m][j] * crop(fulls[j], h)
            own = (
                widths[m] * crop(decay, h) * crop(states[m + 1], h)
                - widths[m] * crop(terms[m], h)
            ) + summed
            out.append((own, h))
        return out

    def advance(prior, pieces, last, natural):
        widths_sent = (1, 1, 0, 0) if last else (2, 2, 1, 1)
        n1, n2, n3, n4, e0, b0, cown, clasts, cfirsts = fine_sweep(
            diffusivity, flag, own_ext, prior, pieces, decay[0], src[0], rate_c[0], recip,
            widths_sent, natural,
        )
        coarse = (
            cown,
            lax.ppermute(clasts, "space", up),
            lax.ppermute(cfirsts, "space", down),
        )
        return finish_round(
            diffusivity, coarse, rate_c[0], source_c[0],
            (b0, n1, n2, n3, n4), e0, decay[0], src[0], last, widths_sent,
        )

    size = lax.axis_size("space")
    up = [(i, (i + 1) % size) for i in range(size)]
    down = [((i + 1) % size, i) for i in range(size)]
    rows = own_start.shape[-3]
    flag = jnp.where(first_slice, 1, 0).astype(jnp.int32).reshape(1)
    pieces = (own4, before4, after4)
    prior = from_previous_slice(
        (own_start, own_start[:, rows - hs:], own_start[:, :hs])
    )
    for k in range(ROUNDS):
        last = k + 1 == ROUNDS
        outs = advance(prior, pieces, last, k == 0)
        if not last:
            own4, lasts, firsts, u4, u4_last, u4_first = outs
            pieces = (
                own4,
                lax.ppermute(lasts, "space", up),
                lax.ppermute(firsts, "space", down),
            )
            prior = from_previous_slice((u4, u4_last, u4_first))
    return outs[0][None]


def solution(mesh):
    placed = (
        P("tm", None, "space", None, None),
        P(None, "space", None, None),
        P(None, "space", None, None),
        P(),
    )
    return jax.shard_map(
        per_device,
        mesh=mesh,
        in_specs=placed,
        out_specs=P("tm", None, "space", None, None),
        check_vma=False,
    )
```

```python
import functools
import math

import jax
import jax.numpy as jnp
from jax import lax
from jax.experimental import pallas as pl
from jax.experimental.pallas import tpu as pltpu
from jax.sharding import PartitionSpec as P

ROUNDS = 3

START_HALO = 5

step_length = 0.5


def lagrange_integral(nodes, j, upper_end):
    coeffs = [1.0]
    scale_down = 1.0
    for i in range(len(nodes)):
        if i != j:
            grown = [0.0] * (len(coeffs) + 1)
            for p in range(len(coeffs)):
                grown[p + 1] = grown[p + 1] + coeffs[p]
                grown[p] = grown[p] - nodes[i] * coeffs[p]
            coeffs = grown
            scale_down = scale_down * (nodes[j] - nodes[i])
    summed_up = 0.0
    for p in range(len(coeffs)):
        summed_up = summed_up + coeffs[p] * upper_end ** (p + 1) / (p + 1)
    return summed_up / scale_down


def node_tables():
    radical = math.sqrt(3.0 / 7.0)
    fine_nodes = [0.0, 0.5 * (1.0 - radical), 0.5, 0.5 * (1.0 + radical), 1.0]
    coarse_nodes = [0.0, 0.5, 1.0]
    integrals = [
        [lagrange_integral(fine_nodes, j, fine_nodes[m]) for j in range(5)] for m in range(5)
    ]
    spread_table = [
        [float(step_length * (integrals[m + 1][j] - integrals[m][j])) for j in range(5)]
        for m in range(4)
    ]
    grouped_table = [
        [spread_table[2 * c][j] + spread_table[2 * c + 1][j] for j in range(5)] for c in range(2)
    ]
    interp_table = []
    for m in range(5):
        weights_row = []
        for k in range(3):
            factor = 1.0
            for i in range(3):
                if i != k:
                    factor = (
                        factor
                        * (fine_nodes[m] - coarse_nodes[i])
                        / (coarse_nodes[k] - coarse_nodes[i])
                    )
            weights_row.append(factor)
        interp_table.append(weights_row)
    widths = [step_length * (fine_nodes[m + 1] - fine_nodes[m]) for m in range(4)]
    return (spread_table, grouped_table, interp_table, widths)


def to_even_odd(a):
    return jnp.concatenate([a[..., 0::2, :], a[..., 1::2, :]], axis=-2)


def from_even_odd(a):
    half = a.shape[-2] // 2
    woven = jnp.stack([a[..., :half, :], a[..., half:, :]], axis=-2)
    return woven.reshape(a.shape)


def crop(field, h):
    a, have = field
    d = have - h
    assert d >= 0
    if d == 0:
        return a
    return lax.slice_in_dim(a, d, a.shape[-3] - d, axis=a.ndim - 3)


def space_halo(a, h):
    if h == 0:
        return a
    size = lax.axis_size("space")
    rows = a.shape[-3]
    assert h <= rows
    up = [(i, (i + 1) % size) for i in range(size)]
    down = [((i + 1) % size, i) for i in range(size)]
    before = lax.ppermute(lax.slice_in_dim(a, rows - h, rows, axis=a.ndim - 3), "space", up)
    after = lax.ppermute(lax.slice_in_dim(a, 0, h, axis=a.ndim - 3), "space", down)
    return jnp.concatenate([before, a, after], axis=a.ndim - 3)


def from_previous_slice(pieces):
    slices = lax.axis_size("tm")
    size = lax.axis_size("space")
    axes = ("tm", "space")

    def moved(piece, shift):
        pairs = [
            (t * size + s, (t + 1) * size + (s + shift) % size)
            for t in range(slices - 1)
            for s in range(size)
        ]
        return lax.ppermute(piece, axes, pairs)

    own, lasts, firsts = pieces
    return moved(own, 0), moved(lasts, 1), moved(firsts, -1)


def react_terms(field, laplace, diffusivity, source):
    first_part = field[0]
    second_part = field[1]
    product = first_part * second_part * second_part
    return jnp.stack(
        [
            diffusivity[0] * laplace[0] - product + source[0],
            diffusivity[1] * laplace[1] + product + source[1],
        ],
        axis=0,
    )


def fine_laplace(a):
    centre = a[..., 1:-1, :, :]
    pair_x = a[..., 2:, :, :] + a[..., :-2, :, :]
    half = centre.shape[-2] // 2
    even = centre[..., :half, :]
    odd = centre[..., half:, :]
    pair_y = jnp.concatenate(
        [odd + jnp.roll(odd, 1, -2), jnp.roll(even, -1, -2) + even], axis=-2
    )
    pair_z = jnp.roll(centre, -1, -1) + jnp.roll(centre, 1, -1)
    return pair_x + pair_y + pair_z - 6.0 * centre


def coarse_laplace(a):
    centre = a[..., 1:-1, :, :]
    pair_x = a[..., 2:, :, :] + a[..., :-2, :, :]
    pair_y = jnp.roll(centre, -1, -2) + jnp.roll(centre, 1, -2)
    pair_z = jnp.roll(centre, -1, -1) + jnp.roll(centre, 1, -1)
    return (pair_x - 2.0 * centre) * 0.25 + (pair_y - 2.0 * centre) * 0.25 + (
        pair_z - 2.0 * centre
    )


def restrict(field):
    a, h = field
    h2 = h - h % 2
    a = crop(field, h2)
    rows = a.shape[-3]
    half = a.shape[-2] // 2
    pairs = a.reshape(a.shape[:-3] + (rows // 2, 2) + a.shape[-2:])
    even = pairs[..., :half, :]
    odd = pairs[..., half:, :]
    upper = even[..., 0, :, :] + even[..., 1, :, :]
    lower = odd[..., 0, :, :] + odd[..., 1, :, :]
    return (upper + lower) * 0.25, h2 // 2


def prolong(a):
    rows = jnp.repeat(a, 2, axis=a.ndim - 3)
    return jnp.concatenate([rows, rows], axis=-2)


def even_odd_load(ref, index=()):
    view = ref.at[index] if index else ref
    lead = (slice(None),) * (len(view.shape) - 2)
    half = view.shape[-2] // 2
    even = view[lead + (pl.ds(0, half, stride=2), slice(None))]
    odd = view[lead + (pl.ds(1, half, stride=2), slice(None))]
    return jnp.concatenate([even, odd], axis=-2)


def kernel_laplace(f):
    centre = f[:, 1:-1]
    pair_x = f[:, 2:] + f[:, :-2]
    half = centre.shape[2] // 2
    even = centre[:, :, :half]
    odd = centre[:, :, half:]
    pair_y = jnp.concatenate(
        [odd + pltpu.roll(odd, 1, 2), pltpu.roll(even, half - 1, 2) + even], axis=2
    )
    lanes = centre.shape[3]
    pair_z = pltpu.roll(centre, lanes - 1, 3) + pltpu.roll(centre, 1, 3)
    return pair_x + pair_y + pair_z - 6.0 * centre


def kernel_restrict(v):
    shape = v.shape
    pairs = v.reshape((shape[0], shape[1] // 2, 2) + shape[2:])
    half = shape[2] // 2
    even = pairs[:, :, :, :half]
    odd = pairs[:, :, :, half:]
    upper = even[:, :, 0] + even[:, :, 1]
    lower = odd[:, :, 0] + odd[:, :, 1]
    return (upper + lower) * 0.25


def sweep_kernel(widths_sent, natural_prior, diff_ref, flag_ref, start_ref, centre_ref, bbefore_ref, bafter_ref,
                 own_ref, before_ref, after_ref, dec_ref, src_ref,
                 rate_ref, n1_ref, n2_ref, n3_ref, n4_ref, e0_ref, b0_ref, cown_ref, clasts_ref,
                 cfirsts_ref):
    spread_table, grouped_table, interp_table, widths = node_tables()
    rows = e0_ref.shape[1]
    hs = (start_ref.shape[1] - rows) // 2
    hd = (dec_ref.shape[1] - rows) // 2
    d0 = diff_ref[0]
    d1 = diff_ref[1]

    def at(ref, h):
        off = hd - h
        return ref[:, off:off + rows + 2 * h]

    def cut(v, have, h):
        d = have - h
        return v[:, d:v.shape[1] - d]

    def terms(f, h):
        laplace = kernel_laplace(f)
        centre = f[:, 1:-1]
        s = at(src_ref, h - 1)
        product = centre[0] * centre[1] * centre[1]
        return jnp.stack([d0 * laplace[0] - product + s[0], d1 * laplace[1] + product + s[1]])

    parts = []
    offset = 0
    for m in range(4):
        w = hs - 1 - m
        parts.append(
            jnp.concatenate(
                [before_ref[:, offset:offset + w], own_ref[m], after_ref[:, offset:offset + w]],
                axis=1,
            )
        )
        offset += w
    if natural_prior:
        pieces = [even_odd_load(r) for r in (bbefore_ref, centre_ref, bafter_ref)]
    else:
        pieces = [r[...] for r in (bbefore_ref, centre_ref, bafter_ref)]
    joined = jnp.concatenate(pieces, axis=1)
    swept = [jnp.where(flag_ref[0] == 1, start_ref[...], joined)]
    found = []
    for m in range(4):
        have = hs - m
        e = terms(swept[m], have)
        found.append(e)
        h = have - 1
        numerator = (cut(swept[m], have, h) + widths[m] * e) + parts[m]
        swept.append(numerator / (1.0 + widths[m] * at(dec_ref, h)))
    found.append(terms(swept[4], hs - 4))
    dec0 = at(dec_ref, 0)
    fulls = [cut(found[j], hs - 1 - j, 0) - dec0 * cut(swept[j], hs - j, 0) for j in range(5)]
    integrated = []
    for c in range(2):
        summed = grouped_table[c][0] * fulls[0]
        for j in range(1, 5):
            summed = summed + grouped_table[c][j] * fulls[j]
        integrated.append(kernel_restrict(summed))
    crows = rows // 2
    hcr = (rate_ref.shape[1] - crows) // 2
    rc = rate_ref[:, hcr:hcr + crows]
    coarse_vals = [kernel_restrict(cut(swept[j], hs - j, 0)) for j in (0, 2, 4)]
    half_step = 0.5 * step_length
    coarse_one = (
        coarse_vals[0] + half_step * rc * coarse_vals[1] + integrated[0]
    ) / (1.0 + half_step * rc)
    sent = [coarse_one, coarse_vals[1], coarse_vals[2], integrated[1]]
    offset = 0
    for i, piece in enumerate(sent):
        cown_ref[i] = piece
        w = widths_sent[i]
        if w:
            clasts_ref[:, offset:offset + w] = piece[:, crows - w:]
            cfirsts_ref[:, offset:offset + w] = piece[:, :w]
        offset += w
    for m, out in ((1, n1_ref), (2, n2_ref), (3, n3_ref), (4, n4_ref)):
        out[...] = cut(swept[m], hs - m, 1)
    e0_ref[...] = cut(found[0], hs - 1, 0)
    b0_ref[...] = cut(swept[0], hs, 0)


def fine_sweep(diffusivity, flag, start, prior, parts, decay, src, rate_c, widths_sent,
               natural_prior):
    rows = start.shape[1] - 2 * START_HALO
    shape = start.shape
    wide = jax.ShapeDtypeStruct((shape[0], rows + 2) + shape[2:], jnp.float32)
    own = jax.ShapeDtypeStruct((shape[0], rows) + shape[2:], jnp.float32)
    cshape = (shape[0], rows // 2, shape[2] // 2, shape[3])
    cown = jax.ShapeDtypeStruct((4,) + cshape, jnp.float32)
    cedge = jax.ShapeDtypeStruct((shape[0], sum(widths_sent)) + cshape[2:], jnp.float32)
    vmem = pl.BlockSpec(memory_space=pltpu.VMEM)
    return pl.pallas_call(
        functools.partial(sweep_kernel, widths_sent, natural_prior),
        out_shape=(wide, wide, wide, wide, own, own, cown, cedge, cedge),
        in_specs=[pl.BlockSpec(memory_space=pltpu.SMEM)] * 2 + [vmem] * 10,
        out_specs=(vmem,) * 9,
    )(diffusivity, flag, start, *prior, *parts, decay, src, rate_c)


def coarse_kernel_laplace(f):
    centre = f[:, 1:-1]
    pair_x = f[:, 2:] + f[:, :-2]
    ny = centre.shape[2]
    lanes = centre.shape[3]
    pair_y = pltpu.roll(centre, ny - 1, 2) + pltpu.roll(centre, 1, 2)
    pair_z = pltpu.roll(centre, lanes - 1, 3) + pltpu.roll(centre, 1, 3)
    return (pair_x - 2.0 * centre) * 0.25 + (pair_y - 2.0 * centre) * 0.25 + (
        pair_z - 2.0 * centre
    )


def finish_kernel(widths_sent, diff_ref, cown_ref, cbefore_ref, cafter_ref, rate_ref, csrc_ref,
                  n1_ref, n2_ref, n3_ref, n4_ref, b_ref, e0_ref, dec_ref, src_ref, *outs):
    spread_table, grouped_table, interp_table, widths = node_tables()
    last = len(outs) == 1
    rows = e0_ref.shape[1]
    crows = rows // 2
    ho = widths_sent[2]
    joined = []
    offset = 0
    for i in range(4):
        w = widths_sent[i]
        if w:
            joined.append(
                jnp.concatenate(
                    [cbefore_ref[:, offset:offset + w], cown_ref[i], cafter_ref[:, offset:offset + w]],
                    axis=1,
                )
            )
        else:
            joined.append(cown_ref[i])
        offset += w
    one, mid, low, late = joined
    hcr = (rate_ref.shape[1] - crows) // 2
    hd = (dec_ref.shape[1] - rows) // 2
    hs = START_HALO
    d0 = diff_ref[0]
    d1 = diff_ref[1]

    def at(ref, h, size, have):
        off = have - h
        return ref[:, off:off + size + 2 * h]

    def cut(v, have, h):
        d = have - h
        return v[:, d:v.shape[1] - d]

    def react(centre, laplace, s):
        product = centre[0] * centre[1] * centre[1]
        return jnp.stack([d0 * laplace[0] - product + s[0], d1 * laplace[1] + product + s[1]])

    def coarse_terms(v):
        return react(v[:, 1:-1], coarse_kernel_laplace(v), at(csrc_ref, ho, crows, hcr))

    half_step = 0.5 * step_length
    rc = at(rate_ref, ho, crows, hcr)
    coarse_two = (
        cut(one, ho + 1, ho)
        + half_step * (coarse_terms(one) - coarse_terms(mid))
        + half_step * rc * low
        + late
    ) / (1.0 + half_step * rc)
    delta_one = cut(one, ho + 1, ho) - cut(mid, ho + 1, ho)
    delta_two = coarse_two - low

    def prolonged(c):
        shape = c.shape
        doubled = jnp.broadcast_to(c[:, :, None], (shape[0], shape[1], 2) + shape[2:])
        doubled = doubled.reshape((shape[0], 2 * shape[1]) + shape[2:])
        return jnp.concatenate([doubled, doubled], axis=2)

    news = {}
    for m, ref in ((1, n1_ref), (2, n2_ref), (3, n3_ref), (4, n4_ref)):
        if last and m < 4:
            continue
        fine = prolonged(interp_table[m][1] * delta_one + interp_table[m][2] * delta_two)
        news[m] = cut(ref[...], 1, ho) + cut(fine, 2 * ho, ho)
    if last:
        half = news[4].shape[2] // 2
        outs[0][:, :, pl.ds(0, half, stride=2), :] = news[4][:, :, :half]
        outs[0][:, :, pl.ds(1, half, stride=2), :] = news[4][:, :, half:]
        return
    own_out, lasts_out, firsts_out, u4_out, u4_last_out, u4_first_out = outs
    src1 = at(src_ref, 0, rows, hd)
    dec0 = at(dec_ref, 0, rows, hd)
    states = [b_ref[...]] + [cut(news[m], 1, 0) for m in range(1, 5)]
    terms = [e0_ref[...]] + [
        react(cut(news[m], 1, 0), kernel_laplace(news[m]), src1) for m in range(1, 5)
    ]
    fulls = [terms[j] - dec0 * states[j] for j in range(5)]
    offset = 0
    for m in range(4):
        summed = spread_table[m][0] * fulls[0]
        for j in range(1, 5):
            summed = summed + spread_table[m][j] * fulls[j]
        part = (widths[m] * dec0 * states[m + 1] - widths[m] * terms[m]) + summed
        own_out[m] = part
        w = hs - 1 - m
        lasts_out[:, offset:offset + w] = part[:, rows - w:]
        firsts_out[:, offset:offset + w] = part[:, :w]
        offset += w
    u4_out[...] = states[4]
    u4_last_out[...] = states[4][:, rows - hs:]
    u4_first_out[...] = states[4][:, :hs]


def finish_round(diffusivity, coarse, rate_c, source_c, swept, e0, decay, src, last, widths_sent):
    begin = swept[0]
    shape = begin.shape
    rows = e0.shape[1]
    field = jax.ShapeDtypeStruct((shape[0], rows) + shape[2:], jnp.float32)
    if last:
        out_shape = (field,)
    else:
        sent = sum(START_HALO - 1 - m for m in range(4))
        edge = jax.ShapeDtypeStruct((shape[0], sent) + shape[2:], jnp.float32)
        rim = jax.ShapeDtypeStruct((shape[0], START_HALO) + shape[2:], jnp.float32)
        out_shape = (jax.ShapeDtypeStruct((4,) + field.shape, jnp.float32), edge, edge, field, rim, rim)
    vmem = pl.BlockSpec(memory_space=pltpu.VMEM)
    args = (diffusivity, *coarse, rate_c, source_c, *swept[1:], begin, e0, decay, src)
    return pl.pallas_call(
        functools.partial(finish_kernel, widths_sent),
        out_shape=out_shape,
        in_specs=[pl.BlockSpec(memory_space=pltpu.SMEM)] + [vmem] * (len(args) - 1),
        out_specs=(vmem,) * len(out_shape),
    )(*args)


def start_kernel(diff_ref, stacked_ref, own_ref, before_ref, after_ref, rate_ref, csrc_ref,
                 ext_ref, dec_ref, src_ref):
    spread_table, grouped_table, interp_table, widths = node_tables()
    rows = own_ref.shape[2]
    hs = (stacked_ref.shape[2] - rows) // 2
    d0 = diff_ref[0]
    d1 = diff_ref[1]
    state = even_odd_load(stacked_ref, (0,))
    decay = even_odd_load(stacked_ref, (1,))
    source = even_odd_load(stacked_ref, (2,))
    ext_ref[...] = state
    dec_ref[...] = decay
    src_ref[...] = source
    inner = state[:, 1:-1]
    dec = decay[:, 1:-1]
    s = source[:, 1:-1]
    laplace = kernel_laplace(state)
    product = inner[0] * inner[1] * inner[1]
    terms = jnp.stack([d0 * laplace[0] - product + s[0], d1 * laplace[1] + product + s[1]])
    full = terms - dec * inner
    edge = hs - 1
    offset = 0
    for m in range(4):
        weight = sum(spread_table[m][j] for j in range(5))
        part = (widths[m] * dec * inner - widths[m] * terms) + weight * full
        own_ref[m] = part[:, edge:edge + rows]
        w = edge - m
        before_ref[:, offset:offset + w] = part[:, m:edge]
        after_ref[:, offset:offset + w] = part[:, edge + rows:edge + rows + w]
        offset += w
    rate_ref[...] = kernel_restrict(dec)
    csrc_ref[...] = kernel_restrict(s)


def start_terms(diffusivity, stacked):
    shape = stacked.shape[1:]
    rows = shape[1] - 2 * START_HALO
    sent = sum(START_HALO - 1 - m for m in range(4))
    edge = jax.ShapeDtypeStruct((shape[0], sent) + shape[2:], jnp.float32)
    cshape = (shape[0], (rows + 2 * (START_HALO - 1)) // 2, shape[2] // 2, shape[3])
    coarse = jax.ShapeDtypeStruct(cshape, jnp.float32)
    vmem = pl.BlockSpec(memory_space=pltpu.VMEM)
    return pl.pallas_call(
        start_kernel,
        out_shape=(
            jax.ShapeDtypeStruct((4, shape[0], rows) + shape[2:], jnp.float32),
            edge, edge, coarse, coarse,
            jax.ShapeDtypeStruct(shape, jnp.float32),
            jax.ShapeDtypeStruct(shape, jnp.float32),
            jax.ShapeDtypeStruct(shape, jnp.float32),
        ),
        in_specs=[pl.BlockSpec(memory_space=pltpu.SMEM)] + [vmem],
        out_specs=(vmem,) * 8,
    )(diffusivity, stacked)


def packed_halo(fields):
    size = lax.axis_size("space")
    rows = fields[0][0].shape[-3]
    axis = fields[0][0].ndim - 3
    up = [(i, (i + 1) % size) for i in range(size)]
    down = [((i + 1) % size, i) for i in range(size)]
    lasts = jnp.concatenate(
        [lax.slice_in_dim(a, rows - w, rows, axis=axis) for a, w in fields], axis=axis
    )
    firsts = jnp.concatenate([lax.slice_in_dim(a, 0, w, axis=axis) for a, w in fields], axis=axis)
    before = lax.ppermute(lasts, "space", up)
    after = lax.ppermute(firsts, "space", down)
    out = []
    offset = 0
    for a, w in fields:
        out.append(
            (
                jnp.concatenate(
                    [
                        lax.slice_in_dim(before, offset, offset + w, axis=axis),
                        a,
                        lax.slice_in_dim(after, offset, offset + w, axis=axis),
                    ],
                    axis=axis,
                ),
                w,
            )
        )
        offset += w
    return out


def per_device(initial, decay_rate, source, diffusivity):
    spread_table, grouped_table, interp_table, widths = node_tables()
    first_slice = lax.axis_index("tm") == 0
    hs = START_HALO
    assert hs == 5 and initial.shape[-3] >= hs

    own_start = initial[0]
    stacked = space_halo(jnp.stack([own_start, decay_rate, source]), hs)
    own4, before4, after4, rate_own, csrc_own, own_ext, dec_ext, src_ext = start_terms(
        diffusivity, stacked
    )
    decay = (dec_ext, hs)
    src = (src_ext, hs)
    rate_c = (rate_own, (hs - 1) // 2)
    source_c = (csrc_own, (hs - 1) // 2)

    def fine_E(field):
        a, h = field
        laplace = fine_laplace(a)
        return react_terms(a[..., 1:-1, :, :], laplace, diffusivity, crop(src, h - 1)), h - 1

    def coarse_E(field):
        a, h = field
        laplace = coarse_laplace(a)
        return react_terms(a[..., 1:-1, :, :], laplace, diffusivity, crop(source_c, h - 1)), h - 1

    def full(field, field_E):
        h = min(field[1], field_E[1])
        return crop(field_E, h) - crop(decay, h) * crop(field, h), h

    def step_terms(states, terms):
        fulls = [full(states[j], terms[j]) for j in range(5)]
        hf = min(f[1] for f in fulls)
        out = []
        for m in range(4):
            h = min(hf, terms[m][1], states[m + 1][1])
            summed = spread_table[m][0] * crop(fulls[0], h)
            for j in range(1, 5):
                summed = summed + spread_table[m][j] * crop(fulls[j], h)
            own = (
                widths[m] * crop(decay, h) * crop(states[m + 1], h)
                - widths[m] * crop(terms[m], h)
            ) + summed
            out.append((own, h))
        return out

    def advance(prior, pieces, last, natural):
        widths_sent = (1, 1, 0, 0) if last else (2, 2, 1, 1)
        n1, n2, n3, n4, e0, b0, cown, clasts, cfirsts = fine_sweep(
            diffusivity, flag, own_ext, prior, pieces, decay[0], src[0], rate_c[0], widths_sent,
            natural,
        )
        coarse = (
            cown,
            lax.ppermute(clasts, "space", up),
            lax.ppermute(cfirsts, "space", down),
        )
        return finish_round(
            diffusivity, coarse, rate_c[0], source_c[0],
            (b0, n1, n2, n3, n4), e0, decay[0], src[0], last, widths_sent,
        )

    size = lax.axis_size("space")
    up = [(i, (i + 1) % size) for i in range(size)]
    down = [((i + 1) % size, i) for i in range(size)]
    rows = own_start.shape[-3]
    flag = jnp.where(first_slice, 1, 0).astype(jnp.int32).reshape(1)
    pieces = (own4, before4, after4)
    prior = from_previous_slice(
        (own_start, own_start[:, rows - hs:], own_start[:, :hs])
    )
    for k in range(ROUNDS):
        last = k + 1 == ROUNDS
        outs = advance(prior, pieces, last, k == 0)
        if not last:
            own4, lasts, firsts, u4, u4_last, u4_first = outs
            pieces = (
                own4,
                lax.ppermute(lasts, "space", up),
                lax.ppermute(firsts, "space", down),
            )
            prior = from_previous_slice((u4, u4_last, u4_first))
    return outs[0][None]


def solution(mesh):
    placed = (
        P("tm", None, "space", None, None),
        P(None, "space", None, None),
        P(None, "space", None, None),
        P(),
    )
    return jax.shard_map(
        per_device,
        mesh=mesh,
        in_specs=placed,
        out_specs=P("tm", None, "space", None, None),
        check_vma=False,
    )
```

```python
import functools
import math

import jax
import jax.numpy as jnp
from jax import lax
from jax.experimental import pallas as pl
from jax.experimental.pallas import tpu as pltpu
from jax.sharding import PartitionSpec as P

ROUNDS = 3

START_HALO = 5

step_length = 0.5


def lagrange_integral(nodes, j, upper_end):
    coeffs = [1.0]
    scale_down = 1.0
    for i in range(len(nodes)):
        if i != j:
            grown = [0.0] * (len(coeffs) + 1)
            for p in range(len(coeffs)):
                grown[p + 1] = grown[p + 1] + coeffs[p]
                grown[p] = grown[p] - nodes[i] * coeffs[p]
            coeffs = grown
            scale_down = scale_down * (nodes[j] - nodes[i])
    summed_up = 0.0
    for p in range(len(coeffs)):
        summed_up = summed_up + coeffs[p] * upper_end ** (p + 1) / (p + 1)
    return summed_up / scale_down


def node_tables():
    radical = math.sqrt(3.0 / 7.0)
    fine_nodes = [0.0, 0.5 * (1.0 - radical), 0.5, 0.5 * (1.0 + radical), 1.0]
    coarse_nodes = [0.0, 0.5, 1.0]
    integrals = [
        [lagrange_integral(fine_nodes, j, fine_nodes[m]) for j in range(5)] for m in range(5)
    ]
    spread_table = [
        [float(step_length * (integrals[m + 1][j] - integrals[m][j])) for j in range(5)]
        for m in range(4)
    ]
    grouped_table = [
        [spread_table[2 * c][j] + spread_table[2 * c + 1][j] for j in range(5)] for c in range(2)
    ]
    interp_table = []
    for m in range(5):
        weights_row = []
        for k in range(3):
            factor = 1.0
            for i in range(3):
                if i != k:
                    factor = (
                        factor
                        * (fine_nodes[m] - coarse_nodes[i])
                        / (coarse_nodes[k] - coarse_nodes[i])
                    )
            weights_row.append(factor)
        interp_table.append(weights_row)
    widths = [step_length * (fine_nodes[m + 1] - fine_nodes[m]) for m in range(4)]
    return (spread_table, grouped_table, interp_table, widths)


def to_even_odd(a):
    return jnp.concatenate([a[..., 0::2, :], a[..., 1::2, :]], axis=-2)


def from_even_odd(a):
    half = a.shape[-2] // 2
    woven = jnp.stack([a[..., :half, :], a[..., half:, :]], axis=-2)
    return woven.reshape(a.shape)


def crop(field, h):
    a, have = field
    d = have - h
    assert d >= 0
    if d == 0:
        return a
    return lax.slice_in_dim(a, d, a.shape[-3] - d, axis=a.ndim - 3)


def space_halo(a, h):
    if h == 0:
        return a
    size = lax.axis_size("space")
    rows = a.shape[-3]
    assert h <= rows
    up = [(i, (i + 1) % size) for i in range(size)]
    down = [((i + 1) % size, i) for i in range(size)]
    before = lax.ppermute(lax.slice_in_dim(a, rows - h, rows, axis=a.ndim - 3), "space", up)
    after = lax.ppermute(lax.slice_in_dim(a, 0, h, axis=a.ndim - 3), "space", down)
    return jnp.concatenate([before, a, after], axis=a.ndim - 3)


def from_previous_slice(pieces):
    slices = lax.axis_size("tm")
    size = lax.axis_size("space")
    axes = ("tm", "space")

    def moved(piece, shift):
        pairs = [
            (t * size + s, (t + 1) * size + (s + shift) % size)
            for t in range(slices - 1)
            for s in range(size)
        ]
        return lax.ppermute(piece, axes, pairs)

    own, lasts, firsts = pieces
    return moved(own, 0), moved(lasts, 1), moved(firsts, -1)


def react_terms(field, laplace, diffusivity, source):
    first_part = field[0]
    second_part = field[1]
    product = first_part * second_part * second_part
    return jnp.stack(
        [
            diffusivity[0] * laplace[0] - product + source[0],
            diffusivity[1] * laplace[1] + product + source[1],
        ],
        axis=0,
    )


def fine_laplace(a):
    centre = a[..., 1:-1, :, :]
    pair_x = a[..., 2:, :, :] + a[..., :-2, :, :]
    half = centre.shape[-2] // 2
    even = centre[..., :half, :]
    odd = centre[..., half:, :]
    pair_y = jnp.concatenate(
        [odd + jnp.roll(odd, 1, -2), jnp.roll(even, -1, -2) + even], axis=-2
    )
    pair_z = jnp.roll(centre, -1, -1) + jnp.roll(centre, 1, -1)
    return pair_x + pair_y + pair_z - 6.0 * centre


def coarse_laplace(a):
    centre = a[..., 1:-1, :, :]
    pair_x = a[..., 2:, :, :] + a[..., :-2, :, :]
    pair_y = jnp.roll(centre, -1, -2) + jnp.roll(centre, 1, -2)
    pair_z = jnp.roll(centre, -1, -1) + jnp.roll(centre, 1, -1)
    return (pair_x - 2.0 * centre) * 0.25 + (pair_y - 2.0 * centre) * 0.25 + (
        pair_z - 2.0 * centre
    )


def restrict(field):
    a, h = field
    h2 = h - h % 2
    a = crop(field, h2)
    rows = a.shape[-3]
    half = a.shape[-2] // 2
    pairs = a.reshape(a.shape[:-3] + (rows // 2, 2) + a.shape[-2:])
    even = pairs[..., :half, :]
    odd = pairs[..., half:, :]
    upper = even[..., 0, :, :] + even[..., 1, :, :]
    lower = odd[..., 0, :, :] + odd[..., 1, :, :]
    return (upper + lower) * 0.25, h2 // 2


def prolong(a):
    rows = jnp.repeat(a, 2, axis=a.ndim - 3)
    return jnp.concatenate([rows, rows], axis=-2)


def even_odd_load(ref, index=()):
    view = ref.at[index] if index != () else ref
    lead = (slice(None),) * (len(view.shape) - 2)
    half = view.shape[-2] // 2
    even = view[lead + (pl.ds(0, half, stride=2), slice(None))]
    odd = view[lead + (pl.ds(1, half, stride=2), slice(None))]
    return jnp.concatenate([even, odd], axis=-2)


def kernel_laplace(f):
    centre = f[:, 1:-1]
    pair_x = f[:, 2:] + f[:, :-2]
    half = centre.shape[2] // 2
    even = centre[:, :, :half]
    odd = centre[:, :, half:]
    pair_y = jnp.concatenate(
        [odd + pltpu.roll(odd, 1, 2), pltpu.roll(even, half - 1, 2) + even], axis=2
    )
    lanes = centre.shape[3]
    pair_z = pltpu.roll(centre, lanes - 1, 3) + pltpu.roll(centre, 1, 3)
    return pair_x + pair_y + pair_z - 6.0 * centre


def kernel_restrict(v):
    shape = v.shape
    pairs = v.reshape((shape[0], shape[1] // 2, 2) + shape[2:])
    half = shape[2] // 2
    even = pairs[:, :, :, :half]
    odd = pairs[:, :, :, half:]
    upper = even[:, :, 0] + even[:, :, 1]
    lower = odd[:, :, 0] + odd[:, :, 1]
    return (upper + lower) * 0.25


def sweep_kernel(widths_sent, natural_prior, diff_ref, flag_ref, start_ref, centre_ref, bbefore_ref, bafter_ref,
                 own_ref, before_ref, after_ref, dec_ref, src_ref,
                 rate_ref, n1_ref, n2_ref, n3_ref, n4_ref, e0_ref, b0_ref, cown_ref, clasts_ref,
                 cfirsts_ref):
    spread_table, grouped_table, interp_table, widths = node_tables()
    rows = e0_ref.shape[1]
    hs = (start_ref.shape[1] - rows) // 2
    hd = (dec_ref.shape[1] - rows) // 2
    d0 = diff_ref[0]
    d1 = diff_ref[1]

    def at(ref, h):
        off = hd - h
        return ref[:, off:off + rows + 2 * h]

    def cut(v, have, h):
        d = have - h
        return v[:, d:v.shape[1] - d]

    def terms(f, h):
        laplace = kernel_laplace(f)
        centre = f[:, 1:-1]
        s = at(src_ref, h - 1)
        product = centre[0] * centre[1] * centre[1]
        return jnp.stack([d0 * laplace[0] - product + s[0], d1 * laplace[1] + product + s[1]])

    parts = []
    offset = 0
    for m in range(4):
        w = hs - 1 - m
        parts.append(
            jnp.concatenate(
                [before_ref[:, offset:offset + w], own_ref[m], after_ref[:, offset:offset + w]],
                axis=1,
            )
        )
        offset += w
    if natural_prior:
        pieces = [even_odd_load(r) for r in (bbefore_ref, centre_ref, bafter_ref)]
    else:
        pieces = [r[...] for r in (bbefore_ref, centre_ref, bafter_ref)]
    joined = jnp.concatenate(pieces, axis=1)
    swept = [jnp.where(flag_ref[0] == 1, start_ref[...], joined)]
    found = []
    for m in range(4):
        have = hs - m
        e = terms(swept[m], have)
        found.append(e)
        h = have - 1
        numerator = (cut(swept[m], have, h) + widths[m] * e) + parts[m]
        swept.append(numerator / (1.0 + widths[m] * at(dec_ref, h)))
    found.append(terms(swept[4], hs - 4))
    dec0 = at(dec_ref, 0)
    fulls = [cut(found[j], hs - 1 - j, 0) - dec0 * cut(swept[j], hs - j, 0) for j in range(5)]
    integrated = []
    for c in range(2):
        summed = grouped_table[c][0] * fulls[0]
        for j in range(1, 5):
            summed = summed + grouped_table[c][j] * fulls[j]
        integrated.append(kernel_restrict(summed))
    crows = rows // 2
    hcr = (rate_ref.shape[1] - crows) // 2
    rc = rate_ref[:, hcr:hcr + crows]
    coarse_vals = [kernel_restrict(cut(swept[j], hs - j, 0)) for j in (0, 2, 4)]
    half_step = 0.5 * step_length
    coarse_one = (
        coarse_vals[0] + half_step * rc * coarse_vals[1] + integrated[0]
    ) / (1.0 + half_step * rc)
    sent = [coarse_one, coarse_vals[1], coarse_vals[2], integrated[1]]
    offset = 0
    for i, piece in enumerate(sent):
        cown_ref[i] = piece
        w = widths_sent[i]
        if w:
            clasts_ref[:, offset:offset + w] = piece[:, crows - w:]
            cfirsts_ref[:, offset:offset + w] = piece[:, :w]
        offset += w
    for m, out in ((1, n1_ref), (2, n2_ref), (3, n3_ref), (4, n4_ref)):
        out[...] = cut(swept[m], hs - m, 1)
    e0_ref[...] = cut(found[0], hs - 1, 0)
    b0_ref[...] = cut(swept[0], hs, 0)


def fine_sweep(diffusivity, flag, start, prior, parts, decay, src, rate_c, widths_sent,
               natural_prior):
    rows = start.shape[1] - 2 * START_HALO
    shape = start.shape
    wide = jax.ShapeDtypeStruct((shape[0], rows + 2) + shape[2:], jnp.float32)
    own = jax.ShapeDtypeStruct((shape[0], rows) + shape[2:], jnp.float32)
    cshape = (shape[0], rows // 2, shape[2] // 2, shape[3])
    cown = jax.ShapeDtypeStruct((4,) + cshape, jnp.float32)
    cedge = jax.ShapeDtypeStruct((shape[0], sum(widths_sent)) + cshape[2:], jnp.float32)
    vmem = pl.BlockSpec(memory_space=pltpu.VMEM)
    return pl.pallas_call(
        functools.partial(sweep_kernel, widths_sent, natural_prior),
        out_shape=(wide, wide, wide, wide, own, own, cown, cedge, cedge),
        in_specs=[pl.BlockSpec(memory_space=pltpu.SMEM)] * 2 + [vmem] * 10,
        out_specs=(vmem,) * 9,
    )(diffusivity, flag, start, *prior, *parts, decay, src, rate_c)


def coarse_kernel_laplace(f):
    centre = f[:, 1:-1]
    pair_x = f[:, 2:] + f[:, :-2]
    ny = centre.shape[2]
    lanes = centre.shape[3]
    pair_y = pltpu.roll(centre, ny - 1, 2) + pltpu.roll(centre, 1, 2)
    pair_z = pltpu.roll(centre, lanes - 1, 3) + pltpu.roll(centre, 1, 3)
    return (pair_x - 2.0 * centre) * 0.25 + (pair_y - 2.0 * centre) * 0.25 + (
        pair_z - 2.0 * centre
    )


def finish_kernel(widths_sent, diff_ref, cown_ref, cbefore_ref, cafter_ref, rate_ref, csrc_ref,
                  n1_ref, n2_ref, n3_ref, n4_ref, b_ref, e0_ref, dec_ref, src_ref, *outs):
    spread_table, grouped_table, interp_table, widths = node_tables()
    last = len(outs) == 1
    rows = e0_ref.shape[1]
    crows = rows // 2
    ho = widths_sent[2]
    joined = []
    offset = 0
    for i in range(4):
        w = widths_sent[i]
        if w:
            joined.append(
                jnp.concatenate(
                    [cbefore_ref[:, offset:offset + w], cown_ref[i], cafter_ref[:, offset:offset + w]],
                    axis=1,
                )
            )
        else:
            joined.append(cown_ref[i])
        offset += w
    one, mid, low, late = joined
    hcr = (rate_ref.shape[1] - crows) // 2
    hd = (dec_ref.shape[1] - rows) // 2
    hs = START_HALO
    d0 = diff_ref[0]
    d1 = diff_ref[1]

    def at(ref, h, size, have):
        off = have - h
        return ref[:, off:off + size + 2 * h]

    def cut(v, have, h):
        d = have - h
        return v[:, d:v.shape[1] - d]

    def react(centre, laplace, s):
        product = centre[0] * centre[1] * centre[1]
        return jnp.stack([d0 * laplace[0] - product + s[0], d1 * laplace[1] + product + s[1]])

    def coarse_terms(v):
        return react(v[:, 1:-1], coarse_kernel_laplace(v), at(csrc_ref, ho, crows, hcr))

    half_step = 0.5 * step_length
    rc = at(rate_ref, ho, crows, hcr)
    coarse_two = (
        cut(one, ho + 1, ho)
        + half_step * (coarse_terms(one) - coarse_terms(mid))
        + half_step * rc * low
        + late
    ) / (1.0 + half_step * rc)
    delta_one = cut(one, ho + 1, ho) - cut(mid, ho + 1, ho)
    delta_two = coarse_two - low

    def prolonged(c):
        shape = c.shape
        doubled = jnp.broadcast_to(c[:, :, None], (shape[0], shape[1], 2) + shape[2:])
        doubled = doubled.reshape((shape[0], 2 * shape[1]) + shape[2:])
        return jnp.concatenate([doubled, doubled], axis=2)

    news = {}
    for m, ref in ((1, n1_ref), (2, n2_ref), (3, n3_ref), (4, n4_ref)):
        if last and m < 4:
            continue
        fine = prolonged(interp_table[m][1] * delta_one + interp_table[m][2] * delta_two)
        news[m] = cut(ref[...], 1, ho) + cut(fine, 2 * ho, ho)
    if last:
        half = news[4].shape[2] // 2
        outs[0][:, :, pl.ds(0, half, stride=2), :] = news[4][:, :, :half]
        outs[0][:, :, pl.ds(1, half, stride=2), :] = news[4][:, :, half:]
        return
    own_out, lasts_out, firsts_out, u4_out, u4_last_out, u4_first_out = outs
    src1 = at(src_ref, 0, rows, hd)
    dec0 = at(dec_ref, 0, rows, hd)
    states = [b_ref[...]] + [cut(news[m], 1, 0) for m in range(1, 5)]
    terms = [e0_ref[...]] + [
        react(cut(news[m], 1, 0), kernel_laplace(news[m]), src1) for m in range(1, 5)
    ]
    fulls = [terms[j] - dec0 * states[j] for j in range(5)]
    offset = 0
    for m in range(4):
        summed = spread_table[m][0] * fulls[0]
        for j in range(1, 5):
            summed = summed + spread_table[m][j] * fulls[j]
        part = (widths[m] * dec0 * states[m + 1] - widths[m] * terms[m]) + summed
        own_out[m] = part
        w = hs - 1 - m
        lasts_out[:, offset:offset + w] = part[:, rows - w:]
        firsts_out[:, offset:offset + w] = part[:, :w]
        offset += w
    u4_out[...] = states[4]
    u4_last_out[...] = states[4][:, rows - hs:]
    u4_first_out[...] = states[4][:, :hs]


def finish_round(diffusivity, coarse, rate_c, source_c, swept, e0, decay, src, last, widths_sent):
    begin = swept[0]
    shape = begin.shape
    rows = e0.shape[1]
    field = jax.ShapeDtypeStruct((shape[0], rows) + shape[2:], jnp.float32)
    if last:
        out_shape = (field,)
    else:
        sent = sum(START_HALO - 1 - m for m in range(4))
        edge = jax.ShapeDtypeStruct((shape[0], sent) + shape[2:], jnp.float32)
        rim = jax.ShapeDtypeStruct((shape[0], START_HALO) + shape[2:], jnp.float32)
        out_shape = (jax.ShapeDtypeStruct((4,) + field.shape, jnp.float32), edge, edge, field, rim, rim)
    vmem = pl.BlockSpec(memory_space=pltpu.VMEM)
    args = (diffusivity, *coarse, rate_c, source_c, *swept[1:], begin, e0, decay, src)
    return pl.pallas_call(
        functools.partial(finish_kernel, widths_sent),
        out_shape=out_shape,
        in_specs=[pl.BlockSpec(memory_space=pltpu.SMEM)] + [vmem] * (len(args) - 1),
        out_specs=(vmem,) * len(out_shape),
    )(*args)


def start_kernel(diff_ref, init_ref, decay_ref, source_ref, got_before_ref, got_after_ref,
                 own_ref, before_ref, after_ref, rate_ref, csrc_ref, ext_ref, dec_ref, src_ref):
    spread_table, grouped_table, interp_table, widths = node_tables()
    rows = own_ref.shape[2]
    hs = (ext_ref.shape[1] - rows) // 2
    hd = hs - 1
    d0 = diff_ref[0]
    d1 = diff_ref[1]

    def joined(ref, offset, w):
        return jnp.concatenate(
            [
                even_odd_load(got_before_ref, (slice(None), pl.ds(offset, w))),
                even_odd_load(ref),
                even_odd_load(got_after_ref, (slice(None), pl.ds(offset, w))),
            ],
            axis=1,
        )

    state = joined(init_ref, 0, hs)
    dec = joined(decay_ref, hs, hd)
    s = joined(source_ref, hs + hd, hd)
    ext_ref[...] = state
    dec_ref[...] = dec
    src_ref[...] = s
    inner = state[:, 1:-1]
    laplace = kernel_laplace(state)
    product = inner[0] * inner[1] * inner[1]
    terms = jnp.stack([d0 * laplace[0] - product + s[0], d1 * laplace[1] + product + s[1]])
    full = terms - dec * inner
    edge = hs - 1
    offset = 0
    for m in range(4):
        weight = sum(spread_table[m][j] for j in range(5))
        part = (widths[m] * dec * inner - widths[m] * terms) + weight * full
        own_ref[m] = part[:, edge:edge + rows]
        w = edge - m
        before_ref[:, offset:offset + w] = part[:, m:edge]
        after_ref[:, offset:offset + w] = part[:, edge + rows:edge + rows + w]
        offset += w
    rate_ref[...] = kernel_restrict(dec)
    csrc_ref[...] = kernel_restrict(s)


def start_terms(diffusivity, own_arrays, got_before, got_after):
    own_shape = own_arrays[0].shape
    rows = own_shape[1]
    shape = (own_shape[0], rows + 2 * START_HALO) + own_shape[2:]
    fixed = jax.ShapeDtypeStruct(
        (own_shape[0], rows + 2 * (START_HALO - 1)) + own_shape[2:], jnp.float32
    )
    sent = sum(START_HALO - 1 - m for m in range(4))
    edge = jax.ShapeDtypeStruct((shape[0], sent) + shape[2:], jnp.float32)
    cshape = (shape[0], (rows + 2 * (START_HALO - 1)) // 2, shape[2] // 2, shape[3])
    coarse = jax.ShapeDtypeStruct(cshape, jnp.float32)
    vmem = pl.BlockSpec(memory_space=pltpu.VMEM)
    return pl.pallas_call(
        start_kernel,
        out_shape=(
            jax.ShapeDtypeStruct((4, shape[0], rows) + shape[2:], jnp.float32),
            edge, edge, coarse, coarse,
            jax.ShapeDtypeStruct(shape, jnp.float32),
            fixed,
            fixed,
        ),
        in_specs=[pl.BlockSpec(memory_space=pltpu.SMEM)] + [vmem] * 5,
        out_specs=(vmem,) * 8,
    )(diffusivity, *own_arrays, got_before, got_after)


def packed_halo(fields):
    size = lax.axis_size("space")
    rows = fields[0][0].shape[-3]
    axis = fields[0][0].ndim - 3
    up = [(i, (i + 1) % size) for i in range(size)]
    down = [((i + 1) % size, i) for i in range(size)]
    lasts = jnp.concatenate(
        [lax.slice_in_dim(a, rows - w, rows, axis=axis) for a, w in fields], axis=axis
    )
    firsts = jnp.concatenate([lax.slice_in_dim(a, 0, w, axis=axis) for a, w in fields], axis=axis)
    before = lax.ppermute(lasts, "space", up)
    after = lax.ppermute(firsts, "space", down)
    out = []
    offset = 0
    for a, w in fields:
        out.append(
            (
                jnp.concatenate(
                    [
                        lax.slice_in_dim(before, offset, offset + w, axis=axis),
                        a,
                        lax.slice_in_dim(after, offset, offset + w, axis=axis),
                    ],
                    axis=axis,
                ),
                w,
            )
        )
        offset += w
    return out


def per_device(initial, decay_rate, source, diffusivity):
    spread_table, grouped_table, interp_table, widths = node_tables()
    first_slice = lax.axis_index("tm") == 0
    hs = START_HALO
    assert hs == 5 and initial.shape[-3] >= hs

    own_start = initial[0]
    size = lax.axis_size("space")
    up = [(i, (i + 1) % size) for i in range(size)]
    down = [((i + 1) % size, i) for i in range(size)]
    rows = own_start.shape[-3]
    widths_in = (hs, hs - 1, hs - 1)
    own_arrays = (own_start, decay_rate, source)
    got_before = lax.ppermute(
        jnp.concatenate([a[:, rows - w:] for a, w in zip(own_arrays, widths_in)], axis=1),
        "space", up,
    )
    got_after = lax.ppermute(
        jnp.concatenate([a[:, :w] for a, w in zip(own_arrays, widths_in)], axis=1),
        "space", down,
    )
    own4, before4, after4, rate_own, csrc_own, own_ext, dec_ext, src_ext = start_terms(
        diffusivity, own_arrays, got_before, got_after
    )
    decay = (dec_ext, hs - 1)
    src = (src_ext, hs - 1)
    rate_c = (rate_own, (hs - 1) // 2)
    source_c = (csrc_own, (hs - 1) // 2)

    def fine_E(field):
        a, h = field
        laplace = fine_laplace(a)
        return react_terms(a[..., 1:-1, :, :], laplace, diffusivity, crop(src, h - 1)), h - 1

    def coarse_E(field):
        a, h = field
        laplace = coarse_laplace(a)
        return react_terms(a[..., 1:-1, :, :], laplace, diffusivity, crop(source_c, h - 1)), h - 1

    def full(field, field_E):
        h = min(field[1], field_E[1])
        return crop(field_E, h) - crop(decay, h) * crop(field, h), h

    def step_terms(states, terms):
        fulls = [full(states[j], terms[j]) for j in range(5)]
        hf = min(f[1] for f in fulls)
        out = []
        for m in range(4):
            h = min(hf, terms[m][1], states[m + 1][1])
            summed = spread_table[m][0] * crop(fulls[0], h)
            for j in range(1, 5):
                summed = summed + spread_table[m][j] * crop(fulls[j], h)
            own = (
                widths[m] * crop(decay, h) * crop(states[m + 1], h)
                - widths[m] * crop(terms[m], h)
            ) + summed
            out.append((own, h))
        return out

    def advance(prior, pieces, last, natural):
        widths_sent = (1, 1, 0, 0) if last else (2, 2, 1, 1)
        n1, n2, n3, n4, e0, b0, cown, clasts, cfirsts = fine_sweep(
            diffusivity, flag, own_ext, prior, pieces, decay[0], src[0], rate_c[0], widths_sent,
            natural,
        )
        coarse = (
            cown,
            lax.ppermute(clasts, "space", up),
            lax.ppermute(cfirsts, "space", down),
        )
        return finish_round(
            diffusivity, coarse, rate_c[0], source_c[0],
            (b0, n1, n2, n3, n4), e0, decay[0], src[0], last, widths_sent,
        )

    size = lax.axis_size("space")
    up = [(i, (i + 1) % size) for i in range(size)]
    down = [((i + 1) % size, i) for i in range(size)]
    rows = own_start.shape[-3]
    flag = jnp.where(first_slice, 1, 0).astype(jnp.int32).reshape(1)
    pieces = (own4, before4, after4)
    prior = from_previous_slice(
        (own_start, own_start[:, rows - hs:], own_start[:, :hs])
    )
    for k in range(ROUNDS):
        last = k + 1 == ROUNDS
        outs = advance(prior, pieces, last, k == 0)
        if not last:
            own4, lasts, firsts, u4, u4_last, u4_first = outs
            pieces = (
                own4,
                lax.ppermute(lasts, "space", up),
                lax.ppermute(firsts, "space", down),
            )
            prior = from_previous_slice((u4, u4_last, u4_first))
    return outs[0][None]


def solution(mesh):
    placed = (
        P("tm", None, "space", None, None),
        P(None, "space", None, None),
        P(None, "space", None, None),
        P(),
    )
    return jax.shard_map(
        per_device,
        mesh=mesh,
        in_specs=placed,
        out_specs=P("tm", None, "space", None, None),
        check_vma=False,
    )
```

```python
import functools
import math

import jax
import jax.numpy as jnp
from jax import lax
from jax.experimental import pallas as pl
from jax.experimental.pallas import tpu as pltpu
from jax.sharding import PartitionSpec as P

ROUNDS = 3

START_HALO = 5

step_length = 0.5


def lagrange_integral(nodes, j, upper_end):
    coeffs = [1.0]
    scale_down = 1.0
    for i in range(len(nodes)):
        if i != j:
            grown = [0.0] * (len(coeffs) + 1)
            for p in range(len(coeffs)):
                grown[p + 1] = grown[p + 1] + coeffs[p]
                grown[p] = grown[p] - nodes[i] * coeffs[p]
            coeffs = grown
            scale_down = scale_down * (nodes[j] - nodes[i])
    summed_up = 0.0
    for p in range(len(coeffs)):
        summed_up = summed_up + coeffs[p] * upper_end ** (p + 1) / (p + 1)
    return summed_up / scale_down


def node_tables():
    radical = math.sqrt(3.0 / 7.0)
    fine_nodes = [0.0, 0.5 * (1.0 - radical), 0.5, 0.5 * (1.0 + radical), 1.0]
    coarse_nodes = [0.0, 0.5, 1.0]
    integrals = [
        [lagrange_integral(fine_nodes, j, fine_nodes[m]) for j in range(5)] for m in range(5)
    ]
    spread_table = [
        [float(step_length * (integrals[m + 1][j] - integrals[m][j])) for j in range(5)]
        for m in range(4)
    ]
    grouped_table = [
        [spread_table[2 * c][j] + spread_table[2 * c + 1][j] for j in range(5)] for c in range(2)
    ]
    interp_table = []
    for m in range(5):
        weights_row = []
        for k in range(3):
            factor = 1.0
            for i in range(3):
                if i != k:
                    factor = (
                        factor
                        * (fine_nodes[m] - coarse_nodes[i])
                        / (coarse_nodes[k] - coarse_nodes[i])
                    )
            weights_row.append(factor)
        interp_table.append(weights_row)
    widths = [step_length * (fine_nodes[m + 1] - fine_nodes[m]) for m in range(4)]
    return (spread_table, grouped_table, interp_table, widths)


def to_even_odd(a):
    return jnp.concatenate([a[..., 0::2, :], a[..., 1::2, :]], axis=-2)


def from_even_odd(a):
    half = a.shape[-2] // 2
    woven = jnp.stack([a[..., :half, :], a[..., half:, :]], axis=-2)
    return woven.reshape(a.shape)


def crop(field, h):
    a, have = field
    d = have - h
    assert d >= 0
    if d == 0:
        return a
    return lax.slice_in_dim(a, d, a.shape[-3] - d, axis=a.ndim - 3)


def space_halo(a, h):
    if h == 0:
        return a
    size = lax.axis_size("space")
    rows = a.shape[-3]
    assert h <= rows
    up = [(i, (i + 1) % size) for i in range(size)]
    down = [((i + 1) % size, i) for i in range(size)]
    before = lax.ppermute(lax.slice_in_dim(a, rows - h, rows, axis=a.ndim - 3), "space", up)
    after = lax.ppermute(lax.slice_in_dim(a, 0, h, axis=a.ndim - 3), "space", down)
    return jnp.concatenate([before, a, after], axis=a.ndim - 3)


def from_previous_slice(pieces):
    slices = lax.axis_size("tm")
    size = lax.axis_size("space")
    axes = ("tm", "space")

    def moved(piece, shift):
        pairs = [
            (t * size + s, (t + 1) * size + (s + shift) % size)
            for t in range(slices - 1)
            for s in range(size)
        ]
        return lax.ppermute(piece, axes, pairs)

    own, lasts, firsts = pieces
    return moved(own, 0), moved(lasts, 1), moved(firsts, -1)


def react_terms(field, laplace, diffusivity, source):
    first_part = field[0]
    second_part = field[1]
    product = first_part * second_part * second_part
    return jnp.stack(
        [
            diffusivity[0] * laplace[0] - product + source[0],
            diffusivity[1] * laplace[1] + product + source[1],
        ],
        axis=0,
    )


def fine_laplace(a):
    centre = a[..., 1:-1, :, :]
    pair_x = a[..., 2:, :, :] + a[..., :-2, :, :]
    half = centre.shape[-2] // 2
    even = centre[..., :half, :]
    odd = centre[..., half:, :]
    pair_y = jnp.concatenate(
        [odd + jnp.roll(odd, 1, -2), jnp.roll(even, -1, -2) + even], axis=-2
    )
    pair_z = jnp.roll(centre, -1, -1) + jnp.roll(centre, 1, -1)
    return pair_x + pair_y + pair_z - 6.0 * centre


def coarse_laplace(a):
    centre = a[..., 1:-1, :, :]
    pair_x = a[..., 2:, :, :] + a[..., :-2, :, :]
    pair_y = jnp.roll(centre, -1, -2) + jnp.roll(centre, 1, -2)
    pair_z = jnp.roll(centre, -1, -1) + jnp.roll(centre, 1, -1)
    return (pair_x - 2.0 * centre) * 0.25 + (pair_y - 2.0 * centre) * 0.25 + (
        pair_z - 2.0 * centre
    )


def restrict(field):
    a, h = field
    h2 = h - h % 2
    a = crop(field, h2)
    rows = a.shape[-3]
    half = a.shape[-2] // 2
    pairs = a.reshape(a.shape[:-3] + (rows // 2, 2) + a.shape[-2:])
    even = pairs[..., :half, :]
    odd = pairs[..., half:, :]
    upper = even[..., 0, :, :] + even[..., 1, :, :]
    lower = odd[..., 0, :, :] + odd[..., 1, :, :]
    return (upper + lower) * 0.25, h2 // 2


def prolong(a):
    rows = jnp.repeat(a, 2, axis=a.ndim - 3)
    return jnp.concatenate([rows, rows], axis=-2)


def even_odd_load(ref, index=()):
    view = ref.at[index] if index != () else ref
    lead = (slice(None),) * (len(view.shape) - 2)
    half = view.shape[-2] // 2
    even = view[lead + (pl.ds(0, half, stride=2), slice(None))]
    odd = view[lead + (pl.ds(1, half, stride=2), slice(None))]
    return jnp.concatenate([even, odd], axis=-2)


def kernel_laplace(f):
    centre = f[:, 1:-1]
    pair_x = f[:, 2:] + f[:, :-2]
    half = centre.shape[2] // 2
    even = centre[:, :, :half]
    odd = centre[:, :, half:]
    pair_y = jnp.concatenate(
        [odd + pltpu.roll(odd, 1, 2), pltpu.roll(even, half - 1, 2) + even], axis=2
    )
    lanes = centre.shape[3]
    pair_z = pltpu.roll(centre, lanes - 1, 3) + pltpu.roll(centre, 1, 3)
    return pair_x + pair_y + pair_z - 6.0 * centre


def kernel_prolong(c):
    shape = c.shape
    doubled = jnp.broadcast_to(c[:, :, None], (shape[0], shape[1], 2) + shape[2:])
    doubled = doubled.reshape((shape[0], 2 * shape[1]) + shape[2:])
    return jnp.concatenate([doubled, doubled], axis=2)


def kernel_restrict(v):
    shape = v.shape
    pairs = v.reshape((shape[0], shape[1] // 2, 2) + shape[2:])
    half = shape[2] // 2
    even = pairs[:, :, :, :half]
    odd = pairs[:, :, :, half:]
    upper = even[:, :, 0] + even[:, :, 1]
    lower = odd[:, :, 0] + odd[:, :, 1]
    return (upper + lower) * 0.25


def sweep_kernel(widths_sent, n_prior, diff_ref, flag_ref, start_ref, *refs):
    prior = refs[:n_prior]
    own_ref, before_ref, after_ref, dec_ref, src_ref, rate_ref = refs[n_prior:n_prior + 6]
    (n1_ref, n2_ref, n3_ref, n4_ref, e0_ref, b0_ref, cown_ref, clasts_ref, cfirsts_ref,
     n4own_ref, n4last_ref, n4first_ref) = refs[n_prior + 6:]
    spread_table, grouped_table, interp_table, widths = node_tables()
    rows = e0_ref.shape[1]
    hs = (start_ref.shape[1] - rows) // 2
    hd = (dec_ref.shape[1] - rows) // 2
    d0 = diff_ref[0]
    d1 = diff_ref[1]

    def at(ref, h):
        off = hd - h
        return ref[:, off:off + rows + 2 * h]

    def cut(v, have, h):
        d = have - h
        return v[:, d:v.shape[1] - d]

    def terms(f, h):
        laplace = kernel_laplace(f)
        centre = f[:, 1:-1]
        s = at(src_ref, h - 1)
        product = centre[0] * centre[1] * centre[1]
        return jnp.stack([d0 * laplace[0] - product + s[0], d1 * laplace[1] + product + s[1]])

    parts = []
    offset = 0
    for m in range(4):
        w = hs - 1 - m
        parts.append(
            jnp.concatenate(
                [before_ref[:, offset:offset + w], own_ref[m], after_ref[:, offset:offset + w]],
                axis=1,
            )
        )
        offset += w
    if n_prior == 3:
        centre_ref, bbefore_ref, bafter_ref = prior
        pieces = [even_odd_load(r) for r in (bbefore_ref, centre_ref, bafter_ref)]
        joined = jnp.concatenate(pieces, axis=1)
    else:
        fc, fb, fa, cc, cb, ca = prior
        fine = jnp.concatenate([fb[...], fc[...], fa[...]], axis=1)
        coarse = jnp.concatenate([cb[...], cc[...], ca[...]], axis=1)
        spare = (2 * coarse.shape[1] - fine.shape[1]) // 2
        joined = fine + cut(kernel_prolong(coarse), hs + spare, hs)
    swept = [jnp.where(flag_ref[0] == 1, start_ref[...], joined)]
    found = []
    for m in range(4):
        have = hs - m
        e = terms(swept[m], have)
        found.append(e)
        h = have - 1
        numerator = (cut(swept[m], have, h) + widths[m] * e) + parts[m]
        swept.append(numerator / (1.0 + widths[m] * at(dec_ref, h)))
    found.append(terms(swept[4], hs - 4))
    dec0 = at(dec_ref, 0)
    fulls = [cut(found[j], hs - 1 - j, 0) - dec0 * cut(swept[j], hs - j, 0) for j in range(5)]
    integrated = []
    for c in range(2):
        summed = grouped_table[c][0] * fulls[0]
        for j in range(1, 5):
            summed = summed + grouped_table[c][j] * fulls[j]
        integrated.append(kernel_restrict(summed))
    crows = rows // 2
    hcr = (rate_ref.shape[1] - crows) // 2
    rc = rate_ref[:, hcr:hcr + crows]
    coarse_vals = [kernel_restrict(cut(swept[j], hs - j, 0)) for j in (0, 2, 4)]
    half_step = 0.5 * step_length
    coarse_one = (
        coarse_vals[0] + half_step * rc * coarse_vals[1] + integrated[0]
    ) / (1.0 + half_step * rc)
    sent = [coarse_one, coarse_vals[1], coarse_vals[2], integrated[1]]
    offset = 0
    for i, piece in enumerate(sent):
        cown_ref[i] = piece
        w = widths_sent[i]
        if w:
            clasts_ref[:, offset:offset + w] = piece[:, crows - w:]
            cfirsts_ref[:, offset:offset + w] = piece[:, :w]
        offset += w
    for m, out in ((1, n1_ref), (2, n2_ref), (3, n3_ref), (4, n4_ref)):
        out[...] = cut(swept[m], hs - m, 1)
    e0_ref[...] = cut(found[0], hs - 1, 0)
    b0_ref[...] = cut(swept[0], hs, 0)
    last_node = cut(swept[4], hs - 4, 0)
    n4own_ref[...] = last_node
    n4last_ref[...] = last_node[:, rows - hs:]
    n4first_ref[...] = last_node[:, :hs]


def fine_sweep(diffusivity, flag, start, prior, parts, decay, src, rate_c, widths_sent):
    rows = start.shape[1] - 2 * START_HALO
    shape = start.shape
    wide = jax.ShapeDtypeStruct((shape[0], rows + 2) + shape[2:], jnp.float32)
    own = jax.ShapeDtypeStruct((shape[0], rows) + shape[2:], jnp.float32)
    cshape = (shape[0], rows // 2, shape[2] // 2, shape[3])
    cown = jax.ShapeDtypeStruct((4,) + cshape, jnp.float32)
    cedge = jax.ShapeDtypeStruct((shape[0], sum(widths_sent)) + cshape[2:], jnp.float32)
    rim = jax.ShapeDtypeStruct((shape[0], START_HALO) + shape[2:], jnp.float32)
    vmem = pl.BlockSpec(memory_space=pltpu.VMEM)
    return pl.pallas_call(
        functools.partial(sweep_kernel, widths_sent, len(prior)),
        out_shape=(wide, wide, wide, wide, own, own, cown, cedge, cedge, own, rim, rim),
        in_specs=[pl.BlockSpec(memory_space=pltpu.SMEM)] * 2 + [vmem] * (7 + len(prior)),
        out_specs=(vmem,) * 12,
    )(diffusivity, flag, start, *prior, *parts, decay, src, rate_c)


def coarse_kernel_laplace(f):
    centre = f[:, 1:-1]
    pair_x = f[:, 2:] + f[:, :-2]
    ny = centre.shape[2]
    lanes = centre.shape[3]
    pair_y = pltpu.roll(centre, ny - 1, 2) + pltpu.roll(centre, 1, 2)
    pair_z = pltpu.roll(centre, lanes - 1, 3) + pltpu.roll(centre, 1, 3)
    return (pair_x - 2.0 * centre) * 0.25 + (pair_y - 2.0 * centre) * 0.25 + (
        pair_z - 2.0 * centre
    )


def finish_kernel(widths_sent, diff_ref, cown_ref, cbefore_ref, cafter_ref, rate_ref, csrc_ref,
                  n1_ref, n2_ref, n3_ref, n4_ref, b_ref, e0_ref, dec_ref, src_ref, *outs):
    spread_table, grouped_table, interp_table, widths = node_tables()
    last = len(outs) == 1
    rows = e0_ref.shape[1]
    crows = rows // 2
    ho = widths_sent[2]
    joined = []
    offset = 0
    for i in range(4):
        w = widths_sent[i]
        if w:
            joined.append(
                jnp.concatenate(
                    [cbefore_ref[:, offset:offset + w], cown_ref[i], cafter_ref[:, offset:offset + w]],
                    axis=1,
                )
            )
        else:
            joined.append(cown_ref[i])
        offset += w
    one, mid, low, late = joined
    hcr = (rate_ref.shape[1] - crows) // 2
    hd = (dec_ref.shape[1] - rows) // 2
    hs = START_HALO
    d0 = diff_ref[0]
    d1 = diff_ref[1]

    def at(ref, h, size, have):
        off = have - h
        return ref[:, off:off + size + 2 * h]

    def cut(v, have, h):
        d = have - h
        return v[:, d:v.shape[1] - d]

    def react(centre, laplace, s):
        product = centre[0] * centre[1] * centre[1]
        return jnp.stack([d0 * laplace[0] - product + s[0], d1 * laplace[1] + product + s[1]])

    def coarse_terms(v):
        return react(v[:, 1:-1], coarse_kernel_laplace(v), at(csrc_ref, ho, crows, hcr))

    half_step = 0.5 * step_length
    rc = at(rate_ref, ho, crows, hcr)
    coarse_two = (
        cut(one, ho + 1, ho)
        + half_step * (coarse_terms(one) - coarse_terms(mid))
        + half_step * rc * low
        + late
    ) / (1.0 + half_step * rc)
    delta_one = cut(one, ho + 1, ho) - cut(mid, ho + 1, ho)
    delta_two = coarse_two - low

    def prolonged(c):
        shape = c.shape
        doubled = jnp.broadcast_to(c[:, :, None], (shape[0], shape[1], 2) + shape[2:])
        doubled = doubled.reshape((shape[0], 2 * shape[1]) + shape[2:])
        return jnp.concatenate([doubled, doubled], axis=2)

    news = {}
    for m, ref in ((1, n1_ref), (2, n2_ref), (3, n3_ref), (4, n4_ref)):
        if last and m < 4:
            continue
        fine = prolonged(interp_table[m][1] * delta_one + interp_table[m][2] * delta_two)
        news[m] = cut(ref[...], 1, ho) + cut(fine, 2 * ho, ho)
    if last:
        half = news[4].shape[2] // 2
        outs[0][:, :, pl.ds(0, half, stride=2), :] = news[4][:, :, :half]
        outs[0][:, :, pl.ds(1, half, stride=2), :] = news[4][:, :, half:]
        return
    own_out, lasts_out, firsts_out, c4_out, c4_last_out, c4_first_out = outs
    src1 = at(src_ref, 0, rows, hd)
    dec0 = at(dec_ref, 0, rows, hd)
    states = [b_ref[...]] + [cut(news[m], 1, 0) for m in range(1, 5)]
    terms = [e0_ref[...]] + [
        react(cut(news[m], 1, 0), kernel_laplace(news[m]), src1) for m in range(1, 5)
    ]
    fulls = [terms[j] - dec0 * states[j] for j in range(5)]
    offset = 0
    for m in range(4):
        summed = spread_table[m][0] * fulls[0]
        for j in range(1, 5):
            summed = summed + spread_table[m][j] * fulls[j]
        part = (widths[m] * dec0 * states[m + 1] - widths[m] * terms[m]) + summed
        own_out[m] = part
        w = hs - 1 - m
        lasts_out[:, offset:offset + w] = part[:, rows - w:]
        firsts_out[:, offset:offset + w] = part[:, :w]
        offset += w
    c4 = cut(interp_table[4][1] * delta_one + interp_table[4][2] * delta_two, ho, 0)
    ch = (hs + 1) // 2
    c4_out[...] = c4
    c4_last_out[...] = c4[:, crows - ch:]
    c4_first_out[...] = c4[:, :ch]


def finish_round(diffusivity, coarse, rate_c, source_c, swept, e0, decay, src, last, widths_sent):
    begin = swept[0]
    shape = begin.shape
    rows = e0.shape[1]
    field = jax.ShapeDtypeStruct((shape[0], rows) + shape[2:], jnp.float32)
    if last:
        out_shape = (field,)
    else:
        sent = sum(START_HALO - 1 - m for m in range(4))
        edge = jax.ShapeDtypeStruct((shape[0], sent) + shape[2:], jnp.float32)
        cshape = (shape[0], rows // 2, shape[2] // 2, shape[3])
        crim = jax.ShapeDtypeStruct((shape[0], (START_HALO + 1) // 2) + cshape[2:], jnp.float32)
        out_shape = (
            jax.ShapeDtypeStruct((4,) + field.shape, jnp.float32), edge, edge,
            jax.ShapeDtypeStruct(cshape, jnp.float32), crim, crim,
        )
    vmem = pl.BlockSpec(memory_space=pltpu.VMEM)
    args = (diffusivity, *coarse, rate_c, source_c, *swept[1:], begin, e0, decay, src)
    return pl.pallas_call(
        functools.partial(finish_kernel, widths_sent),
        out_shape=out_shape,
        in_specs=[pl.BlockSpec(memory_space=pltpu.SMEM)] + [vmem] * (len(args) - 1),
        out_specs=(vmem,) * len(out_shape),
    )(*args)


def start_kernel(diff_ref, init_ref, decay_ref, source_ref, got_before_ref, got_after_ref,
                 own_ref, before_ref, after_ref, rate_ref, csrc_ref, ext_ref, dec_ref, src_ref):
    spread_table, grouped_table, interp_table, widths = node_tables()
    rows = own_ref.shape[2]
    hs = (ext_ref.shape[1] - rows) // 2
    hd = hs - 1
    d0 = diff_ref[0]
    d1 = diff_ref[1]

    def joined(ref, offset, w):
        return jnp.concatenate(
            [
                even_odd_load(got_before_ref, (slice(None), pl.ds(offset, w))),
                even_odd_load(ref),
                even_odd_load(got_after_ref, (slice(None), pl.ds(offset, w))),
            ],
            axis=1,
        )

    state = joined(init_ref, 0, hs)
    dec = joined(decay_ref, hs, hd)
    s = joined(source_ref, hs + hd, hd)
    ext_ref[...] = state
    dec_ref[...] = dec
    src_ref[...] = s
    inner = state[:, 1:-1]
    laplace = kernel_laplace(state)
    product = inner[0] * inner[1] * inner[1]
    terms = jnp.stack([d0 * laplace[0] - product + s[0], d1 * laplace[1] + product + s[1]])
    full = terms - dec * inner
    edge = hs - 1
    offset = 0
    for m in range(4):
        weight = sum(spread_table[m][j] for j in range(5))
        part = (widths[m] * dec * inner - widths[m] * terms) + weight * full
        own_ref[m] = part[:, edge:edge + rows]
        w = edge - m
        before_ref[:, offset:offset + w] = part[:, m:edge]
        after_ref[:, offset:offset + w] = part[:, edge + rows:edge + rows + w]
        offset += w
    rate_ref[...] = kernel_restrict(dec)
    csrc_ref[...] = kernel_restrict(s)


def start_terms(diffusivity, own_arrays, got_before, got_after):
    own_shape = own_arrays[0].shape
    rows = own_shape[1]
    shape = (own_shape[0], rows + 2 * START_HALO) + own_shape[2:]
    fixed = jax.ShapeDtypeStruct(
        (own_shape[0], rows + 2 * (START_HALO - 1)) + own_shape[2:], jnp.float32
    )
    sent = sum(START_HALO - 1 - m for m in range(4))
    edge = jax.ShapeDtypeStruct((shape[0], sent) + shape[2:], jnp.float32)
    cshape = (shape[0], (rows + 2 * (START_HALO - 1)) // 2, shape[2] // 2, shape[3])
    coarse = jax.ShapeDtypeStruct(cshape, jnp.float32)
    vmem = pl.BlockSpec(memory_space=pltpu.VMEM)
    return pl.pallas_call(
        start_kernel,
        out_shape=(
            jax.ShapeDtypeStruct((4, shape[0], rows) + shape[2:], jnp.float32),
            edge, edge, coarse, coarse,
            jax.ShapeDtypeStruct(shape, jnp.float32),
            fixed,
            fixed,
        ),
        in_specs=[pl.BlockSpec(memory_space=pltpu.SMEM)] + [vmem] * 5,
        out_specs=(vmem,) * 8,
    )(diffusivity, *own_arrays, got_before, got_after)


def packed_halo(fields):
    size = lax.axis_size("space")
    rows = fields[0][0].shape[-3]
    axis = fields[0][0].ndim - 3
    up = [(i, (i + 1) % size) for i in range(size)]
    down = [((i + 1) % size, i) for i in range(size)]
    lasts = jnp.concatenate(
        [lax.slice_in_dim(a, rows - w, rows, axis=axis) for a, w in fields], axis=axis
    )
    firsts = jnp.concatenate([lax.slice_in_dim(a, 0, w, axis=axis) for a, w in fields], axis=axis)
    before = lax.ppermute(lasts, "space", up)
    after = lax.ppermute(firsts, "space", down)
    out = []
    offset = 0
    for a, w in fields:
        out.append(
            (
                jnp.concatenate(
                    [
                        lax.slice_in_dim(before, offset, offset + w, axis=axis),
                        a,
                        lax.slice_in_dim(after, offset, offset + w, axis=axis),
                    ],
                    axis=axis,
                ),
                w,
            )
        )
        offset += w
    return out


def per_device(initial, decay_rate, source, diffusivity):
    spread_table, grouped_table, interp_table, widths = node_tables()
    first_slice = lax.axis_index("tm") == 0
    hs = START_HALO
    assert hs == 5 and initial.shape[-3] >= hs

    own_start = initial[0]
    size = lax.axis_size("space")
    up = [(i, (i + 1) % size) for i in range(size)]
    down = [((i + 1) % size, i) for i in range(size)]
    rows = own_start.shape[-3]
    widths_in = (hs, hs - 1, hs - 1)
    own_arrays = (own_start, decay_rate, source)
    got_before = lax.ppermute(
        jnp.concatenate([a[:, rows - w:] for a, w in zip(own_arrays, widths_in)], axis=1),
        "space", up,
    )
    got_after = lax.ppermute(
        jnp.concatenate([a[:, :w] for a, w in zip(own_arrays, widths_in)], axis=1),
        "space", down,
    )
    own4, before4, after4, rate_own, csrc_own, own_ext, dec_ext, src_ext = start_terms(
        diffusivity, own_arrays, got_before, got_after
    )
    decay = (dec_ext, hs - 1)
    src = (src_ext, hs - 1)
    rate_c = (rate_own, (hs - 1) // 2)
    source_c = (csrc_own, (hs - 1) // 2)

    def fine_E(field):
        a, h = field
        laplace = fine_laplace(a)
        return react_terms(a[..., 1:-1, :, :], laplace, diffusivity, crop(src, h - 1)), h - 1

    def coarse_E(field):
        a, h = field
        laplace = coarse_laplace(a)
        return react_terms(a[..., 1:-1, :, :], laplace, diffusivity, crop(source_c, h - 1)), h - 1

    def full(field, field_E):
        h = min(field[1], field_E[1])
        return crop(field_E, h) - crop(decay, h) * crop(field, h), h

    def step_terms(states, terms):
        fulls = [full(states[j], terms[j]) for j in range(5)]
        hf = min(f[1] for f in fulls)
        out = []
        for m in range(4):
            h = min(hf, terms[m][1], states[m + 1][1])
            summed = spread_table[m][0] * crop(fulls[0], h)
            for j in range(1, 5):
                summed = summed + spread_table[m][j] * crop(fulls[j], h)
            own = (
                widths[m] * crop(decay, h) * crop(states[m + 1], h)
                - widths[m] * crop(terms[m], h)
            ) + summed
            out.append((own, h))
        return out

    def advance(prior, pieces, last):
        widths_sent = (1, 1, 0, 0) if last else (2, 2, 1, 1)
        (n1, n2, n3, n4, e0, b0, cown, clasts, cfirsts,
         n4own, n4last, n4first) = fine_sweep(
            diffusivity, flag, own_ext, prior, pieces, decay[0], src[0], rate_c[0], widths_sent,
        )
        sent_node = None if last else from_previous_slice((n4own, n4last, n4first))
        coarse = (
            cown,
            lax.ppermute(clasts, "space", up),
            lax.ppermute(cfirsts, "space", down),
        )
        return finish_round(
            diffusivity, coarse, rate_c[0], source_c[0],
            (b0, n1, n2, n3, n4), e0, decay[0], src[0], last, widths_sent,
        ), sent_node

    size = lax.axis_size("space")
    up = [(i, (i + 1) % size) for i in range(size)]
    down = [((i + 1) % size, i) for i in range(size)]
    rows = own_start.shape[-3]
    flag = jnp.where(first_slice, 1, 0).astype(jnp.int32).reshape(1)
    pieces = (own4, before4, after4)
    prior = from_previous_slice(
        (own_start, own_start[:, rows - hs:], own_start[:, :hs])
    )
    for k in range(ROUNDS):
        last = k + 1 == ROUNDS
        outs, sent_node = advance(prior, pieces, last)
        if not last:
            own4, lasts, firsts, c4, c4_last, c4_first = outs
            pieces = (
                own4,
                lax.ppermute(lasts, "space", up),
                lax.ppermute(firsts, "space", down),
            )
            prior = sent_node + from_previous_slice((c4, c4_last, c4_first))
    return outs[0][None]


def solution(mesh):
    placed = (
        P("tm", None, "space", None, None),
        P(None, "space", None, None),
        P(None, "space", None, None),
        P(),
    )
    return jax.shard_map(
        per_device,
        mesh=mesh,
        in_specs=placed,
        out_specs=P("tm", None, "space", None, None),
        check_vma=False,
    )
```

```python
import functools
import math

import jax
import jax.numpy as jnp
from jax import lax
from jax.experimental import pallas as pl
from jax.experimental.pallas import tpu as pltpu
from jax.sharding import PartitionSpec as P

ROUNDS = 3

START_HALO = 5

step_length = 0.5


def lagrange_integral(nodes, j, upper_end):
    coeffs = [1.0]
    scale_down = 1.0
    for i in range(len(nodes)):
        if i != j:
            grown = [0.0] * (len(coeffs) + 1)
            for p in range(len(coeffs)):
                grown[p + 1] = grown[p + 1] + coeffs[p]
                grown[p] = grown[p] - nodes[i] * coeffs[p]
            coeffs = grown
            scale_down = scale_down * (nodes[j] - nodes[i])
    summed_up = 0.0
    for p in range(len(coeffs)):
        summed_up = summed_up + coeffs[p] * upper_end ** (p + 1) / (p + 1)
    return summed_up / scale_down


def node_tables():
    radical = math.sqrt(3.0 / 7.0)
    fine_nodes = [0.0, 0.5 * (1.0 - radical), 0.5, 0.5 * (1.0 + radical), 1.0]
    coarse_nodes = [0.0, 0.5, 1.0]
    integrals = [
        [lagrange_integral(fine_nodes, j, fine_nodes[m]) for j in range(5)] for m in range(5)
    ]
    spread_table = [
        [float(step_length * (integrals[m + 1][j] - integrals[m][j])) for j in range(5)]
        for m in range(4)
    ]
    grouped_table = [
        [spread_table[2 * c][j] + spread_table[2 * c + 1][j] for j in range(5)] for c in range(2)
    ]
    interp_table = []
    for m in range(5):
        weights_row = []
        for k in range(3):
            factor = 1.0
            for i in range(3):
                if i != k:
                    factor = (
                        factor
                        * (fine_nodes[m] - coarse_nodes[i])
                        / (coarse_nodes[k] - coarse_nodes[i])
                    )
            weights_row.append(factor)
        interp_table.append(weights_row)
    widths = [step_length * (fine_nodes[m + 1] - fine_nodes[m]) for m in range(4)]
    return (spread_table, grouped_table, interp_table, widths)


def to_even_odd(a):
    return jnp.concatenate([a[..., 0::2, :], a[..., 1::2, :]], axis=-2)


def from_even_odd(a):
    half = a.shape[-2] // 2
    woven = jnp.stack([a[..., :half, :], a[..., half:, :]], axis=-2)
    return woven.reshape(a.shape)


def crop(field, h):
    a, have = field
    d = have - h
    assert d >= 0
    if d == 0:
        return a
    return lax.slice_in_dim(a, d, a.shape[-3] - d, axis=a.ndim - 3)


def space_halo(a, h):
    if h == 0:
        return a
    size = lax.axis_size("space")
    rows = a.shape[-3]
    assert h <= rows
    up = [(i, (i + 1) % size) for i in range(size)]
    down = [((i + 1) % size, i) for i in range(size)]
    before = lax.ppermute(lax.slice_in_dim(a, rows - h, rows, axis=a.ndim - 3), "space", up)
    after = lax.ppermute(lax.slice_in_dim(a, 0, h, axis=a.ndim - 3), "space", down)
    return jnp.concatenate([before, a, after], axis=a.ndim - 3)


def from_previous_slice(pieces):
    slices = lax.axis_size("tm")
    size = lax.axis_size("space")
    axes = ("tm", "space")

    def moved(piece, shift):
        pairs = [
            (t * size + s, (t + 1) * size + (s + shift) % size)
            for t in range(slices - 1)
            for s in range(size)
        ]
        return lax.ppermute(piece, axes, pairs)

    own, lasts, firsts = pieces
    return moved(own, 0), moved(lasts, 1), moved(firsts, -1)


def react_terms(field, laplace, diffusivity, source):
    first_part = field[0]
    second_part = field[1]
    product = first_part * second_part * second_part
    return jnp.stack(
        [
            diffusivity[0] * laplace[0] - product + source[0],
            diffusivity[1] * laplace[1] + product + source[1],
        ],
        axis=0,
    )


def fine_laplace(a):
    centre = a[..., 1:-1, :, :]
    pair_x = a[..., 2:, :, :] + a[..., :-2, :, :]
    half = centre.shape[-2] // 2
    even = centre[..., :half, :]
    odd = centre[..., half:, :]
    pair_y = jnp.concatenate(
        [odd + jnp.roll(odd, 1, -2), jnp.roll(even, -1, -2) + even], axis=-2
    )
    pair_z = jnp.roll(centre, -1, -1) + jnp.roll(centre, 1, -1)
    return pair_x + pair_y + pair_z - 6.0 * centre


def coarse_laplace(a):
    centre = a[..., 1:-1, :, :]
    pair_x = a[..., 2:, :, :] + a[..., :-2, :, :]
    pair_y = jnp.roll(centre, -1, -2) + jnp.roll(centre, 1, -2)
    pair_z = jnp.roll(centre, -1, -1) + jnp.roll(centre, 1, -1)
    return (pair_x - 2.0 * centre) * 0.25 + (pair_y - 2.0 * centre) * 0.25 + (
        pair_z - 2.0 * centre
    )


def restrict(field):
    a, h = field
    h2 = h - h % 2
    a = crop(field, h2)
    rows = a.shape[-3]
    half = a.shape[-2] // 2
    pairs = a.reshape(a.shape[:-3] + (rows // 2, 2) + a.shape[-2:])
    even = pairs[..., :half, :]
    odd = pairs[..., half:, :]
    upper = even[..., 0, :, :] + even[..., 1, :, :]
    lower = odd[..., 0, :, :] + odd[..., 1, :, :]
    return (upper + lower) * 0.25, h2 // 2


def prolong(a):
    rows = jnp.repeat(a, 2, axis=a.ndim - 3)
    return jnp.concatenate([rows, rows], axis=-2)


def even_odd_load(ref, index=()):
    view = ref.at[index] if index != () else ref
    lead = (slice(None),) * (len(view.shape) - 2)
    half = view.shape[-2] // 2
    even = view[lead + (pl.ds(0, half, stride=2), slice(None))]
    odd = view[lead + (pl.ds(1, half, stride=2), slice(None))]
    return jnp.concatenate([even, odd], axis=-2)


def kernel_laplace(f):
    centre = f[:, 1:-1]
    pair_x = f[:, 2:] + f[:, :-2]
    half = centre.shape[2] // 2
    even = centre[:, :, :half]
    odd = centre[:, :, half:]
    pair_y = jnp.concatenate(
        [odd + pltpu.roll(odd, 1, 2), pltpu.roll(even, half - 1, 2) + even], axis=2
    )
    lanes = centre.shape[3]
    pair_z = pltpu.roll(centre, lanes - 1, 3) + pltpu.roll(centre, 1, 3)
    return pair_x + pair_y + pair_z - 6.0 * centre


def kernel_prolong(c):
    shape = c.shape
    doubled = jnp.broadcast_to(c[:, :, None], (shape[0], shape[1], 2) + shape[2:])
    doubled = doubled.reshape((shape[0], 2 * shape[1]) + shape[2:])
    return jnp.concatenate([doubled, doubled], axis=2)


def kernel_restrict(v):
    shape = v.shape
    pairs = v.reshape((shape[0], shape[1] // 2, 2) + shape[2:])
    half = shape[2] // 2
    even = pairs[:, :, :, :half]
    odd = pairs[:, :, :, half:]
    upper = even[:, :, 0] + even[:, :, 1]
    lower = odd[:, :, 0] + odd[:, :, 1]
    return (upper + lower) * 0.25


def sweep_kernel(widths_sent, n_prior, diff_ref, flag_ref, start_ref, *refs):
    prior = refs[:n_prior]
    own_ref, before_ref, after_ref, dec_ref, src_ref, rate_ref = refs[n_prior:n_prior + 6]
    (n1_ref, n2_ref, n3_ref, n4_ref, e0_ref, b0_ref, cown_ref, clasts_ref, cfirsts_ref,
     n4own_ref, n4last_ref, n4first_ref) = refs[n_prior + 6:]
    spread_table, grouped_table, interp_table, widths = node_tables()
    rows = e0_ref.shape[1]
    hs = (start_ref.shape[1] - rows) // 2
    hd = (dec_ref.shape[1] - rows) // 2
    d0 = diff_ref[0]
    d1 = diff_ref[1]

    def at(ref, h):
        off = hd - h
        return ref[:, off:off + rows + 2 * h]

    def cut(v, have, h):
        d = have - h
        return v[:, d:v.shape[1] - d]

    def terms(f, h):
        laplace = kernel_laplace(f)
        centre = f[:, 1:-1]
        s = at(src_ref, h - 1)
        product = centre[0] * centre[1] * centre[1]
        return jnp.stack([d0 * laplace[0] - product + s[0], d1 * laplace[1] + product + s[1]])

    parts = []
    offset = 0
    for m in range(4):
        w = hs - 1 - m
        parts.append(
            jnp.concatenate(
                [before_ref[:, offset:offset + w], own_ref[m], after_ref[:, offset:offset + w]],
                axis=1,
            )
        )
        offset += w
    if n_prior == 3:
        centre_ref, bbefore_ref, bafter_ref = prior
        pieces = [even_odd_load(r) for r in (bbefore_ref, centre_ref, bafter_ref)]
        joined = jnp.concatenate(pieces, axis=1)
    else:
        fc, fb, fa, cc, cb, ca = prior
        fine = jnp.concatenate([fb[...], fc[...], fa[...]], axis=1)
        coarse = jnp.concatenate([cb[...], cc[...], ca[...]], axis=1)
        spare = (2 * coarse.shape[1] - fine.shape[1]) // 2
        joined = fine + cut(kernel_prolong(coarse), hs + spare, hs)
    swept = [jnp.where(flag_ref[0] == 1, start_ref[...], joined)]
    found = []
    for m in range(4):
        have = hs - m
        e = terms(swept[m], have)
        found.append(e)
        h = have - 1
        numerator = (cut(swept[m], have, h) + widths[m] * e) + parts[m]
        swept.append(numerator / (1.0 + widths[m] * at(dec_ref, h)))
    found.append(terms(swept[4], hs - 4))
    dec0 = at(dec_ref, 0)
    fulls = [cut(found[j], hs - 1 - j, 0) - dec0 * cut(swept[j], hs - j, 0) for j in range(5)]
    integrated = []
    for c in range(2):
        summed = grouped_table[c][0] * fulls[0]
        for j in range(1, 5):
            summed = summed + grouped_table[c][j] * fulls[j]
        integrated.append(kernel_restrict(summed))
    crows = rows // 2
    hcr = (rate_ref.shape[1] - crows) // 2
    rc = rate_ref[:, hcr:hcr + crows]
    coarse_vals = [kernel_restrict(cut(swept[j], hs - j, 0)) for j in (0, 2, 4)]
    half_step = 0.5 * step_length
    coarse_one = (
        coarse_vals[0] + half_step * rc * coarse_vals[1] + integrated[0]
    ) / (1.0 + half_step * rc)
    sent = [coarse_one, coarse_vals[1], coarse_vals[2], integrated[1]]
    offset = 0
    for i, piece in enumerate(sent):
        cown_ref[i] = piece
        w = widths_sent[i]
        if w:
            clasts_ref[:, offset:offset + w] = piece[:, crows - w:]
            cfirsts_ref[:, offset:offset + w] = piece[:, :w]
        offset += w
    for m, out in ((1, n1_ref), (2, n2_ref), (3, n3_ref), (4, n4_ref)):
        out[...] = cut(swept[m], hs - m, 1)
    e0_ref[...] = cut(found[0], hs - 1, 0)
    b0_ref[...] = cut(swept[0], hs, 0)
    last_node = cut(swept[4], hs - 4, 0)
    n4own_ref[...] = last_node
    n4last_ref[...] = last_node[:, rows - hs:]
    n4first_ref[...] = last_node[:, :hs]


def fine_sweep(diffusivity, flag, start, prior, parts, decay, src, rate_c, widths_sent):
    rows = start.shape[1] - 2 * START_HALO
    shape = start.shape
    wide = jax.ShapeDtypeStruct((shape[0], rows + 2) + shape[2:], jnp.float32)
    own = jax.ShapeDtypeStruct((shape[0], rows) + shape[2:], jnp.float32)
    cshape = (shape[0], rows // 2, shape[2] // 2, shape[3])
    cown = jax.ShapeDtypeStruct((4,) + cshape, jnp.float32)
    cedge = jax.ShapeDtypeStruct((shape[0], sum(widths_sent)) + cshape[2:], jnp.float32)
    rim = jax.ShapeDtypeStruct((shape[0], START_HALO) + shape[2:], jnp.float32)
    vmem = pl.BlockSpec(memory_space=pltpu.VMEM)
    return pl.pallas_call(
        functools.partial(sweep_kernel, widths_sent, len(prior)),
        out_shape=(wide, wide, wide, wide, own, own, cown, cedge, cedge, own, rim, rim),
        in_specs=[pl.BlockSpec(memory_space=pltpu.SMEM)] * 2 + [vmem] * (7 + len(prior)),
        out_specs=(vmem,) * 12,
    )(diffusivity, flag, start, *prior, *parts, decay, src, rate_c)


def coarse_kernel_laplace(f):
    centre = f[:, 1:-1]
    pair_x = f[:, 2:] + f[:, :-2]
    ny = centre.shape[2]
    lanes = centre.shape[3]
    pair_y = pltpu.roll(centre, ny - 1, 2) + pltpu.roll(centre, 1, 2)
    pair_z = pltpu.roll(centre, lanes - 1, 3) + pltpu.roll(centre, 1, 3)
    return (pair_x - 2.0 * centre) * 0.25 + (pair_y - 2.0 * centre) * 0.25 + (
        pair_z - 2.0 * centre
    )


def finish_kernel(widths_sent, diff_ref, cown_ref, cbefore_ref, cafter_ref, rate_ref, csrc_ref,
                  n1_ref, n2_ref, n3_ref, n4_ref, b_ref, e0_ref, dec_ref, src_ref, *outs):
    spread_table, grouped_table, interp_table, widths = node_tables()
    last = len(outs) == 1
    rows = e0_ref.shape[1]
    crows = rows // 2
    ho = widths_sent[2]
    joined = []
    offset = 0
    for i in range(4):
        w = widths_sent[i]
        if w:
            joined.append(
                jnp.concatenate(
                    [cbefore_ref[:, offset:offset + w], cown_ref[i], cafter_ref[:, offset:offset + w]],
                    axis=1,
                )
            )
        else:
            joined.append(cown_ref[i])
        offset += w
    one, mid, low, late = joined
    hcr = (rate_ref.shape[1] - crows) // 2
    hd = (dec_ref.shape[1] - rows) // 2
    hs = START_HALO
    d0 = diff_ref[0]
    d1 = diff_ref[1]

    def at(ref, h, size, have):
        off = have - h
        return ref[:, off:off + size + 2 * h]

    def cut(v, have, h):
        d = have - h
        return v[:, d:v.shape[1] - d]

    def react(centre, laplace, s):
        product = centre[0] * centre[1] * centre[1]
        return jnp.stack([d0 * laplace[0] - product + s[0], d1 * laplace[1] + product + s[1]])

    def coarse_terms(v):
        return react(v[:, 1:-1], coarse_kernel_laplace(v), at(csrc_ref, ho, crows, hcr))

    half_step = 0.5 * step_length
    rc = at(rate_ref, ho, crows, hcr)
    coarse_two = (
        cut(one, ho + 1, ho)
        + half_step * (coarse_terms(one) - coarse_terms(mid))
        + half_step * rc * low
        + late
    ) / (1.0 + half_step * rc)
    delta_one = cut(one, ho + 1, ho) - cut(mid, ho + 1, ho)
    delta_two = coarse_two - low

    def prolonged(c):
        shape = c.shape
        doubled = jnp.broadcast_to(c[:, :, None], (shape[0], shape[1], 2) + shape[2:])
        doubled = doubled.reshape((shape[0], 2 * shape[1]) + shape[2:])
        return jnp.concatenate([doubled, doubled], axis=2)

    news = {}
    for m, ref in ((1, n1_ref), (2, n2_ref), (3, n3_ref), (4, n4_ref)):
        if last and m < 4:
            continue
        fine = prolonged(interp_table[m][1] * delta_one + interp_table[m][2] * delta_two)
        news[m] = cut(ref[...], 1, ho) + cut(fine, 2 * ho, ho)
    if last:
        half = news[4].shape[2] // 2
        outs[0][:, :, pl.ds(0, half, stride=2), :] = news[4][:, :, :half]
        outs[0][:, :, pl.ds(1, half, stride=2), :] = news[4][:, :, half:]
        return
    own_out, lasts_out, firsts_out, c4_out, c4_last_out, c4_first_out = outs
    src1 = at(src_ref, 0, rows, hd)
    dec0 = at(dec_ref, 0, rows, hd)
    states = [b_ref[...]] + [cut(news[m], 1, 0) for m in range(1, 5)]
    terms = [e0_ref[...]] + [
        react(cut(news[m], 1, 0), kernel_laplace(news[m]), src1) for m in range(1, 5)
    ]
    fulls = [terms[j] - dec0 * states[j] for j in range(5)]
    offset = 0
    for m in range(4):
        summed = spread_table[m][0] * fulls[0]
        for j in range(1, 5):
            summed = summed + spread_table[m][j] * fulls[j]
        part = (widths[m] * dec0 * states[m + 1] - widths[m] * terms[m]) + summed
        own_out[m] = part
        w = hs - 1 - m
        lasts_out[:, offset:offset + w] = part[:, rows - w:]
        firsts_out[:, offset:offset + w] = part[:, :w]
        offset += w
    c4 = cut(interp_table[4][1] * delta_one + interp_table[4][2] * delta_two, ho, 0)
    ch = (hs + 1) // 2
    c4_out[...] = c4
    c4_last_out[...] = c4[:, crows - ch:]
    c4_first_out[...] = c4[:, :ch]


def finish_round(diffusivity, coarse, rate_c, source_c, swept, e0, decay, src, last, widths_sent):
    begin = swept[0]
    shape = begin.shape
    rows = e0.shape[1]
    field = jax.ShapeDtypeStruct((shape[0], rows) + shape[2:], jnp.float32)
    if last:
        out_shape = (field,)
    else:
        sent = sum(START_HALO - 1 - m for m in range(4))
        edge = jax.ShapeDtypeStruct((shape[0], sent) + shape[2:], jnp.float32)
        cshape = (shape[0], rows // 2, shape[2] // 2, shape[3])
        crim = jax.ShapeDtypeStruct((shape[0], (START_HALO + 1) // 2) + cshape[2:], jnp.float32)
        out_shape = (
            jax.ShapeDtypeStruct((4,) + field.shape, jnp.float32), edge, edge,
            jax.ShapeDtypeStruct(cshape, jnp.float32), crim, crim,
        )
    vmem = pl.BlockSpec(memory_space=pltpu.VMEM)
    args = (diffusivity, *coarse, rate_c, source_c, *swept[1:], begin, e0, decay, src)
    return pl.pallas_call(
        functools.partial(finish_kernel, widths_sent),
        out_shape=out_shape,
        in_specs=[pl.BlockSpec(memory_space=pltpu.SMEM)] + [vmem] * (len(args) - 1),
        out_specs=(vmem,) * len(out_shape),
    )(*args)


def start_kernel(diff_ref, init_ref, decay_ref, source_ref, got_before_ref, got_after_ref,
                 own_ref, before_ref, after_ref, rate_ref, csrc_ref, ext_ref, dec_ref, src_ref):
    spread_table, grouped_table, interp_table, widths = node_tables()
    rows = own_ref.shape[2]
    hs = (ext_ref.shape[1] - rows) // 2
    hd = hs - 1
    d0 = diff_ref[0]
    d1 = diff_ref[1]

    def joined(ref, offset, w):
        return jnp.concatenate(
            [
                even_odd_load(got_before_ref, (slice(None), pl.ds(offset, w))),
                even_odd_load(ref),
                even_odd_load(got_after_ref, (slice(None), pl.ds(offset, w))),
            ],
            axis=1,
        )

    state = joined(init_ref, 0, hs)
    dec = joined(decay_ref, hs, hd)
    s = joined(source_ref, hs + hd, hd)
    ext_ref[...] = state
    dec_ref[...] = dec
    src_ref[...] = s
    inner = state[:, 1:-1]
    laplace = kernel_laplace(state)
    product = inner[0] * inner[1] * inner[1]
    terms = jnp.stack([d0 * laplace[0] - product + s[0], d1 * laplace[1] + product + s[1]])
    full = terms - dec * inner
    edge = hs - 1
    offset = 0
    for m in range(4):
        weight = sum(spread_table[m][j] for j in range(5))
        part = (widths[m] * dec * inner - widths[m] * terms) + weight * full
        own_ref[m] = part[:, edge:edge + rows]
        w = edge - m
        before_ref[:, offset:offset + w] = part[:, m:edge]
        after_ref[:, offset:offset + w] = part[:, edge + rows:edge + rows + w]
        offset += w
    rate_ref[...] = kernel_restrict(dec)
    csrc_ref[...] = kernel_restrict(s)


def start_terms(diffusivity, own_arrays, got_before, got_after):
    own_shape = own_arrays[0].shape
    rows = own_shape[1]
    shape = (own_shape[0], rows + 2 * START_HALO) + own_shape[2:]
    fixed = jax.ShapeDtypeStruct(
        (own_shape[0], rows + 2 * (START_HALO - 1)) + own_shape[2:], jnp.float32
    )
    sent = sum(START_HALO - 1 - m for m in range(4))
    edge = jax.ShapeDtypeStruct((shape[0], sent) + shape[2:], jnp.float32)
    cshape = (shape[0], (rows + 2 * (START_HALO - 1)) // 2, shape[2] // 2, shape[3])
    coarse = jax.ShapeDtypeStruct(cshape, jnp.float32)
    vmem = pl.BlockSpec(memory_space=pltpu.VMEM)
    return pl.pallas_call(
        start_kernel,
        out_shape=(
            jax.ShapeDtypeStruct((4, shape[0], rows) + shape[2:], jnp.float32),
            edge, edge, coarse, coarse,
            jax.ShapeDtypeStruct(shape, jnp.float32),
            fixed,
            fixed,
        ),
        in_specs=[pl.BlockSpec(memory_space=pltpu.SMEM)] + [vmem] * 5,
        out_specs=(vmem,) * 8,
    )(diffusivity, *own_arrays, got_before, got_after)


def packed_halo(fields):
    size = lax.axis_size("space")
    rows = fields[0][0].shape[-3]
    axis = fields[0][0].ndim - 3
    up = [(i, (i + 1) % size) for i in range(size)]
    down = [((i + 1) % size, i) for i in range(size)]
    lasts = jnp.concatenate(
        [lax.slice_in_dim(a, rows - w, rows, axis=axis) for a, w in fields], axis=axis
    )
    firsts = jnp.concatenate([lax.slice_in_dim(a, 0, w, axis=axis) for a, w in fields], axis=axis)
    before = lax.ppermute(lasts, "space", up)
    after = lax.ppermute(firsts, "space", down)
    out = []
    offset = 0
    for a, w in fields:
        out.append(
            (
                jnp.concatenate(
                    [
                        lax.slice_in_dim(before, offset, offset + w, axis=axis),
                        a,
                        lax.slice_in_dim(after, offset, offset + w, axis=axis),
                    ],
                    axis=axis,
                ),
                w,
            )
        )
        offset += w
    return out


def per_device(initial, decay_rate, source, diffusivity):
    spread_table, grouped_table, interp_table, widths = node_tables()
    first_slice = lax.axis_index("tm") == 0
    hs = START_HALO
    assert hs == 5 and initial.shape[-3] >= hs

    own_start = initial[0]
    size = lax.axis_size("space")
    up = [(i, (i + 1) % size) for i in range(size)]
    down = [((i + 1) % size, i) for i in range(size)]
    rows = own_start.shape[-3]
    widths_in = (hs, hs - 1, hs - 1)
    own_arrays = (own_start, decay_rate, source)
    got_before = lax.ppermute(
        jnp.concatenate([a[:, rows - w:] for a, w in zip(own_arrays, widths_in)], axis=1),
        "space", up,
    )
    got_after = lax.ppermute(
        jnp.concatenate([a[:, :w] for a, w in zip(own_arrays, widths_in)], axis=1),
        "space", down,
    )
    own4, before4, after4, rate_own, csrc_own, own_ext, dec_ext, src_ext = start_terms(
        diffusivity, own_arrays, got_before, got_after
    )
    decay = (dec_ext, hs - 1)
    src = (src_ext, hs - 1)
    rate_c = (rate_own, (hs - 1) // 2)
    source_c = (csrc_own, (hs - 1) // 2)

    def fine_E(field):
        a, h = field
        laplace = fine_laplace(a)
        return react_terms(a[..., 1:-1, :, :], laplace, diffusivity, crop(src, h - 1)), h - 1

    def coarse_E(field):
        a, h = field
        laplace = coarse_laplace(a)
        return react_terms(a[..., 1:-1, :, :], laplace, diffusivity, crop(source_c, h - 1)), h - 1

    def full(field, field_E):
        h = min(field[1], field_E[1])
        return crop(field_E, h) - crop(decay, h) * crop(field, h), h

    def step_terms(states, terms):
        fulls = [full(states[j], terms[j]) for j in range(5)]
        hf = min(f[1] for f in fulls)
        out = []
        for m in range(4):
            h = min(hf, terms[m][1], states[m + 1][1])
            summed = spread_table[m][0] * crop(fulls[0], h)
            for j in range(1, 5):
                summed = summed + spread_table[m][j] * crop(fulls[j], h)
            own = (
                widths[m] * crop(decay, h) * crop(states[m + 1], h)
                - widths[m] * crop(terms[m], h)
            ) + summed
            out.append((own, h))
        return out

    def advance(prior, pieces, last):
        widths_sent = (1, 1, 0, 0) if last else (2, 2, 1, 1)
        (n1, n2, n3, n4, e0, b0, cown, clasts, cfirsts,
         n4own, n4last, n4first) = fine_sweep(
            diffusivity, flag, own_ext, prior, pieces, decay[0], src[0], rate_c[0], widths_sent,
        )
        sent_node = None if last else from_previous_slice((n4own, n4last, n4first))
        coarse = (
            cown,
            lax.ppermute(clasts, "space", up),
            lax.ppermute(cfirsts, "space", down),
        )
        if sent_node is not None:
            coarse, sent_node = lax.optimization_barrier((coarse, sent_node))
        return finish_round(
            diffusivity, coarse, rate_c[0], source_c[0],
            (b0, n1, n2, n3, n4), e0, decay[0], src[0], last, widths_sent,
        ), sent_node

    size = lax.axis_size("space")
    up = [(i, (i + 1) % size) for i in range(size)]
    down = [((i + 1) % size, i) for i in range(size)]
    rows = own_start.shape[-3]
    flag = jnp.where(first_slice, 1, 0).astype(jnp.int32).reshape(1)
    pieces = (own4, before4, after4)
    prior = from_previous_slice(
        (own_start, own_start[:, rows - hs:], own_start[:, :hs])
    )
    for k in range(ROUNDS):
        last = k + 1 == ROUNDS
        outs, sent_node = advance(prior, pieces, last)
        if not last:
            own4, lasts, firsts, c4, c4_last, c4_first = outs
            pieces = (
                own4,
                lax.ppermute(lasts, "space", up),
                lax.ppermute(firsts, "space", down),
            )
            prior = sent_node + from_previous_slice((c4, c4_last, c4_first))
    return outs[0][None]


def solution(mesh):
    placed = (
        P("tm", None, "space", None, None),
        P(None, "space", None, None),
        P(None, "space", None, None),
        P(),
    )
    return jax.shard_map(
        per_device,
        mesh=mesh,
        in_specs=placed,
        out_specs=P("tm", None, "space", None, None),
        check_vma=False,
    )
```

```python
import functools
import math

import jax
import jax.numpy as jnp
from jax import lax
from jax.experimental import pallas as pl
from jax.experimental.pallas import tpu as pltpu
from jax.sharding import PartitionSpec as P

ROUNDS = 3

START_HALO = 5

step_length = 0.5


def lagrange_integral(nodes, j, upper_end):
    coeffs = [1.0]
    scale_down = 1.0
    for i in range(len(nodes)):
        if i != j:
            grown = [0.0] * (len(coeffs) + 1)
            for p in range(len(coeffs)):
                grown[p + 1] = grown[p + 1] + coeffs[p]
                grown[p] = grown[p] - nodes[i] * coeffs[p]
            coeffs = grown
            scale_down = scale_down * (nodes[j] - nodes[i])
    summed_up = 0.0
    for p in range(len(coeffs)):
        summed_up = summed_up + coeffs[p] * upper_end ** (p + 1) / (p + 1)
    return summed_up / scale_down


def node_tables():
    radical = math.sqrt(3.0 / 7.0)
    fine_nodes = [0.0, 0.5 * (1.0 - radical), 0.5, 0.5 * (1.0 + radical), 1.0]
    coarse_nodes = [0.0, 0.5, 1.0]
    integrals = [
        [lagrange_integral(fine_nodes, j, fine_nodes[m]) for j in range(5)] for m in range(5)
    ]
    spread_table = [
        [float(step_length * (integrals[m + 1][j] - integrals[m][j])) for j in range(5)]
        for m in range(4)
    ]
    grouped_table = [
        [spread_table[2 * c][j] + spread_table[2 * c + 1][j] for j in range(5)] for c in range(2)
    ]
    interp_table = []
    for m in range(5):
        weights_row = []
        for k in range(3):
            factor = 1.0
            for i in range(3):
                if i != k:
                    factor = (
                        factor
                        * (fine_nodes[m] - coarse_nodes[i])
                        / (coarse_nodes[k] - coarse_nodes[i])
                    )
            weights_row.append(factor)
        interp_table.append(weights_row)
    widths = [step_length * (fine_nodes[m + 1] - fine_nodes[m]) for m in range(4)]
    return (spread_table, grouped_table, interp_table, widths)


def to_even_odd(a):
    return jnp.concatenate([a[..., 0::2, :], a[..., 1::2, :]], axis=-2)


def from_even_odd(a):
    half = a.shape[-2] // 2
    woven = jnp.stack([a[..., :half, :], a[..., half:, :]], axis=-2)
    return woven.reshape(a.shape)


def crop(field, h):
    a, have = field
    d = have - h
    assert d >= 0
    if d == 0:
        return a
    return lax.slice_in_dim(a, d, a.shape[-3] - d, axis=a.ndim - 3)


def space_halo(a, h):
    if h == 0:
        return a
    size = lax.axis_size("space")
    rows = a.shape[-3]
    assert h <= rows
    up = [(i, (i + 1) % size) for i in range(size)]
    down = [((i + 1) % size, i) for i in range(size)]
    before = lax.ppermute(lax.slice_in_dim(a, rows - h, rows, axis=a.ndim - 3), "space", up)
    after = lax.ppermute(lax.slice_in_dim(a, 0, h, axis=a.ndim - 3), "space", down)
    return jnp.concatenate([before, a, after], axis=a.ndim - 3)


def from_previous_slice(pieces):
    slices = lax.axis_size("tm")
    size = lax.axis_size("space")
    axes = ("tm", "space")

    def moved(piece, shift):
        pairs = [
            (t * size + s, (t + 1) * size + (s + shift) % size)
            for t in range(slices - 1)
            for s in range(size)
        ]
        return lax.ppermute(piece, axes, pairs)

    own, lasts, firsts = pieces
    return moved(own, 0), moved(lasts, 1), moved(firsts, -1)


def react_terms(field, laplace, diffusivity, source):
    first_part = field[0]
    second_part = field[1]
    product = first_part * second_part * second_part
    return jnp.stack(
        [
            diffusivity[0] * laplace[0] - product + source[0],
            diffusivity[1] * laplace[1] + product + source[1],
        ],
        axis=0,
    )


def fine_laplace(a):
    centre = a[..., 1:-1, :, :]
    pair_x = a[..., 2:, :, :] + a[..., :-2, :, :]
    half = centre.shape[-2] // 2
    even = centre[..., :half, :]
    odd = centre[..., half:, :]
    pair_y = jnp.concatenate(
        [odd + jnp.roll(odd, 1, -2), jnp.roll(even, -1, -2) + even], axis=-2
    )
    pair_z = jnp.roll(centre, -1, -1) + jnp.roll(centre, 1, -1)
    return pair_x + pair_y + pair_z - 6.0 * centre


def coarse_laplace(a):
    centre = a[..., 1:-1, :, :]
    pair_x = a[..., 2:, :, :] + a[..., :-2, :, :]
    pair_y = jnp.roll(centre, -1, -2) + jnp.roll(centre, 1, -2)
    pair_z = jnp.roll(centre, -1, -1) + jnp.roll(centre, 1, -1)
    return (pair_x - 2.0 * centre) * 0.25 + (pair_y - 2.0 * centre) * 0.25 + (
        pair_z - 2.0 * centre
    )


def restrict(field):
    a, h = field
    h2 = h - h % 2
    a = crop(field, h2)
    rows = a.shape[-3]
    half = a.shape[-2] // 2
    pairs = a.reshape(a.shape[:-3] + (rows // 2, 2) + a.shape[-2:])
    even = pairs[..., :half, :]
    odd = pairs[..., half:, :]
    upper = even[..., 0, :, :] + even[..., 1, :, :]
    lower = odd[..., 0, :, :] + odd[..., 1, :, :]
    return (upper + lower) * 0.25, h2 // 2


def prolong(a):
    rows = jnp.repeat(a, 2, axis=a.ndim - 3)
    return jnp.concatenate([rows, rows], axis=-2)


def even_odd_load(ref, index=()):
    view = ref.at[index] if index != () else ref
    lead = (slice(None),) * (len(view.shape) - 2)
    half = view.shape[-2] // 2
    even = view[lead + (pl.ds(0, half, stride=2), slice(None))]
    odd = view[lead + (pl.ds(1, half, stride=2), slice(None))]
    return jnp.concatenate([even, odd], axis=-2)


def kernel_laplace(f):
    centre = f[:, 1:-1]
    pair_x = f[:, 2:] + f[:, :-2]
    half = centre.shape[2] // 2
    even = centre[:, :, :half]
    odd = centre[:, :, half:]
    pair_y = jnp.concatenate(
        [odd + pltpu.roll(odd, 1, 2), pltpu.roll(even, half - 1, 2) + even], axis=2
    )
    lanes = centre.shape[3]
    pair_z = pltpu.roll(centre, lanes - 1, 3) + pltpu.roll(centre, 1, 3)
    return pair_x + pair_y + pair_z - 6.0 * centre


def kernel_restrict(v):
    shape = v.shape
    pairs = v.reshape((shape[0], shape[1] // 2, 2) + shape[2:])
    half = shape[2] // 2
    even = pairs[:, :, :, :half]
    odd = pairs[:, :, :, half:]
    upper = even[:, :, 0] + even[:, :, 1]
    lower = odd[:, :, 0] + odd[:, :, 1]
    return (upper + lower) * 0.25


def sweep_kernel(widths_sent, natural_prior, diff_ref, flag_ref, start_ref, centre_ref, bbefore_ref, bafter_ref,
                 own_ref, before_ref, after_ref, dec_ref, src_ref,
                 rate_ref, n1_ref, n2_ref, n3_ref, n4_ref, e0_ref, b0_ref, cown_ref, clasts_ref,
                 cfirsts_ref, v1w_ref):
    spread_table, grouped_table, interp_table, widths = node_tables()
    rows = e0_ref.shape[1]
    hs = (start_ref.shape[1] - rows) // 2
    hd = (dec_ref.shape[1] - rows) // 2
    d0 = diff_ref[0]
    d1 = diff_ref[1]

    def at(ref, h):
        off = hd - h
        return ref[:, off:off + rows + 2 * h]

    def cut(v, have, h):
        d = have - h
        return v[:, d:v.shape[1] - d]

    def terms(f, h):
        laplace = kernel_laplace(f)
        centre = f[:, 1:-1]
        s = at(src_ref, h - 1)
        product = centre[0] * centre[1] * centre[1]
        return jnp.stack([d0 * laplace[0] - product + s[0], d1 * laplace[1] + product + s[1]])

    parts = []
    offset = 0
    for m in range(4):
        w = hs - 1 - m
        parts.append(
            jnp.concatenate(
                [before_ref[:, offset:offset + w], own_ref[m], after_ref[:, offset:offset + w]],
                axis=1,
            )
        )
        offset += w
    if natural_prior:
        pieces = [even_odd_load(r) for r in (bbefore_ref, centre_ref, bafter_ref)]
    else:
        pieces = [r[...] for r in (bbefore_ref, centre_ref, bafter_ref)]
    joined = jnp.concatenate(pieces, axis=1)
    swept = [jnp.where(flag_ref[0] == 1, start_ref[...], joined)]
    found = []
    for m in range(4):
        have = hs - m
        e = terms(swept[m], have)
        found.append(e)
        h = have - 1
        numerator = (cut(swept[m], have, h) + widths[m] * e) + parts[m]
        swept.append(numerator / (1.0 + widths[m] * at(dec_ref, h)))
    found.append(terms(swept[4], hs - 4))
    dec0 = at(dec_ref, 0)
    fulls = [cut(found[j], hs - 1 - j, 0) - dec0 * cut(swept[j], hs - j, 0) for j in range(5)]
    integrated = []
    for c in range(2):
        summed = grouped_table[c][0] * fulls[0]
        for j in range(1, 5):
            summed = summed + grouped_table[c][j] * fulls[j]
        integrated.append(kernel_restrict(summed))
    crows = rows // 2
    hcr = (rate_ref.shape[1] - crows) // 2
    rc = rate_ref[:, hcr:hcr + crows]
    coarse_vals = [kernel_restrict(cut(swept[j], hs - j, 0)) for j in (0, 2, 4)]
    v1w_ref[...] = kernel_restrict(cut(swept[2], hs - 2, 2))
    half_step = 0.5 * step_length
    coarse_one = (
        coarse_vals[0] + half_step * rc * coarse_vals[1] + integrated[0]
    ) / (1.0 + half_step * rc)
    sent = [coarse_one, coarse_vals[1], coarse_vals[2], integrated[1]]
    offset = 0
    for i, piece in enumerate(sent):
        cown_ref[i] = piece
        w = widths_sent[i]
        skip = 1 if i == 1 else 0
        if w - skip:
            clasts_ref[:, offset:offset + w - skip] = piece[:, crows - w:crows - skip]
            cfirsts_ref[:, offset:offset + w - skip] = piece[:, skip:w]
        offset += w - skip
    for m, out in ((1, n1_ref), (2, n2_ref), (3, n3_ref), (4, n4_ref)):
        out[...] = cut(swept[m], hs - m, 1)
    e0_ref[...] = cut(found[0], hs - 1, 0)
    b0_ref[...] = cut(swept[0], hs, 0)


def fine_sweep(diffusivity, flag, start, prior, parts, decay, src, rate_c, widths_sent,
               natural_prior):
    rows = start.shape[1] - 2 * START_HALO
    shape = start.shape
    wide = jax.ShapeDtypeStruct((shape[0], rows + 2) + shape[2:], jnp.float32)
    own = jax.ShapeDtypeStruct((shape[0], rows) + shape[2:], jnp.float32)
    cshape = (shape[0], rows // 2, shape[2] // 2, shape[3])
    cown = jax.ShapeDtypeStruct((4,) + cshape, jnp.float32)
    cedge = jax.ShapeDtypeStruct((shape[0], sum(widths_sent) - 1) + cshape[2:], jnp.float32)
    cwide = jax.ShapeDtypeStruct((shape[0], rows // 2 + 2) + cshape[2:], jnp.float32)
    vmem = pl.BlockSpec(memory_space=pltpu.VMEM)
    return pl.pallas_call(
        functools.partial(sweep_kernel, widths_sent, natural_prior),
        out_shape=(wide, wide, wide, wide, own, own, cown, cedge, cedge, cwide),
        in_specs=[pl.BlockSpec(memory_space=pltpu.SMEM)] * 2 + [vmem] * 10,
        out_specs=(vmem,) * 10,
    )(diffusivity, flag, start, *prior, *parts, decay, src, rate_c)


def coarse_kernel_laplace(f):
    centre = f[:, 1:-1]
    pair_x = f[:, 2:] + f[:, :-2]
    ny = centre.shape[2]
    lanes = centre.shape[3]
    pair_y = pltpu.roll(centre, ny - 1, 2) + pltpu.roll(centre, 1, 2)
    pair_z = pltpu.roll(centre, lanes - 1, 3) + pltpu.roll(centre, 1, 3)
    return (pair_x - 2.0 * centre) * 0.25 + (pair_y - 2.0 * centre) * 0.25 + (
        pair_z - 2.0 * centre
    )


def finish_kernel(widths_sent, diff_ref, cown_ref, cbefore_ref, cafter_ref, v1w_ref, rate_ref, csrc_ref,
                  n1_ref, n2_ref, n3_ref, n4_ref, b_ref, e0_ref, dec_ref, src_ref, *outs):
    spread_table, grouped_table, interp_table, widths = node_tables()
    last = len(outs) == 1
    rows = e0_ref.shape[1]
    crows = rows // 2
    ho = widths_sent[2]
    joined = []
    offset = 0
    for i in range(4):
        w = widths_sent[i]
        skip = 1 if i == 1 else 0
        centre = v1w_ref[...] if skip else cown_ref[i]
        sw = w - skip
        if sw:
            joined.append(
                jnp.concatenate(
                    [cbefore_ref[:, offset:offset + sw], centre, cafter_ref[:, offset:offset + sw]],
                    axis=1,
                )
            )
        else:
            joined.append(centre)
        offset += sw
    one, mid, low, late = joined
    hcr = (rate_ref.shape[1] - crows) // 2
    hd = (dec_ref.shape[1] - rows) // 2
    hs = START_HALO
    d0 = diff_ref[0]
    d1 = diff_ref[1]

    def at(ref, h, size, have):
        off = have - h
        return ref[:, off:off + size + 2 * h]

    def cut(v, have, h):
        d = have - h
        return v[:, d:v.shape[1] - d]

    def react(centre, laplace, s):
        product = centre[0] * centre[1] * centre[1]
        return jnp.stack([d0 * laplace[0] - product + s[0], d1 * laplace[1] + product + s[1]])

    def coarse_terms(v):
        return react(v[:, 1:-1], coarse_kernel_laplace(v), at(csrc_ref, ho, crows, hcr))

    half_step = 0.5 * step_length
    rc = at(rate_ref, ho, crows, hcr)
    coarse_two = (
        cut(one, ho + 1, ho)
        + half_step * (coarse_terms(one) - coarse_terms(mid))
        + half_step * rc * low
        + late
    ) / (1.0 + half_step * rc)
    delta_one = cut(one, ho + 1, ho) - cut(mid, ho + 1, ho)
    delta_two = coarse_two - low

    def prolonged(c):
        shape = c.shape
        doubled = jnp.broadcast_to(c[:, :, None], (shape[0], shape[1], 2) + shape[2:])
        doubled = doubled.reshape((shape[0], 2 * shape[1]) + shape[2:])
        return jnp.concatenate([doubled, doubled], axis=2)

    news = {}
    for m, ref in ((1, n1_ref), (2, n2_ref), (3, n3_ref), (4, n4_ref)):
        if last and m < 4:
            continue
        fine = prolonged(interp_table[m][1] * delta_one + interp_table[m][2] * delta_two)
        news[m] = cut(ref[...], 1, ho) + cut(fine, 2 * ho, ho)
    if last:
        half = news[4].shape[2] // 2
        outs[0][:, :, pl.ds(0, half, stride=2), :] = news[4][:, :, :half]
        outs[0][:, :, pl.ds(1, half, stride=2), :] = news[4][:, :, half:]
        return
    own_out, lasts_out, firsts_out, u4_out, u4_last_out, u4_first_out = outs
    src1 = at(src_ref, 0, rows, hd)
    dec0 = at(dec_ref, 0, rows, hd)
    states = [b_ref[...]] + [cut(news[m], 1, 0) for m in range(1, 5)]
    terms = [e0_ref[...]] + [
        react(cut(news[m], 1, 0), kernel_laplace(news[m]), src1) for m in range(1, 5)
    ]
    fulls = [terms[j] - dec0 * states[j] for j in range(5)]
    offset = 0
    for m in range(4):
        summed = spread_table[m][0] * fulls[0]
        for j in range(1, 5):
            summed = summed + spread_table[m][j] * fulls[j]
        part = (widths[m] * dec0 * states[m + 1] - widths[m] * terms[m]) + summed
        own_out[m] = part
        w = hs - 1 - m
        lasts_out[:, offset:offset + w] = part[:, rows - w:]
        firsts_out[:, offset:offset + w] = part[:, :w]
        offset += w
    u4_out[...] = states[4]
    u4_last_out[...] = states[4][:, rows - hs:]
    u4_first_out[...] = states[4][:, :hs]


def finish_round(diffusivity, coarse, rate_c, source_c, swept, e0, decay, src, last, widths_sent):
    begin = swept[0]
    shape = begin.shape
    rows = e0.shape[1]
    field = jax.ShapeDtypeStruct((shape[0], rows) + shape[2:], jnp.float32)
    if last:
        out_shape = (field,)
    else:
        sent = sum(START_HALO - 1 - m for m in range(4))
        edge = jax.ShapeDtypeStruct((shape[0], sent) + shape[2:], jnp.float32)
        rim = jax.ShapeDtypeStruct((shape[0], START_HALO) + shape[2:], jnp.float32)
        out_shape = (jax.ShapeDtypeStruct((4,) + field.shape, jnp.float32), edge, edge, field, rim, rim)
    vmem = pl.BlockSpec(memory_space=pltpu.VMEM)
    args = (diffusivity, *coarse, rate_c, source_c, *swept[1:], begin, e0, decay, src)
    return pl.pallas_call(
        functools.partial(finish_kernel, widths_sent),
        out_shape=out_shape,
        in_specs=[pl.BlockSpec(memory_space=pltpu.SMEM)] + [vmem] * (len(args) - 1),
        out_specs=(vmem,) * len(out_shape),
    )(*args)


def start_kernel(diff_ref, init_ref, decay_ref, source_ref, got_before_ref, got_after_ref,
                 own_ref, before_ref, after_ref, rate_ref, csrc_ref, ext_ref, dec_ref, src_ref):
    spread_table, grouped_table, interp_table, widths = node_tables()
    rows = own_ref.shape[2]
    hs = (ext_ref.shape[1] - rows) // 2
    hd = hs - 1
    d0 = diff_ref[0]
    d1 = diff_ref[1]

    def joined(ref, offset, w):
        return jnp.concatenate(
            [
                even_odd_load(got_before_ref, (slice(None), pl.ds(offset, w))),
                even_odd_load(ref),
                even_odd_load(got_after_ref, (slice(None), pl.ds(offset, w))),
            ],
            axis=1,
        )

    state = joined(init_ref, 0, hs)
    dec = joined(decay_ref, hs, hd)
    s = joined(source_ref, hs + hd, hd)
    ext_ref[...] = state
    dec_ref[...] = dec
    src_ref[...] = s
    inner = state[:, 1:-1]
    laplace = kernel_laplace(state)
    product = inner[0] * inner[1] * inner[1]
    terms = jnp.stack([d0 * laplace[0] - product + s[0], d1 * laplace[1] + product + s[1]])
    full = terms - dec * inner
    edge = hs - 1
    offset = 0
    for m in range(4):
        weight = sum(spread_table[m][j] for j in range(5))
        part = (widths[m] * dec * inner - widths[m] * terms) + weight * full
        own_ref[m] = part[:, edge:edge + rows]
        w = edge - m
        before_ref[:, offset:offset + w] = part[:, m:edge]
        after_ref[:, offset:offset + w] = part[:, edge + rows:edge + rows + w]
        offset += w
    rate_ref[...] = kernel_restrict(dec)
    csrc_ref[...] = kernel_restrict(s)


def start_terms(diffusivity, own_arrays, got_before, got_after):
    own_shape = own_arrays[0].shape
    rows = own_shape[1]
    shape = (own_shape[0], rows + 2 * START_HALO) + own_shape[2:]
    fixed = jax.ShapeDtypeStruct(
        (own_shape[0], rows + 2 * (START_HALO - 1)) + own_shape[2:], jnp.float32
    )
    sent = sum(START_HALO - 1 - m for m in range(4))
    edge = jax.ShapeDtypeStruct((shape[0], sent) + shape[2:], jnp.float32)
    cshape = (shape[0], (rows + 2 * (START_HALO - 1)) // 2, shape[2] // 2, shape[3])
    coarse = jax.ShapeDtypeStruct(cshape, jnp.float32)
    vmem = pl.BlockSpec(memory_space=pltpu.VMEM)
    return pl.pallas_call(
        start_kernel,
        out_shape=(
            jax.ShapeDtypeStruct((4, shape[0], rows) + shape[2:], jnp.float32),
            edge, edge, coarse, coarse,
            jax.ShapeDtypeStruct(shape, jnp.float32),
            fixed,
            fixed,
        ),
        in_specs=[pl.BlockSpec(memory_space=pltpu.SMEM)] + [vmem] * 5,
        out_specs=(vmem,) * 8,
    )(diffusivity, *own_arrays, got_before, got_after)


def packed_halo(fields):
    size = lax.axis_size("space")
    rows = fields[0][0].shape[-3]
    axis = fields[0][0].ndim - 3
    up = [(i, (i + 1) % size) for i in range(size)]
    down = [((i + 1) % size, i) for i in range(size)]
    lasts = jnp.concatenate(
        [lax.slice_in_dim(a, rows - w, rows, axis=axis) for a, w in fields], axis=axis
    )
    firsts = jnp.concatenate([lax.slice_in_dim(a, 0, w, axis=axis) for a, w in fields], axis=axis)
    before = lax.ppermute(lasts, "space", up)
    after = lax.ppermute(firsts, "space", down)
    out = []
    offset = 0
    for a, w in fields:
        out.append(
            (
                jnp.concatenate(
                    [
                        lax.slice_in_dim(before, offset, offset + w, axis=axis),
                        a,
                        lax.slice_in_dim(after, offset, offset + w, axis=axis),
                    ],
                    axis=axis,
                ),
                w,
            )
        )
        offset += w
    return out


def per_device(initial, decay_rate, source, diffusivity):
    spread_table, grouped_table, interp_table, widths = node_tables()
    first_slice = lax.axis_index("tm") == 0
    hs = START_HALO
    assert hs == 5 and initial.shape[-3] >= hs

    own_start = initial[0]
    size = lax.axis_size("space")
    up = [(i, (i + 1) % size) for i in range(size)]
    down = [((i + 1) % size, i) for i in range(size)]
    rows = own_start.shape[-3]
    widths_in = (hs, hs - 1, hs - 1)
    own_arrays = (own_start, decay_rate, source)
    got_before = lax.ppermute(
        jnp.concatenate([a[:, rows - w:] for a, w in zip(own_arrays, widths_in)], axis=1),
        "space", up,
    )
    got_after = lax.ppermute(
        jnp.concatenate([a[:, :w] for a, w in zip(own_arrays, widths_in)], axis=1),
        "space", down,
    )
    own4, before4, after4, rate_own, csrc_own, own_ext, dec_ext, src_ext = start_terms(
        diffusivity, own_arrays, got_before, got_after
    )
    decay = (dec_ext, hs - 1)
    src = (src_ext, hs - 1)
    rate_c = (rate_own, (hs - 1) // 2)
    source_c = (csrc_own, (hs - 1) // 2)

    def fine_E(field):
        a, h = field
        laplace = fine_laplace(a)
        return react_terms(a[..., 1:-1, :, :], laplace, diffusivity, crop(src, h - 1)), h - 1

    def coarse_E(field):
        a, h = field
        laplace = coarse_laplace(a)
        return react_terms(a[..., 1:-1, :, :], laplace, diffusivity, crop(source_c, h - 1)), h - 1

    def full(field, field_E):
        h = min(field[1], field_E[1])
        return crop(field_E, h) - crop(decay, h) * crop(field, h), h

    def step_terms(states, terms):
        fulls = [full(states[j], terms[j]) for j in range(5)]
        hf = min(f[1] for f in fulls)
        out = []
        for m in range(4):
            h = min(hf, terms[m][1], states[m + 1][1])
            summed = spread_table[m][0] * crop(fulls[0], h)
            for j in range(1, 5):
                summed = summed + spread_table[m][j] * crop(fulls[j], h)
            own = (
                widths[m] * crop(decay, h) * crop(states[m + 1], h)
                - widths[m] * crop(terms[m], h)
            ) + summed
            out.append((own, h))
        return out

    def advance(prior, pieces, last, natural):
        widths_sent = (1, 1, 0, 0) if last else (2, 2, 1, 1)
        n1, n2, n3, n4, e0, b0, cown, clasts, cfirsts, v1w = fine_sweep(
            diffusivity, flag, own_ext, prior, pieces, decay[0], src[0], rate_c[0], widths_sent,
            natural,
        )
        coarse = (
            cown,
            lax.ppermute(clasts, "space", up),
            lax.ppermute(cfirsts, "space", down),
            v1w,
        )
        return finish_round(
            diffusivity, coarse, rate_c[0], source_c[0],
            (b0, n1, n2, n3, n4), e0, decay[0], src[0], last, widths_sent,
        )

    size = lax.axis_size("space")
    up = [(i, (i + 1) % size) for i in range(size)]
    down = [((i + 1) % size, i) for i in range(size)]
    rows = own_start.shape[-3]
    flag = jnp.where(first_slice, 1, 0).astype(jnp.int32).reshape(1)
    pieces = (own4, before4, after4)
    prior = from_previous_slice(
        (own_start, own_start[:, rows - hs:], own_start[:, :hs])
    )
    for k in range(ROUNDS):
        last = k + 1 == ROUNDS
        outs = advance(prior, pieces, last, k == 0)
        if not last:
            own4, lasts, firsts, u4, u4_last, u4_first = outs
            pieces = (
                own4,
                lax.ppermute(lasts, "space", up),
                lax.ppermute(firsts, "space", down),
            )
            prior = from_previous_slice((u4, u4_last, u4_first))
    return outs[0][None]


def solution(mesh):
    placed = (
        P("tm", None, "space", None, None),
        P(None, "space", None, None),
        P(None, "space", None, None),
        P(),
    )
    return jax.shard_map(
        per_device,
        mesh=mesh,
        in_specs=placed,
        out_specs=P("tm", None, "space", None, None),
        check_vma=False,
    )
```

```python
import functools
import math

import jax
import jax.numpy as jnp
from jax import lax
from jax.experimental import pallas as pl
from jax.experimental.pallas import tpu as pltpu
from jax.sharding import PartitionSpec as P

ROUNDS = 3

START_HALO = 5

step_length = 0.5


def lagrange_integral(nodes, j, upper_end):
    coeffs = [1.0]
    scale_down = 1.0
    for i in range(len(nodes)):
        if i != j:
            grown = [0.0] * (len(coeffs) + 1)
            for p in range(len(coeffs)):
                grown[p + 1] = grown[p + 1] + coeffs[p]
                grown[p] = grown[p] - nodes[i] * coeffs[p]
            coeffs = grown
            scale_down = scale_down * (nodes[j] - nodes[i])
    summed_up = 0.0
    for p in range(len(coeffs)):
        summed_up = summed_up + coeffs[p] * upper_end ** (p + 1) / (p + 1)
    return summed_up / scale_down


def node_tables():
    radical = math.sqrt(3.0 / 7.0)
    fine_nodes = [0.0, 0.5 * (1.0 - radical), 0.5, 0.5 * (1.0 + radical), 1.0]
    coarse_nodes = [0.0, 0.5, 1.0]
    integrals = [
        [lagrange_integral(fine_nodes, j, fine_nodes[m]) for j in range(5)] for m in range(5)
    ]
    spread_table = [
        [float(step_length * (integrals[m + 1][j] - integrals[m][j])) for j in range(5)]
        for m in range(4)
    ]
    grouped_table = [
        [spread_table[2 * c][j] + spread_table[2 * c + 1][j] for j in range(5)] for c in range(2)
    ]
    interp_table = []
    for m in range(5):
        weights_row = []
        for k in range(3):
            factor = 1.0
            for i in range(3):
                if i != k:
                    factor = (
                        factor
                        * (fine_nodes[m] - coarse_nodes[i])
                        / (coarse_nodes[k] - coarse_nodes[i])
                    )
            weights_row.append(factor)
        interp_table.append(weights_row)
    widths = [step_length * (fine_nodes[m + 1] - fine_nodes[m]) for m in range(4)]
    return (spread_table, grouped_table, interp_table, widths)


def to_even_odd(a):
    return jnp.concatenate([a[..., 0::2, :], a[..., 1::2, :]], axis=-2)


def from_even_odd(a):
    half = a.shape[-2] // 2
    woven = jnp.stack([a[..., :half, :], a[..., half:, :]], axis=-2)
    return woven.reshape(a.shape)


def crop(field, h):
    a, have = field
    d = have - h
    assert d >= 0
    if d == 0:
        return a
    return lax.slice_in_dim(a, d, a.shape[-3] - d, axis=a.ndim - 3)


def space_halo(a, h):
    if h == 0:
        return a
    size = lax.axis_size("space")
    rows = a.shape[-3]
    assert h <= rows
    up = [(i, (i + 1) % size) for i in range(size)]
    down = [((i + 1) % size, i) for i in range(size)]
    before = lax.ppermute(lax.slice_in_dim(a, rows - h, rows, axis=a.ndim - 3), "space", up)
    after = lax.ppermute(lax.slice_in_dim(a, 0, h, axis=a.ndim - 3), "space", down)
    return jnp.concatenate([before, a, after], axis=a.ndim - 3)


def from_previous_slice(pieces):
    slices = lax.axis_size("tm")
    size = lax.axis_size("space")
    axes = ("tm", "space")

    def moved(piece, shift):
        pairs = [
            (t * size + s, (t + 1) * size + (s + shift) % size)
            for t in range(slices - 1)
            for s in range(size)
        ]
        return lax.ppermute(piece, axes, pairs)

    own, lasts, firsts = pieces
    return moved(own, 0), moved(lasts, 1), moved(firsts, -1)


def react_terms(field, laplace, diffusivity, source):
    first_part = field[0]
    second_part = field[1]
    product = first_part * second_part * second_part
    return jnp.stack(
        [
            diffusivity[0] * laplace[0] - product + source[0],
            diffusivity[1] * laplace[1] + product + source[1],
        ],
        axis=0,
    )


def fine_laplace(a):
    centre = a[..., 1:-1, :, :]
    pair_x = a[..., 2:, :, :] + a[..., :-2, :, :]
    half = centre.shape[-2] // 2
    even = centre[..., :half, :]
    odd = centre[..., half:, :]
    pair_y = jnp.concatenate(
        [odd + jnp.roll(odd, 1, -2), jnp.roll(even, -1, -2) + even], axis=-2
    )
    pair_z = jnp.roll(centre, -1, -1) + jnp.roll(centre, 1, -1)
    return pair_x + pair_y + pair_z - 6.0 * centre


def coarse_laplace(a):
    centre = a[..., 1:-1, :, :]
    pair_x = a[..., 2:, :, :] + a[..., :-2, :, :]
    pair_y = jnp.roll(centre, -1, -2) + jnp.roll(centre, 1, -2)
    pair_z = jnp.roll(centre, -1, -1) + jnp.roll(centre, 1, -1)
    return (pair_x - 2.0 * centre) * 0.25 + (pair_y - 2.0 * centre) * 0.25 + (
        pair_z - 2.0 * centre
    )


def restrict(field):
    a, h = field
    h2 = h - h % 2
    a = crop(field, h2)
    rows = a.shape[-3]
    half = a.shape[-2] // 2
    pairs = a.reshape(a.shape[:-3] + (rows // 2, 2) + a.shape[-2:])
    even = pairs[..., :half, :]
    odd = pairs[..., half:, :]
    upper = even[..., 0, :, :] + even[..., 1, :, :]
    lower = odd[..., 0, :, :] + odd[..., 1, :, :]
    return (upper + lower) * 0.25, h2 // 2


def prolong(a):
    rows = jnp.repeat(a, 2, axis=a.ndim - 3)
    return jnp.concatenate([rows, rows], axis=-2)


def even_odd_load(ref, index=()):
    view = ref.at[index] if index != () else ref
    lead = (slice(None),) * (len(view.shape) - 2)
    half = view.shape[-2] // 2
    even = view[lead + (pl.ds(0, half, stride=2), slice(None))]
    odd = view[lead + (pl.ds(1, half, stride=2), slice(None))]
    return jnp.concatenate([even, odd], axis=-2)


def kernel_laplace(f):
    centre = f[:, 1:-1]
    pair_x = f[:, 2:] + f[:, :-2]
    half = centre.shape[2] // 2
    even = centre[:, :, :half]
    odd = centre[:, :, half:]
    pair_y = jnp.concatenate(
        [odd + pltpu.roll(odd, 1, 2), pltpu.roll(even, half - 1, 2) + even], axis=2
    )
    lanes = centre.shape[3]
    pair_z = pltpu.roll(centre, lanes - 1, 3) + pltpu.roll(centre, 1, 3)
    return pair_x + pair_y + pair_z - 6.0 * centre


def kernel_restrict(v):
    shape = v.shape
    pairs = v.reshape((shape[0], shape[1] // 2, 2) + shape[2:])
    half = shape[2] // 2
    even = pairs[:, :, :, :half]
    odd = pairs[:, :, :, half:]
    upper = even[:, :, 0] + even[:, :, 1]
    lower = odd[:, :, 0] + odd[:, :, 1]
    return (upper + lower) * 0.25


def sweep_kernel(widths_sent, natural_prior, diff_ref, flag_ref, start_ref, centre_ref, bbefore_ref, bafter_ref,
                 own_ref, before_ref, after_ref, dec_ref, src_ref,
                 rate_ref, n1_ref, n2_ref, n3_ref, n4_ref, e0_ref, b0_ref, cown_ref, clasts_ref,
                 cfirsts_ref, v1w_ref):
    spread_table, grouped_table, interp_table, widths = node_tables()
    rows = e0_ref.shape[1]
    hs = (start_ref.shape[1] - rows) // 2
    hd = (dec_ref.shape[1] - rows) // 2
    d0 = diff_ref[0]
    d1 = diff_ref[1]

    def at(ref, h):
        off = hd - h
        return ref[:, off:off + rows + 2 * h]

    def cut(v, have, h):
        d = have - h
        return v[:, d:v.shape[1] - d]

    def terms(f, h):
        laplace = kernel_laplace(f)
        centre = f[:, 1:-1]
        s = at(src_ref, h - 1)
        product = centre[0] * centre[1] * centre[1]
        return jnp.stack([d0 * laplace[0] - product + s[0], d1 * laplace[1] + product + s[1]])

    parts = []
    offset = 0
    for m in range(4):
        w = hs - 1 - m
        parts.append(
            jnp.concatenate(
                [before_ref[:, offset:offset + w], own_ref[m], after_ref[:, offset:offset + w]],
                axis=1,
            )
        )
        offset += w
    if natural_prior:
        pieces = [even_odd_load(r) for r in (bbefore_ref, centre_ref, bafter_ref)]
    else:
        pieces = [r[...] for r in (bbefore_ref, centre_ref, bafter_ref)]
    joined = jnp.concatenate(pieces, axis=1)
    swept = [jnp.where(flag_ref[0] == 1, start_ref[...], joined)]
    found = []
    for m in range(4):
        have = hs - m
        e = terms(swept[m], have)
        found.append(e)
        h = have - 1
        numerator = (cut(swept[m], have, h) + widths[m] * e) + parts[m]
        swept.append(numerator / (1.0 + widths[m] * at(dec_ref, h)))
    found.append(terms(swept[4], hs - 4))
    dec0 = at(dec_ref, 0)
    fulls = [cut(found[j], hs - 1 - j, 0) - dec0 * cut(swept[j], hs - j, 0) for j in range(5)]
    integrated = []
    for c in range(2):
        summed = grouped_table[c][0] * fulls[0]
        for j in range(1, 5):
            summed = summed + grouped_table[c][j] * fulls[j]
        integrated.append(kernel_restrict(summed))
    crows = rows // 2
    hcr = (rate_ref.shape[1] - crows) // 2
    rc = rate_ref[:, hcr:hcr + crows]
    coarse_vals = [kernel_restrict(cut(swept[j], hs - j, 0)) for j in (0, 2, 4)]
    v1w_ref[...] = kernel_restrict(cut(swept[2], hs - 2, 2))
    half_step = 0.5 * step_length
    coarse_one = (
        coarse_vals[0] + half_step * rc * coarse_vals[1] + integrated[0]
    ) / (1.0 + half_step * rc)
    sent = [coarse_one, coarse_vals[1], coarse_vals[2], integrated[1]]
    offset = 0
    for i, piece in enumerate(sent):
        cown_ref[i] = piece
        w = widths_sent[i]
        skip = 1 if i == 1 else 0
        if w - skip:
            clasts_ref[:, offset:offset + w - skip] = piece[:, crows - w:crows - skip]
            cfirsts_ref[:, offset:offset + w - skip] = piece[:, skip:w]
        offset += w - skip
    for m, out in ((1, n1_ref), (2, n2_ref), (3, n3_ref), (4, n4_ref)):
        out[...] = cut(swept[m], hs - m, 1)
    e0_ref[...] = cut(found[0], hs - 1, 0)
    b0_ref[...] = cut(swept[0], hs, 0)


def fine_sweep(diffusivity, flag, start, prior, parts, decay, src, rate_c, widths_sent,
               natural_prior):
    rows = start.shape[1] - 2 * START_HALO
    shape = start.shape
    wide = jax.ShapeDtypeStruct((shape[0], rows + 2) + shape[2:], jnp.float32)
    own = jax.ShapeDtypeStruct((shape[0], rows) + shape[2:], jnp.float32)
    cshape = (shape[0], rows // 2, shape[2] // 2, shape[3])
    cown = jax.ShapeDtypeStruct((4,) + cshape, jnp.float32)
    cedge = jax.ShapeDtypeStruct((shape[0], sum(widths_sent) - 1) + cshape[2:], jnp.float32)
    cwide = jax.ShapeDtypeStruct((shape[0], rows // 2 + 2) + cshape[2:], jnp.float32)
    vmem = pl.BlockSpec(memory_space=pltpu.VMEM)
    return pl.pallas_call(
        functools.partial(sweep_kernel, widths_sent, natural_prior),
        out_shape=(wide, wide, wide, wide, own, own, cown, cedge, cedge, cwide),
        in_specs=[pl.BlockSpec(memory_space=pltpu.SMEM)] * 2 + [vmem] * 10,
        out_specs=(vmem,) * 10,
    )(diffusivity, flag, start, *prior, *parts, decay, src, rate_c)


def coarse_kernel_laplace(f):
    centre = f[:, 1:-1]
    pair_x = f[:, 2:] + f[:, :-2]
    ny = centre.shape[2]
    lanes = centre.shape[3]
    pair_y = pltpu.roll(centre, ny - 1, 2) + pltpu.roll(centre, 1, 2)
    pair_z = pltpu.roll(centre, lanes - 1, 3) + pltpu.roll(centre, 1, 3)
    return (pair_x - 2.0 * centre) * 0.25 + (pair_y - 2.0 * centre) * 0.25 + (
        pair_z - 2.0 * centre
    )


def finish_kernel(widths_sent, diff_ref, cown_ref, cbefore_ref, cafter_ref, v1w_ref, rate_ref, csrc_ref,
                  n1_ref, n2_ref, n3_ref, n4_ref, b_ref, e0_ref, dec_ref, src_ref, *outs):
    spread_table, grouped_table, interp_table, widths = node_tables()
    last = len(outs) == 1
    rows = e0_ref.shape[1]
    crows = rows // 2
    ho = widths_sent[2]
    joined = []
    offset = 0
    for i in range(4):
        w = widths_sent[i]
        skip = 1 if i == 1 else 0
        centre = v1w_ref[...] if skip else cown_ref[i]
        sw = w - skip
        if sw:
            joined.append(
                jnp.concatenate(
                    [cbefore_ref[:, offset:offset + sw], centre, cafter_ref[:, offset:offset + sw]],
                    axis=1,
                )
            )
        else:
            joined.append(centre)
        offset += sw
    one, mid, low, late = joined
    hcr = (rate_ref.shape[1] - crows) // 2
    hd = (dec_ref.shape[1] - rows) // 2
    hs = START_HALO
    d0 = diff_ref[0]
    d1 = diff_ref[1]

    def at(ref, h, size, have):
        off = have - h
        return ref[:, off:off + size + 2 * h]

    def cut(v, have, h):
        d = have - h
        return v[:, d:v.shape[1] - d]

    def react(centre, laplace, s):
        product = centre[0] * centre[1] * centre[1]
        return jnp.stack([d0 * laplace[0] - product + s[0], d1 * laplace[1] + product + s[1]])

    def coarse_terms(v):
        return react(v[:, 1:-1], coarse_kernel_laplace(v), at(csrc_ref, ho, crows, hcr))

    half_step = 0.5 * step_length
    rc = at(rate_ref, ho, crows, hcr)
    coarse_two = (
        cut(one, ho + 1, ho)
        + half_step * (coarse_terms(one) - coarse_terms(mid))
        + half_step * rc * low
        + late
    ) / (1.0 + half_step * rc)
    delta_one = cut(one, ho + 1, ho) - cut(mid, ho + 1, ho)
    delta_two = coarse_two - low

    def prolonged(c):
        shape = c.shape
        doubled = jnp.broadcast_to(c[:, :, None], (shape[0], shape[1], 2) + shape[2:])
        doubled = doubled.reshape((shape[0], 2 * shape[1]) + shape[2:])
        return jnp.concatenate([doubled, doubled], axis=2)

    news = {}
    for m, ref in ((1, n1_ref), (2, n2_ref), (3, n3_ref), (4, n4_ref)):
        if last and m < 4:
            continue
        fine = prolonged(interp_table[m][1] * delta_one + interp_table[m][2] * delta_two)
        news[m] = cut(ref[...], 1, ho) + cut(fine, 2 * ho, ho)
    if last:
        half = news[4].shape[2] // 2
        outs[0][:, :, pl.ds(0, half, stride=2), :] = news[4][:, :, :half]
        outs[0][:, :, pl.ds(1, half, stride=2), :] = news[4][:, :, half:]
        return
    own_out, lasts_out, firsts_out, u4_out, u4_last_out, u4_first_out = outs
    src1 = at(src_ref, 0, rows, hd)
    dec0 = at(dec_ref, 0, rows, hd)
    states = [b_ref[...]] + [cut(news[m], 1, 0) for m in range(1, 5)]
    terms = [e0_ref[...]] + [
        react(cut(news[m], 1, 0), kernel_laplace(news[m]), src1) for m in range(1, 5)
    ]
    fulls = [terms[j] - dec0 * states[j] for j in range(5)]
    offset = 0
    for m in range(4):
        summed = spread_table[m][0] * fulls[0]
        for j in range(1, 5):
            summed = summed + spread_table[m][j] * fulls[j]
        part = (widths[m] * dec0 * states[m + 1] - widths[m] * terms[m]) + summed
        own_out[m] = part
        w = hs - 1 - m
        lasts_out[:, offset:offset + w] = part[:, rows - w:]
        firsts_out[:, offset:offset + w] = part[:, :w]
        offset += w
    u4_out[...] = news[4]
    u4_last_out[...] = states[4][:, rows - hs:rows - 1]
    u4_first_out[...] = states[4][:, 1:hs]


def finish_round(diffusivity, coarse, rate_c, source_c, swept, e0, decay, src, last, widths_sent):
    begin = swept[0]
    shape = begin.shape
    rows = e0.shape[1]
    field = jax.ShapeDtypeStruct((shape[0], rows) + shape[2:], jnp.float32)
    if last:
        out_shape = (field,)
    else:
        sent = sum(START_HALO - 1 - m for m in range(4))
        edge = jax.ShapeDtypeStruct((shape[0], sent) + shape[2:], jnp.float32)
        rim = jax.ShapeDtypeStruct((shape[0], START_HALO - 1) + shape[2:], jnp.float32)
        centre = jax.ShapeDtypeStruct((shape[0], rows + 2) + shape[2:], jnp.float32)
        out_shape = (jax.ShapeDtypeStruct((4,) + field.shape, jnp.float32), edge, edge, centre, rim, rim)
    vmem = pl.BlockSpec(memory_space=pltpu.VMEM)
    args = (diffusivity, *coarse, rate_c, source_c, *swept[1:], begin, e0, decay, src)
    return pl.pallas_call(
        functools.partial(finish_kernel, widths_sent),
        out_shape=out_shape,
        in_specs=[pl.BlockSpec(memory_space=pltpu.SMEM)] + [vmem] * (len(args) - 1),
        out_specs=(vmem,) * len(out_shape),
    )(*args)


def start_kernel(diff_ref, init_ref, decay_ref, source_ref, got_before_ref, got_after_ref,
                 own_ref, before_ref, after_ref, rate_ref, csrc_ref, ext_ref, dec_ref, src_ref):
    spread_table, grouped_table, interp_table, widths = node_tables()
    rows = own_ref.shape[2]
    hs = (ext_ref.shape[1] - rows) // 2
    hd = hs - 1
    d0 = diff_ref[0]
    d1 = diff_ref[1]

    def joined(ref, offset, w):
        return jnp.concatenate(
            [
                even_odd_load(got_before_ref, (slice(None), pl.ds(offset, w))),
                even_odd_load(ref),
                even_odd_load(got_after_ref, (slice(None), pl.ds(offset, w))),
            ],
            axis=1,
        )

    state = joined(init_ref, 0, hs)
    dec = joined(decay_ref, hs, hd)
    s = joined(source_ref, hs + hd, hd)
    ext_ref[...] = state
    dec_ref[...] = dec
    src_ref[...] = s
    inner = state[:, 1:-1]
    laplace = kernel_laplace(state)
    product = inner[0] * inner[1] * inner[1]
    terms = jnp.stack([d0 * laplace[0] - product + s[0], d1 * laplace[1] + product + s[1]])
    full = terms - dec * inner
    edge = hs - 1
    offset = 0
    for m in range(4):
        weight = sum(spread_table[m][j] for j in range(5))
        part = (widths[m] * dec * inner - widths[m] * terms) + weight * full
        own_ref[m] = part[:, edge:edge + rows]
        w = edge - m
        before_ref[:, offset:offset + w] = part[:, m:edge]
        after_ref[:, offset:offset + w] = part[:, edge + rows:edge + rows + w]
        offset += w
    rate_ref[...] = kernel_restrict(dec)
    csrc_ref[...] = kernel_restrict(s)


def start_terms(diffusivity, own_arrays, got_before, got_after):
    own_shape = own_arrays[0].shape
    rows = own_shape[1]
    shape = (own_shape[0], rows + 2 * START_HALO) + own_shape[2:]
    fixed = jax.ShapeDtypeStruct(
        (own_shape[0], rows + 2 * (START_HALO - 1)) + own_shape[2:], jnp.float32
    )
    sent = sum(START_HALO - 1 - m for m in range(4))
    edge = jax.ShapeDtypeStruct((shape[0], sent) + shape[2:], jnp.float32)
    cshape = (shape[0], (rows + 2 * (START_HALO - 1)) // 2, shape[2] // 2, shape[3])
    coarse = jax.ShapeDtypeStruct(cshape, jnp.float32)
    vmem = pl.BlockSpec(memory_space=pltpu.VMEM)
    return pl.pallas_call(
        start_kernel,
        out_shape=(
            jax.ShapeDtypeStruct((4, shape[0], rows) + shape[2:], jnp.float32),
            edge, edge, coarse, coarse,
            jax.ShapeDtypeStruct(shape, jnp.float32),
            fixed,
            fixed,
        ),
        in_specs=[pl.BlockSpec(memory_space=pltpu.SMEM)] + [vmem] * 5,
        out_specs=(vmem,) * 8,
    )(diffusivity, *own_arrays, got_before, got_after)


def packed_halo(fields):
    size = lax.axis_size("space")
    rows = fields[0][0].shape[-3]
    axis = fields[0][0].ndim - 3
    up = [(i, (i + 1) % size) for i in range(size)]
    down = [((i + 1) % size, i) for i in range(size)]
    lasts = jnp.concatenate(
        [lax.slice_in_dim(a, rows - w, rows, axis=axis) for a, w in fields], axis=axis
    )
    firsts = jnp.concatenate([lax.slice_in_dim(a, 0, w, axis=axis) for a, w in fields], axis=axis)
    before = lax.ppermute(lasts, "space", up)
    after = lax.ppermute(firsts, "space", down)
    out = []
    offset = 0
    for a, w in fields:
        out.append(
            (
                jnp.concatenate(
                    [
                        lax.slice_in_dim(before, offset, offset + w, axis=axis),
                        a,
                        lax.slice_in_dim(after, offset, offset + w, axis=axis),
                    ],
                    axis=axis,
                ),
                w,
            )
        )
        offset += w
    return out


def per_device(initial, decay_rate, source, diffusivity):
    spread_table, grouped_table, interp_table, widths = node_tables()
    first_slice = lax.axis_index("tm") == 0
    hs = START_HALO
    assert hs == 5 and initial.shape[-3] >= hs

    own_start = initial[0]
    size = lax.axis_size("space")
    up = [(i, (i + 1) % size) for i in range(size)]
    down = [((i + 1) % size, i) for i in range(size)]
    rows = own_start.shape[-3]
    widths_in = (hs, hs - 1, hs - 1)
    own_arrays = (own_start, decay_rate, source)
    got_before = lax.ppermute(
        jnp.concatenate([a[:, rows - w:] for a, w in zip(own_arrays, widths_in)], axis=1),
        "space", up,
    )
    got_after = lax.ppermute(
        jnp.concatenate([a[:, :w] for a, w in zip(own_arrays, widths_in)], axis=1),
        "space", down,
    )
    own4, before4, after4, rate_own, csrc_own, own_ext, dec_ext, src_ext = start_terms(
        diffusivity, own_arrays, got_before, got_after
    )
    decay = (dec_ext, hs - 1)
    src = (src_ext, hs - 1)
    rate_c = (rate_own, (hs - 1) // 2)
    source_c = (csrc_own, (hs - 1) // 2)

    def fine_E(field):
        a, h = field
        laplace = fine_laplace(a)
        return react_terms(a[..., 1:-1, :, :], laplace, diffusivity, crop(src, h - 1)), h - 1

    def coarse_E(field):
        a, h = field
        laplace = coarse_laplace(a)
        return react_terms(a[..., 1:-1, :, :], laplace, diffusivity, crop(source_c, h - 1)), h - 1

    def full(field, field_E):
        h = min(field[1], field_E[1])
        return crop(field_E, h) - crop(decay, h) * crop(field, h), h

    def step_terms(states, terms):
        fulls = [full(states[j], terms[j]) for j in range(5)]
        hf = min(f[1] for f in fulls)
        out = []
        for m in range(4):
            h = min(hf, terms[m][1], states[m + 1][1])
            summed = spread_table[m][0] * crop(fulls[0], h)
            for j in range(1, 5):
                summed = summed + spread_table[m][j] * crop(fulls[j], h)
            own = (
                widths[m] * crop(decay, h) * crop(states[m + 1], h)
                - widths[m] * crop(terms[m], h)
            ) + summed
            out.append((own, h))
        return out

    def advance(prior, pieces, last, natural):
        widths_sent = (1, 1, 0, 0) if last else (2, 2, 1, 1)
        n1, n2, n3, n4, e0, b0, cown, clasts, cfirsts, v1w = fine_sweep(
            diffusivity, flag, own_ext, prior, pieces, decay[0], src[0], rate_c[0], widths_sent,
            natural,
        )
        coarse = (
            cown,
            lax.ppermute(clasts, "space", up),
            lax.ppermute(cfirsts, "space", down),
            v1w,
        )
        return finish_round(
            diffusivity, coarse, rate_c[0], source_c[0],
            (b0, n1, n2, n3, n4), e0, decay[0], src[0], last, widths_sent,
        )

    size = lax.axis_size("space")
    up = [(i, (i + 1) % size) for i in range(size)]
    down = [((i + 1) % size, i) for i in range(size)]
    rows = own_start.shape[-3]
    flag = jnp.where(first_slice, 1, 0).astype(jnp.int32).reshape(1)
    pieces = (own4, before4, after4)
    prior = from_previous_slice(
        (own_start, own_start[:, rows - hs:], own_start[:, :hs])
    )
    for k in range(ROUNDS):
        last = k + 1 == ROUNDS
        outs = advance(prior, pieces, last, k == 0)
        if not last:
            own4, lasts, firsts, u4, u4_last, u4_first = outs
            pieces = (
                own4,
                lax.ppermute(lasts, "space", up),
                lax.ppermute(firsts, "space", down),
            )
            prior = from_previous_slice((u4, u4_last, u4_first))
    return outs[0][None]


def solution(mesh):
    placed = (
        P("tm", None, "space", None, None),
        P(None, "space", None, None),
        P(None, "space", None, None),
        P(),
    )
    return jax.shard_map(
        per_device,
        mesh=mesh,
        in_specs=placed,
        out_specs=P("tm", None, "space", None, None),
        check_vma=False,
    )
```
